32 devices in a mesh: dp: 4 (over y, x), tensor: 8 (over z, core).
Axes of the slice: x: 2, y: 2, z: 4, core: 2. Of those that a mesh axis runs over, the one named last changes fastest.
Arguments:
- tokens: bfloat16 [2688, 1024], P('dp', 'tensor'), may hold values from -6 to 6
- cotangent: bfloat16 [2688, 1024], P('dp', 'tensor'), may hold values from -6 to 6
- lengths: int32 [4, 4], replicated, may hold values from 24 to 192, as said below
- owners: int32 [4, 4], replicated, may hold values from 0 to 3, as said below
- proj_weight: bfloat16 [1024, 4, 1024], replicated, may hold values from -0.1875 to 0.1875
- norm_gain: float32 [1024], replicated, may hold values from 0.5 to 2
- out_weight: bfloat16 [1024, 1024], replicated, may hold values from -0.1875 to 0.1875
Outputs:
- mixed: bfloat16 [1728, 1024], P('dp', 'tensor')
- token_grad: bfloat16 [2688, 1024], P('dp', 'tensor')
- proj_grad: float32 [1024, 4, 1024], P('dp', None, 'tensor')
- out_grad: float32 [1024, 1024], P('tensor', 'dp')
The draws below stay inside these ranges and needn't reach their ends.
Inputs may be any that keep to these rules, and one draw needn't show every extreme that they name: Sequence i of loader shard j has lengths[j, i] rows stored back to back from the shard's first row; the sequences sent to any one owner sum to exactly 432 rows. owners[j, i] is the owner of sequence i of loader shard j; each row names every owner once.
All inputs are finite; a program needn't handle non-finite values.
Results may differ from the reference program's by a relative error of at most 0.012.
Values may be sent and summed in bfloat16 or wider, within the bound.
No kernel may reach another device: no remote copies, remote signals or barrier semaphores. Data moves between devices by JAX's collectives and lax.ppermute only.
A program may use at most 128 MiB of HBM per device.

```python
import math
import jax
import jax.numpy as jnp
from jax import lax

D = 1024
H = 8
MAXLEN = 192
LOAD_ROWS = 672
OWN_ROWS = 432
N_DP = 4
N_TENSOR = 8


def routing_plan(key):
    unit_len = MAXLEN // 16
    base_len = 9 * unit_len
    spread = 2 * unit_len
    drift_max = 5 * unit_len
    loader_ids = jnp.arange(N_DP, dtype=jnp.int32)
    levels = jax.random.randint(jax.random.fold_in(key, 11), (N_DP,), 0, spread + 1, dtype=jnp.int32)
    levels = levels.at[0].set(spread).at[1].set(0)
    cycle_terms = levels - jnp.roll(levels, -1)
    drifts = jax.random.randint(jax.random.fold_in(key, 12), (N_DP,), 0, drift_max + 1, dtype=jnp.int32)
    drifts = drifts.at[0].set(drift_max).at[1].set(0)
    cycle_order = jax.random.permutation(jax.random.fold_in(key, 13), N_DP).astype(jnp.int32)
    cycle_order = jnp.where(cycle_order == 0, cycle_order[1], jnp.where(loader_ids == 1, 0, cycle_order)).astype(jnp.int32)
    rows_j = loader_ids[:, None]
    cols_o = loader_ids[None, :]
    length_grid = base_len + cycle_terms[(cycle_order[cols_o] - rows_j) % N_DP] + drifts[rows_j] - drifts[(rows_j + cols_o) % N_DP]
    row_seeds = jax.random.split(jax.random.fold_in(key, 14), N_DP)
    owner_table = jax.vmap(lambda row_seed: jax.random.permutation(row_seed, N_DP))(row_seeds).astype(jnp.int32)
    length_table = jnp.take_along_axis(length_grid.astype(jnp.int32), owner_table, axis=1).astype(jnp.int32)
    return (length_table, owner_table)


def draw_lengths(key, part):
    return routing_plan(key)[0]


def draw_owners(key, part):
    return routing_plan(key)[1]


def level_of(stream_key, dims, shards, low, high):
    factor_of = 1.0
    for axis_at, shards_of in shards:
        steps = jax.random.uniform(jax.random.fold_in(jax.random.fold_in(stream_key, 6), axis_at), (shards_of,), jnp.float32, low / len(shards), high / len(shards))
        factor_of = factor_of * jnp.repeat(jnp.exp(steps), dims[axis_at] // shards_of).reshape((-1,) + (1,) * (len(dims) - 1 - axis_at))
    return factor_of


def bell_draw(own_key, extent, deviation, most, cuts=(), held_as=jnp.bfloat16):
    factor_of = level_of(own_key, extent, cuts, -0.22, 0.18) if cuts else 1.0
    entries = jax.random.normal(own_key, extent, jnp.float32) * deviation * factor_of
    return jnp.minimum(jnp.maximum(entries, -most), most).astype(held_as)


def setup_inputs(seed: int = 0) -> dict:
    key_of = jax.random.split(jax.random.key(seed), 8)
    return {
        "tokens": bell_draw(key_of[0], (N_DP * LOAD_ROWS, D), 1.0, 6.0, ((0, 4), (1, 8))),
        "cotangent": bell_draw(key_of[1], (N_DP * LOAD_ROWS, D), 1.0, 6.0, ((0, 4), (1, 8))),
        "lengths": draw_lengths(jax.random.fold_in(key_of[7], 71), 0),
        "owners": draw_owners(jax.random.fold_in(key_of[7], 71), 0),
        "proj_weight": bell_draw(key_of[4], (D, 4, D), D ** -0.5, 0.1875),
        "norm_gain": jnp.clip(jnp.exp(jax.random.uniform(key_of[5], (D,), jnp.float32, math.log(0.5), math.log(2.0))), 0.5, 2.0),
        "out_weight": bell_draw(key_of[6], (D, D), D ** -0.5, 0.1875),
    }


norm_eps = 1e-05

def silu_slope(argument):
    sigmoid_val = jax.nn.sigmoid(argument)
    return sigmoid_val * (1.0 + argument * (1.0 - sigmoid_val))

def exclusive_sum(counts, axis):
    return jnp.cumsum(counts, axis=axis) - counts

def stored(array):
    return lax.optimization_barrier(array.astype(jnp.bfloat16)).astype(jnp.float32)

def rounded_sum(left_part, right_part):

    def add_group(running, operands):
        product = jnp.dot(operands[0], operands[1], preferred_element_type=jnp.float32)
        return (running + stored(product), None)
    start_sum = jnp.zeros((left_part.shape[1], right_part.shape[2]), jnp.float32)
    running, unused_out = lax.scan(add_group, start_sum, (left_part, right_part))
    return running

def reference(tokens, cotangent, lengths, owners, proj_weight, norm_gain, out_weight):
    head_dim = D // H
    score_scale = 1.0 / math.sqrt(head_dim)
    group_width = D // N_TENSOR
    seq_count = lengths.shape[1]
    row_count = seq_count * MAXLEN
    places = jnp.arange(MAXLEN, dtype=jnp.int32)
    starts = exclusive_sum(lengths, 1).astype(jnp.int32)
    live_mask = places[None, None, :] < lengths[:, :, None]
    shard_base = (jnp.arange(N_DP, dtype=jnp.int32) * LOAD_ROWS)[:, None, None]
    pick_rows = (shard_base + jnp.minimum(starts[:, :, None] + places[None, None, :], LOAD_ROWS - 1)).astype(jnp.int32)
    flat_proj = proj_weight.reshape(D, 4 * D)
    head_gains = norm_gain.reshape(H, head_dim)
    proj_groups = proj_weight.reshape(D, 4, N_TENSOR, group_width).transpose(2, 1, 3, 0).reshape(N_TENSOR, 4 * group_width, D)
    out_groups = out_weight.reshape(N_TENSOR, group_width, D)
    causal = places[:, None] >= places[None, :]
    zero_bf = jnp.zeros((), jnp.bfloat16)
    contract_rows = (((0,), (0,)), ((), ()))
    contract_cols = (((1,), (1,)), ((), ()))

    def one_shard(totals, pieces):
        shard_rows, shard_live = pieces
        inputs = jnp.where(shard_live[..., None], tokens[shard_rows], zero_bf).reshape(row_count, D)
        upstream = jnp.where(shard_live[..., None], cotangent[shard_rows], zero_bf).reshape(row_count, D)
        projected = jnp.dot(inputs, flat_proj, preferred_element_type=jnp.float32)
        activated = stored(jax.nn.silu(projected)).reshape(seq_count, MAXLEN, 4, H, head_dim)
        gating = activated[:, :, 0]
        values = activated[:, :, 1]
        queries = activated[:, :, 2]
        keys_head = activated[:, :, 3]
        scores = jnp.einsum('smhd,snhd->shmn', queries, keys_head)
        allowed = causal[None, None] & shard_live[:, None, :, None] & shard_live[:, None, None, :]
        weights = stored(jnp.where(allowed, jax.nn.silu(scores * score_scale) / MAXLEN, 0.0))
        attended = jnp.einsum('shmn,snhd->smhd', weights, values)
        inv_rms = lax.rsqrt(lax.optimization_barrier(jnp.mean(attended * attended, axis=-1, keepdims=True)) + norm_eps)
        normed = attended * inv_rms * head_gains
        gated_rows = (normed * gating).astype(jnp.bfloat16).reshape(row_count, D)
        out_sum = rounded_sum(gated_rows.reshape(row_count, N_TENSOR, group_width).transpose(1, 0, 2), out_groups)
        mixed_rows = (inputs.astype(jnp.float32) + out_sum).astype(jnp.bfloat16)
        down_grad = lax.dot_general(upstream, out_weight, contract_cols, preferred_element_type=jnp.float32)
        down_grad = down_grad.reshape(seq_count, MAXLEN, H, head_dim)
        d_normed = down_grad * gating
        d_gating = down_grad * normed
        scaled = head_gains * d_normed
        d_attended = stored(inv_rms * scaled - attended * inv_rms ** 3 * lax.optimization_barrier(jnp.mean(attended * scaled, axis=-1, keepdims=True)))
        d_weights = jnp.einsum('smhd,snhd->shmn', d_attended, values)
        d_values = jnp.einsum('shmn,smhd->snhd', weights, d_attended)
        d_scores = stored(jnp.where(allowed, d_weights * silu_slope(scores * score_scale) * (score_scale / MAXLEN), 0.0))
        d_queries = jnp.einsum('shmn,snhd->smhd', d_scores, keys_head)
        d_keys = jnp.einsum('shmn,smhd->snhd', d_scores, queries)
        d_activated = jnp.stack([d_gating, d_values, d_queries, d_keys], axis=2).reshape(row_count, 4 * D)
        d_projected = (d_activated * silu_slope(projected)).astype(jnp.bfloat16)
        grouped = d_projected.reshape(row_count, 4, N_TENSOR, group_width).transpose(2, 0, 1, 3).reshape(N_TENSOR, row_count, 4 * group_width)
        token_rows = (upstream.astype(jnp.float32) + rounded_sum(grouped, proj_groups)).astype(jnp.bfloat16)
        proj_total = totals[0] + lax.dot_general(inputs, d_projected, contract_rows, preferred_element_type=jnp.float32)
        out_total = totals[1] + lax.dot_general(gated_rows, upstream, contract_rows, preferred_element_type=jnp.float32)
        return ((proj_total, out_total), (mixed_rows, token_rows))
    start_totals = (jnp.zeros((D, 4 * D), jnp.float32), jnp.zeros((D, D), jnp.float32))
    totals, outputs = lax.scan(one_shard, start_totals, (pick_rows, live_mask))
    mixed_seqs, grad_seqs = outputs
    owner_ids = jnp.arange(N_DP, dtype=jnp.int32)
    seq_ids = jnp.arange(seq_count, dtype=jnp.int32)
    sent_to = owners[:, :, None] == owner_ids[None, None, :]
    recv_len = lax.optimization_barrier(jnp.sum(jnp.where(sent_to, lengths[:, :, None], 0), axis=1)).T.astype(jnp.int32)
    recv_seq = lax.optimization_barrier(jnp.sum(jnp.where(sent_to, seq_ids[None, :, None], 0), axis=1)).T.astype(jnp.int32)
    recv_start = exclusive_sum(recv_len, 1).astype(jnp.int32)
    compact_ids = jnp.arange(OWN_ROWS, dtype=jnp.int32)
    slot_ids = (lax.optimization_barrier(jnp.sum((compact_ids[None, :, None] >= recv_start[:, None, :]).astype(jnp.int32), axis=2)) - 1).astype(jnp.int32)
    slot_start = jnp.take_along_axis(recv_start, slot_ids, axis=1)
    slot_seq = jnp.take_along_axis(recv_seq, slot_ids, axis=1)
    flat_ids = ((slot_ids * seq_count + slot_seq) * MAXLEN + compact_ids[None, :] - slot_start).astype(jnp.int32)
    mixed_all = mixed_seqs.reshape(-1, D)[flat_ids.reshape(-1)]
    load_ids = jnp.arange(LOAD_ROWS, dtype=jnp.int32)
    seq_of = (lax.optimization_barrier(jnp.sum((load_ids[None, :, None] >= starts[:, None, :]).astype(jnp.int32), axis=2)) - 1).astype(jnp.int32)
    start_of = jnp.take_along_axis(starts, seq_of, axis=1)
    row_used = load_ids[None, :] < lax.optimization_barrier(jnp.sum(lengths, axis=1))[:, None]
    shard_ids = jnp.arange(N_DP, dtype=jnp.int32)[:, None]
    grad_ids = ((shard_ids * seq_count + seq_of) * MAXLEN + jnp.minimum(load_ids[None, :] - start_of, MAXLEN - 1)).astype(jnp.int32)
    gathered = grad_seqs.reshape(-1, D)[grad_ids.reshape(-1)].reshape(N_DP, LOAD_ROWS, D)
    token_grad = jnp.where(row_used[..., None], gathered, zero_bf).reshape(N_DP * LOAD_ROWS, D)
    return (mixed_all, token_grad, totals[0].reshape(D, 4, D), totals[1])
```

```python
import math

import jax
import jax.numpy as jnp
from jax import lax
from jax.sharding import PartitionSpec as P

D = 1024
H = 8
MAXLEN = 192


norm_eps = 1e-05


def silu_slope(argument):
    sigmoid_val = jax.nn.sigmoid(argument)
    return sigmoid_val * (1.0 + argument * (1.0 - sigmoid_val))


def exclusive_sum(counts):
    return jnp.cumsum(counts) - counts


def local(tokens, cotangent, lengths, owners, proj_weight, norm_gain, out_weight):
    f32 = jnp.float32
    bf16 = jnp.bfloat16
    dp_count = lax.axis_size("dp")
    tensor_count = lax.axis_size("tensor")
    dp_index = lax.axis_index("dp")
    tensor_index = lax.axis_index("tensor")
    col_width = tokens.shape[1]
    load_rows = tokens.shape[0]
    head_dim = D // H
    score_scale = 1.0 / math.sqrt(head_dim)
    owned_rows = dp_count * (9 * MAXLEN // 16)
    places = jnp.arange(MAXLEN, dtype=jnp.int32)
    peer_ids = jnp.arange(dp_count, dtype=jnp.int32)
    seq_ids = jnp.arange(lengths.shape[1], dtype=jnp.int32)
    zero_bf = jnp.zeros((), bf16)

    my_lengths = lengths[dp_index]
    my_owners = owners[dp_index]
    my_starts = exclusive_sum(my_lengths)
    sent_to = my_owners[None, :] == peer_ids[:, None]
    send_start = jnp.sum(jnp.where(sent_to, my_starts[None, :], 0), axis=1)
    send_ids = jnp.minimum(send_start[:, None] + places[None, :], load_rows - 1)
    both = jnp.concatenate([tokens, cotangent], axis=1)
    send_both = both[send_ids]
    recv_both = lax.all_to_all(send_both, "dp", split_axis=0, concat_axis=0, tiled=True)

    recv_len = jnp.sum(jnp.where(owners == dp_index, lengths, 0), axis=1)
    recv_start = exclusive_sum(recv_len)
    compact_ids = jnp.arange(owned_rows, dtype=jnp.int32)
    compact_slot = (
        jnp.sum((compact_ids[:, None] >= recv_start[None, :]).astype(jnp.int32), axis=1) - 1
    )
    slot_pick = compact_slot[:, None] == peer_ids[None, :]
    compact_start = jnp.sum(jnp.where(slot_pick, recv_start[None, :], 0), axis=1)
    gather_ids = compact_slot * MAXLEN + compact_ids - compact_start
    own_both = recv_both.reshape(dp_count * MAXLEN, 2 * col_width)[gather_ids]
    own_tokens = own_both[:, :col_width]
    own_cotan = own_both[:, col_width:]

    gathered = lax.all_gather(own_both, "tensor", axis=0, tiled=False)
    g_tok = gathered[..., :col_width]
    g_cot = gathered[..., col_width:]

    head_start = tensor_index * H // tensor_count * head_dim
    own_start = tensor_index * col_width
    inner_start = own_start - head_start
    head_proj = lax.dynamic_slice_in_dim(proj_weight, head_start, head_dim, 2).reshape(
        tensor_count, col_width, 4 * head_dim
    )
    own_proj = lax.dynamic_slice_in_dim(proj_weight, own_start, col_width, 2).reshape(
        tensor_count, col_width, 4 * col_width
    )
    head_out = lax.dynamic_slice_in_dim(out_weight, head_start, head_dim, 0).reshape(
        head_dim, tensor_count, col_width
    )
    own_out = lax.dynamic_slice_in_dim(out_weight, own_start, col_width, 0).reshape(
        col_width, tensor_count, col_width
    )
    head_gain = lax.dynamic_slice_in_dim(norm_gain, head_start, head_dim, 0)

    projected = jnp.einsum("trc,tcn->rn", g_tok, head_proj, preferred_element_type=f32)
    down_grad = jnp.einsum("trc,dtc->rd", g_cot, head_out, preferred_element_type=f32)
    proj4 = projected.reshape(owned_rows, 4, head_dim)
    activated = jax.nn.silu(proj4).astype(bf16)
    gating = activated[:, 0]
    values = activated[:, 1]
    queries = activated[:, 2]
    keys_head = activated[:, 3]
    scores = jnp.einsum("md,nd->mn", queries, keys_head, preferred_element_type=f32)
    allowed = (compact_slot[:, None] == compact_slot[None, :]) & (
        compact_ids[:, None] >= compact_ids[None, :]
    )
    weights = jnp.where(allowed, jax.nn.silu(scores * score_scale) / MAXLEN, 0.0).astype(bf16)
    attended = jnp.einsum("mn,nd->md", weights, values, preferred_element_type=f32)
    inv_rms = lax.rsqrt(jnp.mean(attended * attended, axis=-1, keepdims=True) + norm_eps)
    normed = attended * inv_rms * head_gain
    gated = (normed * gating).astype(bf16)
    own_gated = lax.dynamic_slice_in_dim(gated, inner_start, col_width, 1)
    out_part = jnp.einsum("rc,ctk->trk", own_gated, own_out, preferred_element_type=f32)
    out_sum = lax.psum_scatter(
        out_part.astype(bf16), "tensor", scatter_dimension=0, tiled=True
    ).reshape(owned_rows, col_width)
    mixed_out = (own_tokens.astype(f32) + out_sum.astype(f32)).astype(bf16)

    d_normed = down_grad * gating
    d_gating = down_grad * normed
    scaled = head_gain * d_normed
    d_attended = (
        inv_rms * scaled
        - attended * inv_rms**3 * jnp.mean(attended * scaled, axis=-1, keepdims=True)
    ).astype(bf16)
    d_weights = jnp.einsum("md,nd->mn", d_attended, values, preferred_element_type=f32)
    d_values = jnp.einsum("mn,md->nd", weights, d_attended, preferred_element_type=f32)
    d_scores = jnp.where(
        allowed, d_weights * silu_slope(scores * score_scale) * (score_scale / MAXLEN), 0.0
    ).astype(bf16)
    d_queries = jnp.einsum("mn,nd->md", d_scores, keys_head, preferred_element_type=f32)
    d_keys = jnp.einsum("mn,md->nd", d_scores, queries, preferred_element_type=f32)
    d_activated = jnp.stack([d_gating, d_values, d_queries, d_keys], axis=1)
    d_projected = (d_activated * silu_slope(proj4)).astype(bf16)
    own_grad = lax.dynamic_slice_in_dim(d_projected, inner_start, col_width, 2).reshape(
        owned_rows, 4 * col_width
    )
    grad_part = jnp.einsum("rn,tkn->trk", own_grad, own_proj, preferred_element_type=f32)
    grad_sum = lax.psum_scatter(
        grad_part.astype(bf16), "tensor", scatter_dimension=0, tiled=True
    ).reshape(owned_rows, col_width)
    token_rows = (own_cotan.astype(f32) + grad_sum.astype(f32)).astype(bf16)

    proj_term = jnp.einsum("trc,rn->tcn", g_tok, own_grad, preferred_element_type=f32)
    out_term = jnp.einsum("trc,rd->tcd", g_cot, own_gated, preferred_element_type=f32)
    terms = jnp.concatenate(
        [proj_term.reshape(D, 4 * col_width), out_term.reshape(D, col_width)], axis=1
    ).astype(bf16)
    term_sum = lax.psum_scatter(terms, "dp", scatter_dimension=0, tiled=True).astype(f32)
    proj_grad = term_sum[:, : 4 * col_width].reshape(-1, 4, col_width)
    out_grad = term_sum[:, 4 * col_width :].T

    back_src = jnp.minimum(recv_start[:, None] + places[None, :], owned_rows - 1)
    back_send = token_rows[back_src]
    back_grads = lax.all_to_all(back_send, "dp", split_axis=0, concat_axis=0, tiled=True)
    back_grads = back_grads.reshape(dp_count * MAXLEN, col_width)
    load_ids = jnp.arange(load_rows, dtype=jnp.int32)
    seq_of = jnp.sum((load_ids[:, None] >= my_starts[None, :]).astype(jnp.int32), axis=1) - 1
    seq_pick = seq_of[:, None] == seq_ids[None, :]
    owner_of = jnp.sum(jnp.where(seq_pick, my_owners[None, :], 0), axis=1)
    start_of = jnp.sum(jnp.where(seq_pick, my_starts[None, :], 0), axis=1)
    back_ids = owner_of * MAXLEN + jnp.minimum(load_ids - start_of, MAXLEN - 1)
    row_used = load_ids < jnp.sum(my_lengths)
    token_grad = jnp.where(row_used[:, None], back_grads[back_ids], zero_bf)
    return (mixed_out, token_grad, proj_grad, out_grad)


def solution(mesh):
    in_specs = (P("dp", "tensor"), P("dp", "tensor"), P(), P(), P(), P(), P())
    out_specs = (P("dp", "tensor"), P("dp", "tensor"), P("dp", None, "tensor"), P("tensor", "dp"))
    return jax.shard_map(local, mesh=mesh, in_specs=in_specs, out_specs=out_specs, check_vma=False)
```

```python
import math

import jax
import jax.numpy as jnp
from jax import lax
from jax.sharding import PartitionSpec as P

D = 1024
H = 8
MAXLEN = 192


norm_eps = 1e-05


def silu_slope(argument):
    sigmoid_val = jax.nn.sigmoid(argument)
    return sigmoid_val * (1.0 + argument * (1.0 - sigmoid_val))


def exclusive_sum(counts):
    return jnp.cumsum(counts) - counts


def local(tokens, cotangent, lengths, owners, proj_weight, norm_gain, out_weight):
    f32 = jnp.float32
    bf16 = jnp.bfloat16
    dp_count = lax.axis_size("dp")
    tensor_count = lax.axis_size("tensor")
    dp_index = lax.axis_index("dp")
    tensor_index = lax.axis_index("tensor")
    col_width = tokens.shape[1]
    load_rows = tokens.shape[0]
    head_dim = D // H
    score_scale = 1.0 / math.sqrt(head_dim)
    owned_rows = dp_count * (9 * MAXLEN // 16)
    places = jnp.arange(MAXLEN, dtype=jnp.int32)
    peer_ids = jnp.arange(dp_count, dtype=jnp.int32)
    seq_ids = jnp.arange(lengths.shape[1], dtype=jnp.int32)
    zero_bf = jnp.zeros((), bf16)

    my_lengths = lengths[dp_index]
    my_owners = owners[dp_index]
    my_starts = exclusive_sum(my_lengths)
    sent_to = my_owners[None, :] == peer_ids[:, None]
    send_start = jnp.sum(jnp.where(sent_to, my_starts[None, :], 0), axis=1)
    send_ids = jnp.minimum(send_start[:, None] + places[None, :], load_rows - 1)
    both = jnp.concatenate([tokens, cotangent], axis=1)
    send_both = both[send_ids]
    recv_both = lax.all_to_all(send_both, "dp", split_axis=0, concat_axis=0, tiled=True)

    recv_len = jnp.sum(jnp.where(owners == dp_index, lengths, 0), axis=1)
    recv_start = exclusive_sum(recv_len)
    compact_ids = jnp.arange(owned_rows, dtype=jnp.int32)
    compact_slot = (
        jnp.sum((compact_ids[:, None] >= recv_start[None, :]).astype(jnp.int32), axis=1) - 1
    )
    slot_pick = compact_slot[:, None] == peer_ids[None, :]
    compact_start = jnp.sum(jnp.where(slot_pick, recv_start[None, :], 0), axis=1)
    gather_ids = compact_slot * MAXLEN + compact_ids - compact_start
    own_both = recv_both.reshape(dp_count * MAXLEN, 2 * col_width)[gather_ids]
    own_tokens = own_both[:, :col_width]
    own_cotan = own_both[:, col_width:]

    gathered = lax.all_gather(own_both, "tensor", axis=0, tiled=False)
    g_tok = gathered[..., :col_width]
    g_cot = gathered[..., col_width:]

    head_start = tensor_index * H // tensor_count * head_dim
    own_start = tensor_index * col_width
    inner_start = own_start - head_start
    head_proj = lax.dynamic_slice_in_dim(proj_weight, head_start, head_dim, 2).reshape(
        tensor_count, col_width, 4 * head_dim
    )
    own_proj = lax.dynamic_slice_in_dim(proj_weight, own_start, col_width, 2).reshape(
        tensor_count, col_width, 4 * col_width
    )
    head_out = lax.dynamic_slice_in_dim(out_weight, head_start, head_dim, 0).reshape(
        head_dim, tensor_count, col_width
    )
    head_gain = lax.dynamic_slice_in_dim(norm_gain, head_start, head_dim, 0)

    projected = jnp.einsum("trc,tcn->rn", g_tok, head_proj, preferred_element_type=f32)
    down_grad = jnp.einsum("trc,dtc->rd", g_cot, head_out, preferred_element_type=f32)
    proj4 = projected.reshape(owned_rows, 4, head_dim)
    activated = jax.nn.silu(proj4).astype(bf16)
    gating = activated[:, 0]
    values = activated[:, 1]
    queries = activated[:, 2]
    keys_head = activated[:, 3]
    scores = jnp.einsum("md,nd->mn", queries, keys_head, preferred_element_type=f32)
    allowed = (compact_slot[:, None] == compact_slot[None, :]) & (
        compact_ids[:, None] >= compact_ids[None, :]
    )
    weights = jnp.where(allowed, jax.nn.silu(scores * score_scale) / MAXLEN, 0.0).astype(bf16)
    attended = jnp.einsum("mn,nd->md", weights, values, preferred_element_type=f32)
    inv_rms = lax.rsqrt(jnp.mean(attended * attended, axis=-1, keepdims=True) + norm_eps)
    normed = attended * inv_rms * head_gain
    gated = (normed * gating).astype(bf16)
    own_gated = lax.dynamic_slice_in_dim(gated, inner_start, col_width, 1)
    g_gated = lax.all_gather(own_gated, "tensor", axis=0, tiled=False)
    out_cols = lax.dynamic_slice_in_dim(out_weight, own_start, col_width, 1).reshape(
        tensor_count, col_width, col_width
    )
    out_sum = jnp.einsum("trc,tck->rk", g_gated, out_cols, preferred_element_type=f32)
    mixed_out = (own_tokens.astype(f32) + out_sum).astype(bf16)

    d_normed = down_grad * gating
    d_gating = down_grad * normed
    scaled = head_gain * d_normed
    d_attended = (
        inv_rms * scaled
        - attended * inv_rms**3 * jnp.mean(attended * scaled, axis=-1, keepdims=True)
    ).astype(bf16)
    d_weights = jnp.einsum("md,nd->mn", d_attended, values, preferred_element_type=f32)
    d_values = jnp.einsum("mn,md->nd", weights, d_attended, preferred_element_type=f32)
    d_scores = jnp.where(
        allowed, d_weights * silu_slope(scores * score_scale) * (score_scale / MAXLEN), 0.0
    ).astype(bf16)
    d_queries = jnp.einsum("mn,nd->md", d_scores, keys_head, preferred_element_type=f32)
    d_keys = jnp.einsum("mn,md->nd", d_scores, queries, preferred_element_type=f32)
    d_activated = jnp.stack([d_gating, d_values, d_queries, d_keys], axis=1)
    d_projected = (d_activated * silu_slope(proj4)).astype(bf16)
    own_grad = lax.dynamic_slice_in_dim(d_projected, inner_start, col_width, 2).reshape(
        owned_rows, 4 * col_width
    )
    grad_part = jnp.einsum("rn,tkn->trk", own_grad, own_proj, preferred_element_type=f32)
    grad_pieces = lax.all_to_all(
        grad_part.astype(bf16), "tensor", split_axis=0, concat_axis=0, tiled=True
    )
    grad_sum = jnp.sum(grad_pieces.astype(f32), axis=0)
    token_rows = (own_cotan.astype(f32) + grad_sum).astype(bf16)

    proj_term = jnp.einsum("trc,rn->tcn", g_tok, own_grad, preferred_element_type=f32)
    out_term = jnp.einsum("trc,rd->tcd", g_cot, own_gated, preferred_element_type=f32)
    terms = jnp.concatenate(
        [proj_term.reshape(D, 4 * col_width), out_term.reshape(D, col_width)], axis=1
    ).astype(bf16)
    term_pieces = lax.all_to_all(
        terms.reshape(dp_count, D // dp_count, 5 * col_width), "dp", 0, 0, tiled=True
    )
    term_sum = jnp.sum(term_pieces.astype(f32), axis=0)
    proj_grad = term_sum[:, : 4 * col_width].reshape(-1, 4, col_width)
    out_grad = term_sum[:, 4 * col_width :].T

    back_src = jnp.minimum(recv_start[:, None] + places[None, :], owned_rows - 1)
    back_send = token_rows[back_src]
    back_grads = lax.all_to_all(back_send, "dp", split_axis=0, concat_axis=0, tiled=True)
    back_grads = back_grads.reshape(dp_count * MAXLEN, col_width)
    load_ids = jnp.arange(load_rows, dtype=jnp.int32)
    seq_of = jnp.sum((load_ids[:, None] >= my_starts[None, :]).astype(jnp.int32), axis=1) - 1
    seq_pick = seq_of[:, None] == seq_ids[None, :]
    owner_of = jnp.sum(jnp.where(seq_pick, my_owners[None, :], 0), axis=1)
    start_of = jnp.sum(jnp.where(seq_pick, my_starts[None, :], 0), axis=1)
    back_ids = owner_of * MAXLEN + jnp.minimum(load_ids - start_of, MAXLEN - 1)
    row_used = load_ids < jnp.sum(my_lengths)
    token_grad = jnp.where(row_used[:, None], back_grads[back_ids], zero_bf)
    return (mixed_out, token_grad, proj_grad, out_grad)


def solution(mesh):
    in_specs = (P("dp", "tensor"), P("dp", "tensor"), P(), P(), P(), P(), P())
    out_specs = (P("dp", "tensor"), P("dp", "tensor"), P("dp", None, "tensor"), P("tensor", "dp"))
    return jax.shard_map(local, mesh=mesh, in_specs=in_specs, out_specs=out_specs, check_vma=False)
```

```python
import math

import jax
import jax.numpy as jnp
from jax import lax
from jax.sharding import PartitionSpec as P

D = 1024
H = 8
MAXLEN = 192


norm_eps = 1e-05


def silu_slope(argument):
    sigmoid_val = jax.nn.sigmoid(argument)
    return sigmoid_val * (1.0 + argument * (1.0 - sigmoid_val))


def exclusive_sum(counts):
    return jnp.cumsum(counts) - counts


def local(tokens, cotangent, lengths, owners, proj_weight, norm_gain, out_weight):
    f32 = jnp.float32
    bf16 = jnp.bfloat16
    dp_count = lax.axis_size("dp")
    tensor_count = lax.axis_size("tensor")
    dp_index = lax.axis_index("dp")
    tensor_index = lax.axis_index("tensor")
    col_width = tokens.shape[1]
    load_rows = tokens.shape[0]
    head_dim = D // H
    score_scale = 1.0 / math.sqrt(head_dim)
    owned_rows = dp_count * (9 * MAXLEN // 16)
    places = jnp.arange(MAXLEN, dtype=jnp.int32)
    peer_ids = jnp.arange(dp_count, dtype=jnp.int32)
    zero_bf = jnp.zeros((), bf16)

    my_lengths = lengths[dp_index]
    my_owners = owners[dp_index]
    my_starts = exclusive_sum(my_lengths)
    sent_to = my_owners[None, :] == peer_ids[:, None]
    send_start = jnp.sum(jnp.where(sent_to, my_starts[None, :], 0), axis=1)
    both = jnp.concatenate([tokens, cotangent], axis=1)
    both_pad = jnp.concatenate([both, jnp.zeros((MAXLEN, 2 * col_width), bf16)], axis=0)
    send_both = jnp.stack(
        [lax.dynamic_slice_in_dim(both_pad, send_start[p], MAXLEN, 0) for p in range(dp_count)]
    )
    recv_both = lax.all_to_all(send_both, "dp", split_axis=0, concat_axis=0, tiled=True)

    recv_len = jnp.sum(jnp.where(owners == dp_index, lengths, 0), axis=1)
    recv_start = exclusive_sum(recv_len)
    compact_ids = jnp.arange(owned_rows, dtype=jnp.int32)
    compact_slot = (
        jnp.sum((compact_ids[:, None] >= recv_start[None, :]).astype(jnp.int32), axis=1) - 1
    )
    own_buf = jnp.zeros((owned_rows + MAXLEN, 2 * col_width), bf16)
    for j in range(dp_count):
        own_buf = lax.dynamic_update_slice_in_dim(own_buf, recv_both[j], recv_start[j], 0)
    own_both = own_buf[:owned_rows]
    own_tokens = own_both[:, :col_width]
    own_cotan = own_both[:, col_width:]

    gathered = lax.all_gather(own_both, "tensor", axis=0, tiled=False)
    g_tok = gathered[..., :col_width]
    g_cot = gathered[..., col_width:]

    head_start = tensor_index * H // tensor_count * head_dim
    own_start = tensor_index * col_width
    inner_start = own_start - head_start
    head_proj = lax.dynamic_slice_in_dim(proj_weight, head_start, head_dim, 2).reshape(
        tensor_count, col_width, 4 * head_dim
    )
    own_proj = lax.dynamic_slice_in_dim(proj_weight, own_start, col_width, 2).reshape(
        tensor_count, col_width, 4 * col_width
    )
    head_out = lax.dynamic_slice_in_dim(out_weight, head_start, head_dim, 0).reshape(
        head_dim, tensor_count, col_width
    )
    head_gain = lax.dynamic_slice_in_dim(norm_gain, head_start, head_dim, 0)

    projected = jnp.einsum("trc,tcn->rn", g_tok, head_proj, preferred_element_type=f32)
    down_grad = jnp.einsum("trc,dtc->rd", g_cot, head_out, preferred_element_type=f32)
    proj4 = projected.reshape(owned_rows, 4, head_dim)
    activated = jax.nn.silu(proj4).astype(bf16)
    gating = activated[:, 0]
    values = activated[:, 1]
    queries = activated[:, 2]
    keys_head = activated[:, 3]
    scores = jnp.einsum("md,nd->mn", queries, keys_head, preferred_element_type=f32)
    allowed = (compact_slot[:, None] == compact_slot[None, :]) & (
        compact_ids[:, None] >= compact_ids[None, :]
    )
    weights = jnp.where(allowed, jax.nn.silu(scores * score_scale) / MAXLEN, 0.0).astype(bf16)
    attended = jnp.einsum("mn,nd->md", weights, values, preferred_element_type=f32)
    inv_rms = lax.rsqrt(jnp.mean(attended * attended, axis=-1, keepdims=True) + norm_eps)
    normed = attended * inv_rms * head_gain
    gated = (normed * gating).astype(bf16)
    own_gated = lax.dynamic_slice_in_dim(gated, inner_start, col_width, 1)
    own_out = lax.dynamic_slice_in_dim(out_weight, own_start, col_width, 0).reshape(
        col_width, tensor_count, col_width
    )
    out_part = jnp.einsum("rc,ctk->trk", own_gated, own_out, preferred_element_type=f32)
    out_sum = lax.psum_scatter(
        out_part.astype(bf16), "tensor", scatter_dimension=0, tiled=True
    ).reshape(owned_rows, col_width)
    mixed_out = (own_tokens.astype(f32) + out_sum.astype(f32)).astype(bf16)

    d_normed = down_grad * gating
    d_gating = down_grad * normed
    scaled = head_gain * d_normed
    d_attended = (
        inv_rms * scaled
        - attended * inv_rms**3 * jnp.mean(attended * scaled, axis=-1, keepdims=True)
    ).astype(bf16)
    d_weights = jnp.einsum("md,nd->mn", d_attended, values, preferred_element_type=f32)
    d_values = jnp.einsum("mn,md->nd", weights, d_attended, preferred_element_type=f32)
    d_scores = jnp.where(
        allowed, d_weights * silu_slope(scores * score_scale) * (score_scale / MAXLEN), 0.0
    ).astype(bf16)
    d_queries = jnp.einsum("mn,nd->md", d_scores, keys_head, preferred_element_type=f32)
    d_keys = jnp.einsum("mn,md->nd", d_scores, queries, preferred_element_type=f32)
    d_activated = jnp.stack([d_gating, d_values, d_queries, d_keys], axis=1)
    d_projected = (d_activated * silu_slope(proj4)).astype(bf16)
    own_grad = lax.dynamic_slice_in_dim(d_projected, inner_start, col_width, 2).reshape(
        owned_rows, 4 * col_width
    )
    grad_part = jnp.einsum("rn,tkn->trk", own_grad, own_proj, preferred_element_type=f32)
    grad_pieces = lax.all_to_all(
        grad_part.astype(bf16), "tensor", split_axis=0, concat_axis=0, tiled=True
    )
    grad_sum = jnp.sum(grad_pieces.astype(f32), axis=0)
    token_rows = (own_cotan.astype(f32) + grad_sum).astype(bf16)

    proj_term = jnp.einsum("trc,rn->tcn", g_tok, own_grad, preferred_element_type=f32)
    out_term = jnp.einsum("trc,rd->tcd", g_cot, own_gated, preferred_element_type=f32)
    terms = jnp.concatenate(
        [proj_term.reshape(D, 4 * col_width), out_term.reshape(D, col_width)], axis=1
    ).astype(bf16)
    term_sum = lax.psum_scatter(terms, "dp", scatter_dimension=0, tiled=True).astype(f32)
    proj_grad = term_sum[:, : 4 * col_width].reshape(-1, 4, col_width)
    out_grad = term_sum[:, 4 * col_width :].T

    rows_pad = jnp.concatenate([token_rows, jnp.zeros((MAXLEN, col_width), bf16)], axis=0)
    back_send = jnp.stack(
        [lax.dynamic_slice_in_dim(rows_pad, recv_start[j], MAXLEN, 0) for j in range(dp_count)]
    )
    back_grads = lax.all_to_all(back_send, "dp", split_axis=0, concat_axis=0, tiled=True)
    grad_buf = jnp.zeros((load_rows + MAXLEN, col_width), bf16)
    for i in range(lengths.shape[1]):
        slab = lax.dynamic_index_in_dim(back_grads, my_owners[i], 0, keepdims=False)
        grad_buf = lax.dynamic_update_slice_in_dim(grad_buf, slab, my_starts[i], 0)
    load_ids = jnp.arange(load_rows, dtype=jnp.int32)
    row_used = load_ids < jnp.sum(my_lengths)
    token_grad = jnp.where(row_used[:, None], grad_buf[:load_rows], zero_bf)
    return (mixed_out, token_grad, proj_grad, out_grad)


def solution(mesh):
    in_specs = (P("dp", "tensor"), P("dp", "tensor"), P(), P(), P(), P(), P())
    out_specs = (P("dp", "tensor"), P("dp", "tensor"), P("dp", None, "tensor"), P("tensor", "dp"))
    return jax.shard_map(local, mesh=mesh, in_specs=in_specs, out_specs=out_specs, check_vma=False)
```

```python
import math

import jax
import jax.numpy as jnp
from jax import lax
from jax.sharding import PartitionSpec as P

D = 1024
H = 8
MAXLEN = 192


norm_eps = 1e-05


def silu_slope(argument):
    sigmoid_val = jax.nn.sigmoid(argument)
    return sigmoid_val * (1.0 + argument * (1.0 - sigmoid_val))


def exclusive_sum(counts):
    return jnp.cumsum(counts) - counts


def local(tokens, cotangent, lengths, owners, proj_weight, norm_gain, out_weight):
    f32 = jnp.float32
    bf16 = jnp.bfloat16
    dp_count = lax.axis_size("dp")
    tensor_count = lax.axis_size("tensor")
    dp_index = lax.axis_index("dp")
    tensor_index = lax.axis_index("tensor")
    col_width = tokens.shape[1]
    load_rows = tokens.shape[0]
    head_dim = D // H
    score_scale = 1.0 / math.sqrt(head_dim)
    owned_rows = dp_count * (9 * MAXLEN // 16)
    places = jnp.arange(MAXLEN, dtype=jnp.int32)
    peer_ids = jnp.arange(dp_count, dtype=jnp.int32)
    seq_ids = jnp.arange(lengths.shape[1], dtype=jnp.int32)
    zero_bf = jnp.zeros((), bf16)

    my_lengths = lengths[dp_index]
    my_owners = owners[dp_index]
    my_starts = exclusive_sum(my_lengths)
    sent_to = my_owners[None, :] == peer_ids[:, None]
    send_start = jnp.sum(jnp.where(sent_to, my_starts[None, :], 0), axis=1)
    send_ids = jnp.minimum(send_start[:, None] + places[None, :], load_rows - 1)
    both = jnp.concatenate([tokens, cotangent], axis=1)
    send_both = both[send_ids]
    recv_both = lax.all_to_all(send_both, "dp", split_axis=0, concat_axis=0, tiled=True)

    recv_len = jnp.sum(jnp.where(owners == dp_index, lengths, 0), axis=1)
    recv_start = exclusive_sum(recv_len)
    compact_ids = jnp.arange(owned_rows, dtype=jnp.int32)
    compact_slot = (
        jnp.sum((compact_ids[:, None] >= recv_start[None, :]).astype(jnp.int32), axis=1) - 1
    )
    slot_pick = compact_slot[:, None] == peer_ids[None, :]
    compact_start = jnp.sum(jnp.where(slot_pick, recv_start[None, :], 0), axis=1)
    gather_ids = compact_slot * MAXLEN + compact_ids - compact_start
    own_both = recv_both.reshape(dp_count * MAXLEN, 2 * col_width)[gather_ids]
    own_tokens = own_both[:, :col_width]
    own_cotan = own_both[:, col_width:]

    half_count = tensor_count // 2
    core = tensor_index % 2
    same_core = [[2 * z + c for z in range(half_count)] for c in range(2)]
    sibling = [(t, t ^ 1) for t in range(tensor_count)]
    mine = lax.all_gather(own_both, "tensor", axis=0, tiled=False, axis_index_groups=same_core)
    other = lax.ppermute(mine, "tensor", sibling)
    mine_tok, mine_cot = mine[..., :col_width], mine[..., col_width:]
    other_tok, other_cot = other[..., :col_width], other[..., col_width:]

    def by_core(weight, axis):
        split = weight.reshape(weight.shape[:axis] + (half_count, 2) + weight.shape[axis + 1 :])
        return (
            lax.dynamic_index_in_dim(split, core, axis + 1, keepdims=False),
            lax.dynamic_index_in_dim(split, 1 - core, axis + 1, keepdims=False),
        )

    def reduce_blocks(part):
        keep, send = by_core(part, 0)
        pair_sum = (keep.astype(f32) + lax.ppermute(send, "tensor", sibling).astype(f32)).astype(bf16)
        pieces = lax.all_to_all(pair_sum, "tensor", 0, 0, tiled=True, axis_index_groups=same_core)
        return jnp.sum(pieces.astype(f32), axis=0)

    head_start = tensor_index * H // tensor_count * head_dim
    own_start = tensor_index * col_width
    inner_start = own_start - head_start
    head_proj = lax.dynamic_slice_in_dim(proj_weight, head_start, head_dim, 2).reshape(
        tensor_count, col_width, 4 * head_dim
    )
    own_proj = lax.dynamic_slice_in_dim(proj_weight, own_start, col_width, 2).reshape(
        tensor_count, col_width, 4 * col_width
    )
    head_out = lax.dynamic_slice_in_dim(out_weight, head_start, head_dim, 0).reshape(
        head_dim, tensor_count, col_width
    )
    head_gain = lax.dynamic_slice_in_dim(norm_gain, head_start, head_dim, 0)

    proj_mine, proj_other = by_core(head_proj, 0)
    projected = jnp.einsum(
        "trc,tcn->rn", mine_tok, proj_mine, preferred_element_type=f32
    ) + jnp.einsum("trc,tcn->rn", other_tok, proj_other, preferred_element_type=f32)
    out_mine, out_other = by_core(head_out, 1)
    down_grad = jnp.einsum(
        "trc,dtc->rd", mine_cot, out_mine, preferred_element_type=f32
    ) + jnp.einsum("trc,dtc->rd", other_cot, out_other, preferred_element_type=f32)
    proj4 = projected.reshape(owned_rows, 4, head_dim)
    activated = jax.nn.silu(proj4).astype(bf16)
    gating = activated[:, 0]
    values = activated[:, 1]
    queries = activated[:, 2]
    keys_head = activated[:, 3]
    scores = jnp.einsum("md,nd->mn", queries, keys_head, preferred_element_type=f32)
    allowed = (compact_slot[:, None] == compact_slot[None, :]) & (
        compact_ids[:, None] >= compact_ids[None, :]
    )
    weights = jnp.where(allowed, jax.nn.silu(scores * score_scale) / MAXLEN, 0.0).astype(bf16)
    attended = jnp.einsum("mn,nd->md", weights, values, preferred_element_type=f32)
    inv_rms = lax.rsqrt(jnp.mean(attended * attended, axis=-1, keepdims=True) + norm_eps)
    normed = attended * inv_rms * head_gain
    gated = (normed * gating).astype(bf16)
    own_gated = lax.dynamic_slice_in_dim(gated, inner_start, col_width, 1)
    own_out = lax.dynamic_slice_in_dim(out_weight, own_start, col_width, 0).reshape(
        col_width, tensor_count, col_width
    )
    out_part = jnp.einsum("rc,ctk->trk", own_gated, own_out, preferred_element_type=f32)
    out_sum = reduce_blocks(out_part.astype(bf16))
    mixed_out = (own_tokens.astype(f32) + out_sum).astype(bf16)

    d_normed = down_grad * gating
    d_gating = down_grad * normed
    scaled = head_gain * d_normed
    d_attended = (
        inv_rms * scaled
        - attended * inv_rms**3 * jnp.mean(attended * scaled, axis=-1, keepdims=True)
    ).astype(bf16)
    d_weights = jnp.einsum("md,nd->mn", d_attended, values, preferred_element_type=f32)
    d_values = jnp.einsum("mn,md->nd", weights, d_attended, preferred_element_type=f32)
    d_scores = jnp.where(
        allowed, d_weights * silu_slope(scores * score_scale) * (score_scale / MAXLEN), 0.0
    ).astype(bf16)
    d_queries = jnp.einsum("mn,nd->md", d_scores, keys_head, preferred_element_type=f32)
    d_keys = jnp.einsum("mn,md->nd", d_scores, queries, preferred_element_type=f32)
    d_activated = jnp.stack([d_gating, d_values, d_queries, d_keys], axis=1)
    d_projected = (d_activated * silu_slope(proj4)).astype(bf16)
    own_grad = lax.dynamic_slice_in_dim(d_projected, inner_start, col_width, 2).reshape(
        owned_rows, 4 * col_width
    )
    grad_part = jnp.einsum("rn,tkn->trk", own_grad, own_proj, preferred_element_type=f32)
    grad_sum = reduce_blocks(grad_part.astype(bf16))
    token_rows = (own_cotan.astype(f32) + grad_sum).astype(bf16)

    def by_rows(term_mine, term_other):
        pair = jnp.stack([term_mine, term_other], axis=1)
        pair = jnp.where(core == 0, pair, pair[:, ::-1])
        return pair.reshape((D,) + term_mine.shape[2:])

    proj_term = by_rows(
        jnp.einsum("trc,rn->tcn", mine_tok, own_grad, preferred_element_type=f32),
        jnp.einsum("trc,rn->tcn", other_tok, own_grad, preferred_element_type=f32),
    )
    out_term = by_rows(
        jnp.einsum("trc,rd->tcd", mine_cot, own_gated, preferred_element_type=f32),
        jnp.einsum("trc,rd->tcd", other_cot, own_gated, preferred_element_type=f32),
    )
    terms = jnp.concatenate([proj_term, out_term], axis=1).astype(bf16)
    term_sum = lax.psum_scatter(terms, "dp", scatter_dimension=0, tiled=True).astype(f32)
    proj_grad = term_sum[:, : 4 * col_width].reshape(-1, 4, col_width)
    out_grad = term_sum[:, 4 * col_width :].T

    back_src = jnp.minimum(recv_start[:, None] + places[None, :], owned_rows - 1)
    back_send = token_rows[back_src]
    back_grads = lax.all_to_all(back_send, "dp", split_axis=0, concat_axis=0, tiled=True)
    back_grads = back_grads.reshape(dp_count * MAXLEN, col_width)
    load_ids = jnp.arange(load_rows, dtype=jnp.int32)
    seq_of = jnp.sum((load_ids[:, None] >= my_starts[None, :]).astype(jnp.int32), axis=1) - 1
    seq_pick = seq_of[:, None] == seq_ids[None, :]
    owner_of = jnp.sum(jnp.where(seq_pick, my_owners[None, :], 0), axis=1)
    start_of = jnp.sum(jnp.where(seq_pick, my_starts[None, :], 0), axis=1)
    back_ids = owner_of * MAXLEN + jnp.minimum(load_ids - start_of, MAXLEN - 1)
    row_used = load_ids < jnp.sum(my_lengths)
    token_grad = jnp.where(row_used[:, None], back_grads[back_ids], zero_bf)
    return (mixed_out, token_grad, proj_grad, out_grad)


def solution(mesh):
    in_specs = (P("dp", "tensor"), P("dp", "tensor"), P(), P(), P(), P(), P())
    out_specs = (P("dp", "tensor"), P("dp", "tensor"), P("dp", None, "tensor"), P("tensor", "dp"))
    return jax.shard_map(local, mesh=mesh, in_specs=in_specs, out_specs=out_specs, check_vma=False)
```

```python
import math

import jax
import jax.numpy as jnp
from jax import lax
from jax.sharding import PartitionSpec as P

D = 1024
H = 8
MAXLEN = 192


norm_eps = 1e-05


def silu_slope(argument):
    sigmoid_val = jax.nn.sigmoid(argument)
    return sigmoid_val * (1.0 + argument * (1.0 - sigmoid_val))


def exclusive_sum(counts):
    return jnp.cumsum(counts) - counts


def local(tokens, cotangent, lengths, owners, proj_weight, norm_gain, out_weight):
    f32 = jnp.float32
    bf16 = jnp.bfloat16
    dp_count = lax.axis_size("dp")
    tensor_count = lax.axis_size("tensor")
    dp_index = lax.axis_index("dp")
    tensor_index = lax.axis_index("tensor")
    col_width = tokens.shape[1]
    load_rows = tokens.shape[0]
    head_dim = D // H
    score_scale = 1.0 / math.sqrt(head_dim)
    owned_rows = dp_count * (9 * MAXLEN // 16)
    places = jnp.arange(MAXLEN, dtype=jnp.int32)
    peer_ids = jnp.arange(dp_count, dtype=jnp.int32)
    seq_ids = jnp.arange(lengths.shape[1], dtype=jnp.int32)
    zero_bf = jnp.zeros((), bf16)

    my_lengths = lengths[dp_index]
    my_owners = owners[dp_index]
    my_starts = exclusive_sum(my_lengths)
    sent_to = my_owners[None, :] == peer_ids[:, None]
    send_start = jnp.sum(jnp.where(sent_to, my_starts[None, :], 0), axis=1)
    send_ids = jnp.minimum(send_start[:, None] + places[None, :], load_rows - 1)
    both = jnp.concatenate([tokens, cotangent], axis=1)
    send_both = both[send_ids]
    recv_both = lax.all_to_all(send_both, "dp", split_axis=0, concat_axis=0, tiled=True)

    recv_len = jnp.sum(jnp.where(owners == dp_index, lengths, 0), axis=1)
    recv_start = exclusive_sum(recv_len)
    compact_ids = jnp.arange(owned_rows, dtype=jnp.int32)
    compact_slot = (
        jnp.sum((compact_ids[:, None] >= recv_start[None, :]).astype(jnp.int32), axis=1) - 1
    )
    slot_pick = compact_slot[:, None] == peer_ids[None, :]
    compact_start = jnp.sum(jnp.where(slot_pick, recv_start[None, :], 0), axis=1)
    gather_ids = compact_slot * MAXLEN + compact_ids - compact_start
    own_both = recv_both.reshape(dp_count * MAXLEN, 2 * col_width)[gather_ids]
    own_tokens = own_both[:, :col_width]
    own_cotan = own_both[:, col_width:]

    half_count = tensor_count // 2
    core = tensor_index % 2
    same_core = [[2 * z + c for z in range(half_count)] for c in range(2)]
    sibling = [(t, t ^ 1) for t in range(tensor_count)]
    mine = lax.all_gather(own_both, "tensor", axis=0, tiled=False, axis_index_groups=same_core)
    other = lax.ppermute(mine, "tensor", sibling)
    mine_tok, mine_cot = mine[..., :col_width], mine[..., col_width:]
    other_tok, other_cot = other[..., :col_width], other[..., col_width:]

    def by_core(weight, axis):
        split = weight.reshape(weight.shape[:axis] + (half_count, 2) + weight.shape[axis + 1 :])
        return (
            lax.dynamic_index_in_dim(split, core, axis + 1, keepdims=False),
            lax.dynamic_index_in_dim(split, 1 - core, axis + 1, keepdims=False),
        )

    def reduce_blocks(part):
        keep, send = by_core(part, 0)
        pair_sum = (keep.astype(f32) + lax.ppermute(send, "tensor", sibling).astype(f32)).astype(bf16)
        pieces = lax.all_to_all(pair_sum, "tensor", 0, 0, tiled=True, axis_index_groups=same_core)
        return jnp.sum(pieces.astype(f32), axis=0)

    head_start = tensor_index * H // tensor_count * head_dim
    own_start = tensor_index * col_width
    inner_start = own_start - head_start
    head_proj = lax.dynamic_slice_in_dim(proj_weight, head_start, head_dim, 2).reshape(
        tensor_count, col_width, 4 * head_dim
    )
    own_proj = lax.dynamic_slice_in_dim(proj_weight, own_start, col_width, 2).reshape(
        tensor_count, col_width, 4 * col_width
    )
    head_out = lax.dynamic_slice_in_dim(out_weight, head_start, head_dim, 0).reshape(
        head_dim, tensor_count, col_width
    )
    head_gain = lax.dynamic_slice_in_dim(norm_gain, head_start, head_dim, 0)

    proj_mine, proj_other = by_core(head_proj, 0)
    projected = jnp.einsum(
        "trc,tcn->rn", mine_tok, proj_mine, preferred_element_type=f32
    ) + jnp.einsum("trc,tcn->rn", other_tok, proj_other, preferred_element_type=f32)
    out_mine, out_other = by_core(head_out, 1)
    down_grad = jnp.einsum(
        "trc,dtc->rd", mine_cot, out_mine, preferred_element_type=f32
    ) + jnp.einsum("trc,dtc->rd", other_cot, out_other, preferred_element_type=f32)
    proj4 = projected.reshape(owned_rows, 4, head_dim)
    activated = jax.nn.silu(proj4).astype(bf16)
    gating = activated[:, 0]
    values = activated[:, 1]
    queries = activated[:, 2]
    keys_head = activated[:, 3]
    scores = jnp.einsum("md,nd->mn", queries, keys_head, preferred_element_type=f32)
    allowed = (compact_slot[:, None] == compact_slot[None, :]) & (
        compact_ids[:, None] >= compact_ids[None, :]
    )
    weights = jnp.where(allowed, jax.nn.silu(scores * score_scale) / MAXLEN, 0.0).astype(bf16)
    attended = jnp.einsum("mn,nd->md", weights, values, preferred_element_type=f32)
    inv_rms = lax.rsqrt(jnp.mean(attended * attended, axis=-1, keepdims=True) + norm_eps)
    normed = attended * inv_rms * head_gain
    gated = (normed * gating).astype(bf16)
    own_gated = lax.dynamic_slice_in_dim(gated, inner_start, col_width, 1)
    own_out = lax.dynamic_slice_in_dim(out_weight, own_start, col_width, 0).reshape(
        col_width, tensor_count, col_width
    )
    out_part = jnp.einsum("rc,ctk->trk", own_gated, own_out, preferred_element_type=f32)

    d_normed = down_grad * gating
    d_gating = down_grad * normed
    scaled = head_gain * d_normed
    d_attended = (
        inv_rms * scaled
        - attended * inv_rms**3 * jnp.mean(attended * scaled, axis=-1, keepdims=True)
    ).astype(bf16)
    d_weights = jnp.einsum("md,nd->mn", d_attended, values, preferred_element_type=f32)
    d_values = jnp.einsum("mn,md->nd", weights, d_attended, preferred_element_type=f32)
    d_scores = jnp.where(
        allowed, d_weights * silu_slope(scores * score_scale) * (score_scale / MAXLEN), 0.0
    ).astype(bf16)
    d_queries = jnp.einsum("mn,nd->md", d_scores, keys_head, preferred_element_type=f32)
    d_keys = jnp.einsum("mn,md->nd", d_scores, queries, preferred_element_type=f32)
    d_activated = jnp.stack([d_gating, d_values, d_queries, d_keys], axis=1)
    d_projected = (d_activated * silu_slope(proj4)).astype(bf16)
    own_grad = lax.dynamic_slice_in_dim(d_projected, inner_start, col_width, 2).reshape(
        owned_rows, 4 * col_width
    )
    grad_part = jnp.einsum("rn,tkn->trk", own_grad, own_proj, preferred_element_type=f32)
    both_sum = reduce_blocks(jnp.concatenate([out_part, grad_part], axis=2).astype(bf16))
    out_sum = both_sum[:, :col_width]
    grad_sum = both_sum[:, col_width:]
    mixed_out = (own_tokens.astype(f32) + out_sum).astype(bf16)
    token_rows = (own_cotan.astype(f32) + grad_sum).astype(bf16)

    def by_rows(term_mine, term_other):
        pair = jnp.stack([term_mine, term_other], axis=1)
        pair = jnp.where(core == 0, pair, pair[:, ::-1])
        return pair.reshape((D,) + term_mine.shape[2:])

    proj_term = by_rows(
        jnp.einsum("trc,rn->tcn", mine_tok, own_grad, preferred_element_type=f32),
        jnp.einsum("trc,rn->tcn", other_tok, own_grad, preferred_element_type=f32),
    )
    out_term = by_rows(
        jnp.einsum("trc,rd->tcd", mine_cot, own_gated, preferred_element_type=f32),
        jnp.einsum("trc,rd->tcd", other_cot, own_gated, preferred_element_type=f32),
    )
    terms = jnp.concatenate([proj_term, out_term], axis=1).astype(bf16)
    term_sum = lax.psum_scatter(terms, "dp", scatter_dimension=0, tiled=True).astype(f32)
    proj_grad = term_sum[:, : 4 * col_width].reshape(-1, 4, col_width)
    out_grad = term_sum[:, 4 * col_width :].T

    back_src = jnp.minimum(recv_start[:, None] + places[None, :], owned_rows - 1)
    back_send = token_rows[back_src]
    back_grads = lax.all_to_all(back_send, "dp", split_axis=0, concat_axis=0, tiled=True)
    back_grads = back_grads.reshape(dp_count * MAXLEN, col_width)
    load_ids = jnp.arange(load_rows, dtype=jnp.int32)
    seq_of = jnp.sum((load_ids[:, None] >= my_starts[None, :]).astype(jnp.int32), axis=1) - 1
    seq_pick = seq_of[:, None] == seq_ids[None, :]
    owner_of = jnp.sum(jnp.where(seq_pick, my_owners[None, :], 0), axis=1)
    start_of = jnp.sum(jnp.where(seq_pick, my_starts[None, :], 0), axis=1)
    back_ids = owner_of * MAXLEN + jnp.minimum(load_ids - start_of, MAXLEN - 1)
    row_used = load_ids < jnp.sum(my_lengths)
    token_grad = jnp.where(row_used[:, None], back_grads[back_ids], zero_bf)
    return (mixed_out, token_grad, proj_grad, out_grad)


def solution(mesh):
    in_specs = (P("dp", "tensor"), P("dp", "tensor"), P(), P(), P(), P(), P())
    out_specs = (P("dp", "tensor"), P("dp", "tensor"), P("dp", None, "tensor"), P("tensor", "dp"))
    return jax.shard_map(local, mesh=mesh, in_specs=in_specs, out_specs=out_specs, check_vma=False)
```

```python
import math

import jax
import jax.numpy as jnp
from jax import lax
from jax.sharding import PartitionSpec as P

D = 1024
H = 8
MAXLEN = 192


norm_eps = 1e-05


def silu_slope(argument):
    sigmoid_val = jax.nn.sigmoid(argument)
    return sigmoid_val * (1.0 + argument * (1.0 - sigmoid_val))


def exclusive_sum(counts):
    return jnp.cumsum(counts) - counts


def local(tokens, cotangent, lengths, owners, proj_weight, norm_gain, out_weight):
    f32 = jnp.float32
    bf16 = jnp.bfloat16
    dp_count = lax.axis_size("dp")
    tensor_count = lax.axis_size("tensor")
    dp_index = lax.axis_index("dp")
    tensor_index = lax.axis_index("tensor")
    col_width = tokens.shape[1]
    load_rows = tokens.shape[0]
    head_dim = D // H
    score_scale = 1.0 / math.sqrt(head_dim)
    owned_rows = dp_count * (9 * MAXLEN // 16)
    places = jnp.arange(MAXLEN, dtype=jnp.int32)
    peer_ids = jnp.arange(dp_count, dtype=jnp.int32)
    seq_ids = jnp.arange(lengths.shape[1], dtype=jnp.int32)
    zero_bf = jnp.zeros((), bf16)

    my_lengths = lengths[dp_index]
    my_owners = owners[dp_index]
    my_starts = exclusive_sum(my_lengths)
    sent_to = my_owners[None, :] == peer_ids[:, None]
    send_start = jnp.sum(jnp.where(sent_to, my_starts[None, :], 0), axis=1)
    send_ids = jnp.minimum(send_start[:, None] + places[None, :], load_rows - 1)
    both = jnp.concatenate([tokens, cotangent], axis=1)
    send_both = both[send_ids]
    recv_both = lax.all_to_all(send_both, "dp", split_axis=0, concat_axis=0, tiled=True)

    recv_len = jnp.sum(jnp.where(owners == dp_index, lengths, 0), axis=1)
    recv_start = exclusive_sum(recv_len)
    compact_ids = jnp.arange(owned_rows, dtype=jnp.int32)
    compact_slot = (
        jnp.sum((compact_ids[:, None] >= recv_start[None, :]).astype(jnp.int32), axis=1) - 1
    )
    slot_pick = compact_slot[:, None] == peer_ids[None, :]
    compact_start = jnp.sum(jnp.where(slot_pick, recv_start[None, :], 0), axis=1)
    gather_ids = compact_slot * MAXLEN + compact_ids - compact_start
    own_both = recv_both.reshape(dp_count * MAXLEN, 2 * col_width)[gather_ids]
    own_tokens = own_both[:, :col_width]
    own_cotan = own_both[:, col_width:]

    half_count = tensor_count // 2
    core = tensor_index % 2
    same_core = [[2 * z + c for z in range(half_count)] for c in range(2)]
    sibling = [(t, t ^ 1) for t in range(tensor_count)]
    mine = lax.all_gather(own_both, "tensor", axis=0, tiled=False, axis_index_groups=same_core)
    other = lax.ppermute(mine, "tensor", sibling)
    mine_tok, mine_cot = mine[..., :col_width], mine[..., col_width:]
    other_tok, other_cot = other[..., :col_width], other[..., col_width:]

    def by_core(weight, axis):
        split = weight.reshape(weight.shape[:axis] + (half_count, 2) + weight.shape[axis + 1 :])
        return (
            lax.dynamic_index_in_dim(split, core, axis + 1, keepdims=False),
            lax.dynamic_index_in_dim(split, 1 - core, axis + 1, keepdims=False),
        )

    def reduce_blocks(part):
        keep, send = by_core(part, 0)
        pair_sum = (keep.astype(f32) + lax.ppermute(send, "tensor", sibling).astype(f32)).astype(bf16)
        pieces = lax.all_to_all(pair_sum, "tensor", 0, 0, tiled=True, axis_index_groups=same_core)
        return jnp.sum(pieces.astype(f32), axis=0)

    head_start = tensor_index * H // tensor_count * head_dim
    own_start = tensor_index * col_width
    inner_start = own_start - head_start
    head_proj = lax.dynamic_slice_in_dim(proj_weight, head_start, head_dim, 2).reshape(
        tensor_count, col_width, 4 * head_dim
    )
    own_proj = lax.dynamic_slice_in_dim(proj_weight, own_start, col_width, 2).reshape(
        tensor_count, col_width, 4 * col_width
    )
    head_out = lax.dynamic_slice_in_dim(out_weight, head_start, head_dim, 0).reshape(
        head_dim, tensor_count, col_width
    )
    head_gain = lax.dynamic_slice_in_dim(norm_gain, head_start, head_dim, 0)

    proj_mine, proj_other = by_core(head_proj, 0)
    projected = jnp.einsum(
        "trc,tcn->rn", mine_tok, proj_mine, preferred_element_type=f32
    ) + jnp.einsum("trc,tcn->rn", other_tok, proj_other, preferred_element_type=f32)
    out_mine, out_other = by_core(head_out, 1)
    down_grad = jnp.einsum(
        "trc,dtc->rd", mine_cot, out_mine, preferred_element_type=f32
    ) + jnp.einsum("trc,dtc->rd", other_cot, out_other, preferred_element_type=f32)
    proj4 = projected.reshape(owned_rows, 4, head_dim)
    activated = jax.nn.silu(proj4).astype(bf16)
    gating = activated[:, 0]
    values = activated[:, 1]
    queries = activated[:, 2]
    keys_head = activated[:, 3]
    scores = jnp.einsum("md,nd->mn", queries, keys_head, preferred_element_type=f32)
    allowed = (compact_slot[:, None] == compact_slot[None, :]) & (
        compact_ids[:, None] >= compact_ids[None, :]
    )
    weights = jnp.where(allowed, jax.nn.silu(scores * score_scale) / MAXLEN, 0.0).astype(bf16)
    attended = jnp.einsum("mn,nd->md", weights, values, preferred_element_type=f32)
    inv_rms = lax.rsqrt(jnp.mean(attended * attended, axis=-1, keepdims=True) + norm_eps)
    normed = attended * inv_rms * head_gain
    gated = (normed * gating).astype(bf16)
    own_gated = lax.dynamic_slice_in_dim(gated, inner_start, col_width, 1)
    own_out = lax.dynamic_slice_in_dim(out_weight, own_start, col_width, 0).reshape(
        col_width, tensor_count, col_width
    )
    out_part = jnp.einsum("rc,ctk->trk", own_gated, own_out, preferred_element_type=f32)

    d_normed = down_grad * gating
    d_gating = down_grad * normed
    scaled = head_gain * d_normed
    d_attended = (
        inv_rms * scaled
        - attended * inv_rms**3 * jnp.mean(attended * scaled, axis=-1, keepdims=True)
    ).astype(bf16)
    d_weights = jnp.einsum("md,nd->mn", d_attended, values, preferred_element_type=f32)
    d_values = jnp.einsum("mn,md->nd", weights, d_attended, preferred_element_type=f32)
    d_scores = jnp.where(
        allowed, d_weights * silu_slope(scores * score_scale) * (score_scale / MAXLEN), 0.0
    ).astype(bf16)
    d_queries = jnp.einsum("mn,nd->md", d_scores, keys_head, preferred_element_type=f32)
    d_keys = jnp.einsum("mn,md->nd", d_scores, queries, preferred_element_type=f32)
    d_activated = jnp.stack([d_gating, d_values, d_queries, d_keys], axis=1)
    d_projected = (d_activated * silu_slope(proj4)).astype(bf16)
    own_grad = lax.dynamic_slice_in_dim(d_projected, inner_start, col_width, 2).reshape(
        owned_rows, 4 * col_width
    )
    grad_part = jnp.einsum("rn,tkn->trk", own_grad, own_proj, preferred_element_type=f32)
    both_sum = reduce_blocks(jnp.concatenate([out_part, grad_part], axis=2).astype(bf16))
    out_sum = both_sum[:, :col_width]
    grad_sum = both_sum[:, col_width:]
    mixed_out = (own_tokens.astype(f32) + out_sum).astype(bf16)
    token_rows = (own_cotan.astype(f32) + grad_sum).astype(bf16)

    def by_rows(term_mine, term_other):
        pair = jnp.stack([term_mine, term_other], axis=1)
        pair = jnp.where(core == 0, pair, pair[:, ::-1])
        return pair.reshape((D,) + term_mine.shape[2:])

    proj_term = by_rows(
        jnp.einsum("trc,rn->tcn", mine_tok, own_grad, preferred_element_type=f32),
        jnp.einsum("trc,rn->tcn", other_tok, own_grad, preferred_element_type=f32),
    )
    out_term = by_rows(
        jnp.einsum("trc,rd->tcd", mine_cot, own_gated, preferred_element_type=f32),
        jnp.einsum("trc,rd->tcd", other_cot, own_gated, preferred_element_type=f32),
    )
    terms = jnp.concatenate([proj_term, out_term], axis=1).astype(bf16)
    bit_count = dp_count.bit_length() - 1
    term_sum = terms.reshape((2,) * bit_count + (D // dp_count,) + terms.shape[1:]).astype(f32)
    for level in range(bit_count - 1, -1, -1):
        my_bit = (dp_index >> level) & 1
        keep = lax.dynamic_index_in_dim(term_sum, my_bit, 0, keepdims=False)
        send = lax.dynamic_index_in_dim(term_sum, 1 - my_bit, 0, keepdims=False)
        partners = [(d, d ^ (1 << level)) for d in range(dp_count)]
        term_sum = keep + lax.ppermute(send.astype(bf16), "dp", partners).astype(f32)
    proj_grad = term_sum[:, : 4 * col_width].reshape(-1, 4, col_width)
    out_grad = term_sum[:, 4 * col_width :].T

    back_src = jnp.minimum(recv_start[:, None] + places[None, :], owned_rows - 1)
    back_send = token_rows[back_src]
    back_grads = lax.all_to_all(back_send, "dp", split_axis=0, concat_axis=0, tiled=True)
    back_grads = back_grads.reshape(dp_count * MAXLEN, col_width)
    load_ids = jnp.arange(load_rows, dtype=jnp.int32)
    seq_of = jnp.sum((load_ids[:, None] >= my_starts[None, :]).astype(jnp.int32), axis=1) - 1
    seq_pick = seq_of[:, None] == seq_ids[None, :]
    owner_of = jnp.sum(jnp.where(seq_pick, my_owners[None, :], 0), axis=1)
    start_of = jnp.sum(jnp.where(seq_pick, my_starts[None, :], 0), axis=1)
    back_ids = owner_of * MAXLEN + jnp.minimum(load_ids - start_of, MAXLEN - 1)
    row_used = load_ids < jnp.sum(my_lengths)
    token_grad = jnp.where(row_used[:, None], back_grads[back_ids], zero_bf)
    return (mixed_out, token_grad, proj_grad, out_grad)


def solution(mesh):
    in_specs = (P("dp", "tensor"), P("dp", "tensor"), P(), P(), P(), P(), P())
    out_specs = (P("dp", "tensor"), P("dp", "tensor"), P("dp", None, "tensor"), P("tensor", "dp"))
    return jax.shard_map(local, mesh=mesh, in_specs=in_specs, out_specs=out_specs, check_vma=False)
```

```python
import math

import jax
import jax.numpy as jnp
from jax import lax
from jax.sharding import PartitionSpec as P

D = 1024
H = 8
MAXLEN = 192


norm_eps = 1e-05


def silu_slope(argument):
    sigmoid_val = jax.nn.sigmoid(argument)
    return sigmoid_val * (1.0 + argument * (1.0 - sigmoid_val))


def exclusive_sum(counts):
    return jnp.cumsum(counts) - counts


def local(tokens, cotangent, lengths, owners, proj_weight, norm_gain, out_weight):
    f32 = jnp.float32
    bf16 = jnp.bfloat16
    dp_count = lax.axis_size("dp")
    tensor_count = lax.axis_size("tensor")
    dp_index = lax.axis_index("dp")
    tensor_index = lax.axis_index("tensor")
    col_width = tokens.shape[1]
    load_rows = tokens.shape[0]
    head_dim = D // H
    score_scale = 1.0 / math.sqrt(head_dim)
    owned_rows = dp_count * (9 * MAXLEN // 16)
    places = jnp.arange(MAXLEN, dtype=jnp.int32)
    peer_ids = jnp.arange(dp_count, dtype=jnp.int32)
    seq_ids = jnp.arange(lengths.shape[1], dtype=jnp.int32)

    my_lengths = lengths[dp_index]
    my_owners = owners[dp_index]
    my_starts = exclusive_sum(my_lengths)
    sent_to = my_owners[None, :] == peer_ids[:, None]
    send_start = jnp.sum(jnp.where(sent_to, my_starts[None, :], 0), axis=1)
    send_ids = jnp.minimum(send_start[:, None] + places[None, :], load_rows - 1)
    def pick_rows(row_ids, source):
        one_hot = (row_ids[:, None] == jnp.arange(source.shape[0], dtype=jnp.int32)[None, :]).astype(bf16)
        return jnp.dot(one_hot, source, preferred_element_type=f32).astype(bf16)

    flat_send = send_ids.reshape(-1)
    send_both = jnp.concatenate(
        [pick_rows(flat_send, tokens), pick_rows(flat_send, cotangent)], axis=1
    ).reshape(dp_count, MAXLEN, 2 * col_width)
    recv_both = lax.all_to_all(send_both, "dp", split_axis=0, concat_axis=0, tiled=True)

    recv_len = jnp.sum(jnp.where(owners == dp_index, lengths, 0), axis=1)
    recv_start = exclusive_sum(recv_len)
    compact_ids = jnp.arange(owned_rows, dtype=jnp.int32)
    compact_slot = (
        jnp.sum((compact_ids[:, None] >= recv_start[None, :]).astype(jnp.int32), axis=1) - 1
    )
    slot_pick = compact_slot[:, None] == peer_ids[None, :]
    compact_start = jnp.sum(jnp.where(slot_pick, recv_start[None, :], 0), axis=1)
    gather_ids = compact_slot * MAXLEN + compact_ids - compact_start
    own_both = pick_rows(gather_ids, recv_both.reshape(dp_count * MAXLEN, 2 * col_width))
    own_tokens = own_both[:, :col_width]
    own_cotan = own_both[:, col_width:]

    half_count = tensor_count // 2
    core = tensor_index % 2
    same_core = [[2 * z + c for z in range(half_count)] for c in range(2)]
    sibling = [(t, t ^ 1) for t in range(tensor_count)]
    mine = lax.all_gather(own_both, "tensor", axis=0, tiled=False, axis_index_groups=same_core)
    other = lax.ppermute(mine, "tensor", sibling)
    mine_tok, mine_cot = mine[..., :col_width], mine[..., col_width:]
    other_tok, other_cot = other[..., :col_width], other[..., col_width:]

    def by_core(weight, axis):
        split = weight.reshape(weight.shape[:axis] + (half_count, 2) + weight.shape[axis + 1 :])
        return (
            lax.dynamic_index_in_dim(split, core, axis + 1, keepdims=False),
            lax.dynamic_index_in_dim(split, 1 - core, axis + 1, keepdims=False),
        )

    def reduce_blocks(part):
        keep, send = by_core(part, 0)
        pair_sum = (keep.astype(f32) + lax.ppermute(send, "tensor", sibling).astype(f32)).astype(bf16)
        pieces = lax.all_to_all(pair_sum, "tensor", 0, 0, tiled=True, axis_index_groups=same_core)
        return jnp.sum(pieces.astype(f32), axis=0)

    head_start = tensor_index * H // tensor_count * head_dim
    own_start = tensor_index * col_width
    inner_start = own_start - head_start
    head_proj = lax.dynamic_slice_in_dim(proj_weight, head_start, head_dim, 2).reshape(
        tensor_count, col_width, 4 * head_dim
    )
    own_proj = lax.dynamic_slice_in_dim(proj_weight, own_start, col_width, 2).reshape(
        tensor_count, col_width, 4 * col_width
    )
    head_out = lax.dynamic_slice_in_dim(out_weight, head_start, head_dim, 0).reshape(
        head_dim, tensor_count, col_width
    )
    head_gain = lax.dynamic_slice_in_dim(norm_gain, head_start, head_dim, 0)

    proj_mine, proj_other = by_core(head_proj, 0)
    projected = jnp.einsum(
        "trc,tcn->rn", mine_tok, proj_mine, preferred_element_type=f32
    ) + jnp.einsum("trc,tcn->rn", other_tok, proj_other, preferred_element_type=f32)
    out_mine, out_other = by_core(head_out, 1)
    down_grad = jnp.einsum(
        "trc,dtc->rd", mine_cot, out_mine, preferred_element_type=f32
    ) + jnp.einsum("trc,dtc->rd", other_cot, out_other, preferred_element_type=f32)
    proj4 = projected.reshape(owned_rows, 4, head_dim)
    activated = jax.nn.silu(proj4).astype(bf16)
    gating = activated[:, 0]
    values = activated[:, 1]
    queries = activated[:, 2]
    keys_head = activated[:, 3]
    scores = jnp.einsum("md,nd->mn", queries, keys_head, preferred_element_type=f32)
    allowed = (compact_slot[:, None] == compact_slot[None, :]) & (
        compact_ids[:, None] >= compact_ids[None, :]
    )
    weights = jnp.where(allowed, jax.nn.silu(scores * score_scale) / MAXLEN, 0.0).astype(bf16)
    attended = jnp.einsum("mn,nd->md", weights, values, preferred_element_type=f32)
    inv_rms = lax.rsqrt(jnp.mean(attended * attended, axis=-1, keepdims=True) + norm_eps)
    normed = attended * inv_rms * head_gain
    gated = (normed * gating).astype(bf16)
    own_gated = lax.dynamic_slice_in_dim(gated, inner_start, col_width, 1)
    own_out = lax.dynamic_slice_in_dim(out_weight, own_start, col_width, 0).reshape(
        col_width, tensor_count, col_width
    )
    out_part = jnp.einsum("rc,ctk->trk", own_gated, own_out, preferred_element_type=f32)

    d_normed = down_grad * gating
    d_gating = down_grad * normed
    scaled = head_gain * d_normed
    d_attended = (
        inv_rms * scaled
        - attended * inv_rms**3 * jnp.mean(attended * scaled, axis=-1, keepdims=True)
    ).astype(bf16)
    d_weights = jnp.einsum("md,nd->mn", d_attended, values, preferred_element_type=f32)
    d_values = jnp.einsum("mn,md->nd", weights, d_attended, preferred_element_type=f32)
    d_scores = jnp.where(
        allowed, d_weights * silu_slope(scores * score_scale) * (score_scale / MAXLEN), 0.0
    ).astype(bf16)
    d_queries = jnp.einsum("mn,nd->md", d_scores, keys_head, preferred_element_type=f32)
    d_keys = jnp.einsum("mn,md->nd", d_scores, queries, preferred_element_type=f32)
    d_activated = jnp.stack([d_gating, d_values, d_queries, d_keys], axis=1)
    d_projected = (d_activated * silu_slope(proj4)).astype(bf16)
    own_grad = lax.dynamic_slice_in_dim(d_projected, inner_start, col_width, 2).reshape(
        owned_rows, 4 * col_width
    )
    grad_part = jnp.einsum("rn,tkn->trk", own_grad, own_proj, preferred_element_type=f32)
    both_sum = reduce_blocks(jnp.concatenate([out_part, grad_part], axis=2).astype(bf16))
    out_sum = both_sum[:, :col_width]
    grad_sum = both_sum[:, col_width:]
    mixed_out = (own_tokens.astype(f32) + out_sum).astype(bf16)
    token_rows = (own_cotan.astype(f32) + grad_sum).astype(bf16)

    def by_rows(term_mine, term_other):
        pair = jnp.stack([term_mine, term_other], axis=1)
        pair = jnp.where(core == 0, pair, pair[:, ::-1])
        return pair.reshape((D,) + term_mine.shape[2:])

    proj_term = by_rows(
        jnp.einsum("trc,rn->tcn", mine_tok, own_grad, preferred_element_type=f32),
        jnp.einsum("trc,rn->tcn", other_tok, own_grad, preferred_element_type=f32),
    )
    out_term = by_rows(
        jnp.einsum("trc,rd->tcd", mine_cot, own_gated, preferred_element_type=f32),
        jnp.einsum("trc,rd->tcd", other_cot, own_gated, preferred_element_type=f32),
    )
    terms = jnp.concatenate([proj_term, out_term], axis=1).astype(bf16)
    bit_count = dp_count.bit_length() - 1
    term_sum = terms.reshape((2,) * bit_count + (D // dp_count,) + terms.shape[1:]).astype(f32)
    for level in range(bit_count - 1, -1, -1):
        my_bit = (dp_index >> level) & 1
        keep = lax.dynamic_index_in_dim(term_sum, my_bit, 0, keepdims=False)
        send = lax.dynamic_index_in_dim(term_sum, 1 - my_bit, 0, keepdims=False)
        partners = [(d, d ^ (1 << level)) for d in range(dp_count)]
        term_sum = keep + lax.ppermute(send.astype(bf16), "dp", partners).astype(f32)
    proj_grad = term_sum[:, : 4 * col_width].reshape(-1, 4, col_width)
    out_grad = term_sum[:, 4 * col_width :].T

    back_src = jnp.minimum(recv_start[:, None] + places[None, :], owned_rows - 1)
    back_send = pick_rows(back_src.reshape(-1), token_rows).reshape(dp_count, MAXLEN, col_width)
    back_grads = lax.all_to_all(back_send, "dp", split_axis=0, concat_axis=0, tiled=True)
    back_grads = back_grads.reshape(dp_count * MAXLEN, col_width)
    load_ids = jnp.arange(load_rows, dtype=jnp.int32)
    seq_of = jnp.sum((load_ids[:, None] >= my_starts[None, :]).astype(jnp.int32), axis=1) - 1
    seq_pick = seq_of[:, None] == seq_ids[None, :]
    owner_of = jnp.sum(jnp.where(seq_pick, my_owners[None, :], 0), axis=1)
    start_of = jnp.sum(jnp.where(seq_pick, my_starts[None, :], 0), axis=1)
    back_ids = owner_of * MAXLEN + jnp.minimum(load_ids - start_of, MAXLEN - 1)
    row_used = load_ids < jnp.sum(my_lengths)
    token_grad = pick_rows(jnp.where(row_used, back_ids, -1), back_grads)
    return (mixed_out, token_grad, proj_grad, out_grad)


def solution(mesh):
    in_specs = (P("dp", "tensor"), P("dp", "tensor"), P(), P(), P(), P(), P())
    out_specs = (P("dp", "tensor"), P("dp", "tensor"), P("dp", None, "tensor"), P("tensor", "dp"))
    return jax.shard_map(local, mesh=mesh, in_specs=in_specs, out_specs=out_specs, check_vma=False)
```

```python
import math

import jax
import jax.numpy as jnp
from jax import lax
from jax.sharding import PartitionSpec as P

D = 1024
H = 8
MAXLEN = 192


norm_eps = 1e-05


def silu_slope(argument):
    sigmoid_val = jax.nn.sigmoid(argument)
    return sigmoid_val * (1.0 + argument * (1.0 - sigmoid_val))


def exclusive_sum(counts):
    return jnp.cumsum(counts) - counts


def local(tokens, cotangent, lengths, owners, proj_weight, norm_gain, out_weight):
    f32 = jnp.float32
    bf16 = jnp.bfloat16
    dp_count = lax.axis_size("dp")
    tensor_count = lax.axis_size("tensor")
    dp_index = lax.axis_index("dp")
    tensor_index = lax.axis_index("tensor")
    col_width = tokens.shape[1]
    load_rows = tokens.shape[0]
    head_dim = D // H
    score_scale = 1.0 / math.sqrt(head_dim)
    owned_rows = dp_count * (9 * MAXLEN // 16)
    places = jnp.arange(MAXLEN, dtype=jnp.int32)
    peer_ids = jnp.arange(dp_count, dtype=jnp.int32)
    seq_ids = jnp.arange(lengths.shape[1], dtype=jnp.int32)

    my_lengths = lengths[dp_index]
    my_owners = owners[dp_index]
    my_starts = exclusive_sum(my_lengths)
    sent_to = my_owners[None, :] == peer_ids[:, None]
    send_start = jnp.sum(jnp.where(sent_to, my_starts[None, :], 0), axis=1)
    send_ids = jnp.minimum(send_start[:, None] + places[None, :], load_rows - 1)
    def pick_rows(row_ids, source):
        one_hot = (row_ids[:, None] == jnp.arange(source.shape[0], dtype=jnp.int32)[None, :]).astype(bf16)
        return jnp.dot(one_hot, source, preferred_element_type=f32).astype(bf16)

    flat_send = send_ids.reshape(-1)
    send_both = jnp.concatenate(
        [pick_rows(flat_send, tokens), pick_rows(flat_send, cotangent)], axis=1
    ).reshape(dp_count, MAXLEN, 2 * col_width)
    recv_both = lax.all_to_all(send_both, "dp", split_axis=0, concat_axis=0, tiled=True)

    half_count = tensor_count // 2
    core = tensor_index % 2

    def by_core(weight, axis):
        split = weight.reshape(weight.shape[:axis] + (half_count, 2) + weight.shape[axis + 1 :])
        return (
            lax.dynamic_index_in_dim(split, core, axis + 1, keepdims=False),
            lax.dynamic_index_in_dim(split, 1 - core, axis + 1, keepdims=False),
        )

    head_start = tensor_index * H // tensor_count * head_dim
    own_start = tensor_index * col_width
    inner_start = own_start - head_start
    head_proj = lax.dynamic_slice_in_dim(proj_weight, head_start, head_dim, 2).reshape(
        tensor_count, col_width, 4 * head_dim
    )
    own_proj = lax.dynamic_slice_in_dim(proj_weight, own_start, col_width, 2).reshape(
        tensor_count, col_width, 4 * col_width
    )
    head_out = lax.dynamic_slice_in_dim(out_weight, head_start, head_dim, 0).reshape(
        head_dim, tensor_count, col_width
    )
    head_gain = lax.dynamic_slice_in_dim(norm_gain, head_start, head_dim, 0)

    proj_mine, proj_other = by_core(head_proj, 0)
    out_mine, out_other = by_core(head_out, 1)
    own_out = lax.dynamic_slice_in_dim(out_weight, own_start, col_width, 0).reshape(
        col_width, tensor_count, col_width
    )
    weight_pack = (proj_mine, proj_other, out_mine, out_other, own_proj, own_out, head_gain)
    recv_both, weight_pack = lax.optimization_barrier((recv_both, weight_pack))
    proj_mine, proj_other, out_mine, out_other, own_proj, own_out, head_gain = weight_pack

    recv_len = jnp.sum(jnp.where(owners == dp_index, lengths, 0), axis=1)
    recv_start = exclusive_sum(recv_len)
    compact_ids = jnp.arange(owned_rows, dtype=jnp.int32)
    compact_slot = (
        jnp.sum((compact_ids[:, None] >= recv_start[None, :]).astype(jnp.int32), axis=1) - 1
    )
    slot_pick = compact_slot[:, None] == peer_ids[None, :]
    compact_start = jnp.sum(jnp.where(slot_pick, recv_start[None, :], 0), axis=1)
    gather_ids = compact_slot * MAXLEN + compact_ids - compact_start
    own_both = pick_rows(gather_ids, recv_both.reshape(dp_count * MAXLEN, 2 * col_width))
    own_tokens = own_both[:, :col_width]
    own_cotan = own_both[:, col_width:]

    same_core = [[2 * z + c for z in range(half_count)] for c in range(2)]
    sibling = [(t, t ^ 1) for t in range(tensor_count)]
    mine = lax.all_gather(own_both, "tensor", axis=0, tiled=False, axis_index_groups=same_core)
    other = lax.ppermute(mine, "tensor", sibling)
    mine_tok, mine_cot = mine[..., :col_width], mine[..., col_width:]
    other_tok, other_cot = other[..., :col_width], other[..., col_width:]

    def reduce_blocks(part):
        keep, send = by_core(part, 0)
        pair_sum = (keep.astype(f32) + lax.ppermute(send, "tensor", sibling).astype(f32)).astype(bf16)
        pieces = lax.all_to_all(pair_sum, "tensor", 0, 0, tiled=True, axis_index_groups=same_core)
        return jnp.sum(pieces.astype(f32), axis=0)

    projected = jnp.einsum(
        "trc,tcn->rn", mine_tok, proj_mine, preferred_element_type=f32
    ) + jnp.einsum("trc,tcn->rn", other_tok, proj_other, preferred_element_type=f32)
    down_grad = jnp.einsum(
        "trc,dtc->rd", mine_cot, out_mine, preferred_element_type=f32
    ) + jnp.einsum("trc,dtc->rd", other_cot, out_other, preferred_element_type=f32)
    proj4 = projected.reshape(owned_rows, 4, head_dim)
    activated = jax.nn.silu(proj4).astype(bf16)
    gating = activated[:, 0]
    values = activated[:, 1]
    queries = activated[:, 2]
    keys_head = activated[:, 3]
    scores = jnp.einsum("md,nd->mn", queries, keys_head, preferred_element_type=f32)
    allowed = (compact_slot[:, None] == compact_slot[None, :]) & (
        compact_ids[:, None] >= compact_ids[None, :]
    )
    weights = jnp.where(allowed, jax.nn.silu(scores * score_scale) / MAXLEN, 0.0).astype(bf16)
    attended = jnp.einsum("mn,nd->md", weights, values, preferred_element_type=f32)
    inv_rms = lax.rsqrt(jnp.mean(attended * attended, axis=-1, keepdims=True) + norm_eps)
    normed = attended * inv_rms * head_gain
    gated = (normed * gating).astype(bf16)
    own_gated = lax.dynamic_slice_in_dim(gated, inner_start, col_width, 1)
    out_part = jnp.einsum("rc,ctk->trk", own_gated, own_out, preferred_element_type=f32)

    d_normed = down_grad * gating
    d_gating = down_grad * normed
    scaled = head_gain * d_normed
    d_attended = (
        inv_rms * scaled
        - attended * inv_rms**3 * jnp.mean(attended * scaled, axis=-1, keepdims=True)
    ).astype(bf16)
    d_weights = jnp.einsum("md,nd->mn", d_attended, values, preferred_element_type=f32)
    d_values = jnp.einsum("mn,md->nd", weights, d_attended, preferred_element_type=f32)
    d_scores = jnp.where(
        allowed, d_weights * silu_slope(scores * score_scale) * (score_scale / MAXLEN), 0.0
    ).astype(bf16)
    d_queries = jnp.einsum("mn,nd->md", d_scores, keys_head, preferred_element_type=f32)
    d_keys = jnp.einsum("mn,md->nd", d_scores, queries, preferred_element_type=f32)
    d_activated = jnp.stack([d_gating, d_values, d_queries, d_keys], axis=1)
    d_projected = (d_activated * silu_slope(proj4)).astype(bf16)
    own_grad = lax.dynamic_slice_in_dim(d_projected, inner_start, col_width, 2).reshape(
        owned_rows, 4 * col_width
    )
    grad_part = jnp.einsum("rn,tkn->trk", own_grad, own_proj, preferred_element_type=f32)
    both_sum = reduce_blocks(jnp.concatenate([out_part, grad_part], axis=2).astype(bf16))
    out_sum = both_sum[:, :col_width]
    grad_sum = both_sum[:, col_width:]
    mixed_out = (own_tokens.astype(f32) + out_sum).astype(bf16)
    token_rows = (own_cotan.astype(f32) + grad_sum).astype(bf16)

    def by_rows(term_mine, term_other):
        pair = jnp.stack([term_mine, term_other], axis=1)
        pair = jnp.where(core == 0, pair, pair[:, ::-1])
        return pair.reshape((D,) + term_mine.shape[2:])

    proj_term = by_rows(
        jnp.einsum("trc,rn->tcn", mine_tok, own_grad, preferred_element_type=f32),
        jnp.einsum("trc,rn->tcn", other_tok, own_grad, preferred_element_type=f32),
    )
    out_term = by_rows(
        jnp.einsum("trc,rd->tcd", mine_cot, own_gated, preferred_element_type=f32),
        jnp.einsum("trc,rd->tcd", other_cot, own_gated, preferred_element_type=f32),
    )
    terms = jnp.concatenate([proj_term, out_term], axis=1).astype(bf16)
    bit_count = dp_count.bit_length() - 1
    term_sum = terms.reshape((2,) * bit_count + (D // dp_count,) + terms.shape[1:]).astype(f32)
    for level in range(bit_count - 1, -1, -1):
        my_bit = (dp_index >> level) & 1
        keep = lax.dynamic_index_in_dim(term_sum, my_bit, 0, keepdims=False)
        send = lax.dynamic_index_in_dim(term_sum, 1 - my_bit, 0, keepdims=False)
        partners = [(d, d ^ (1 << level)) for d in range(dp_count)]
        term_sum = keep + lax.ppermute(send.astype(bf16), "dp", partners).astype(f32)
    proj_grad = term_sum[:, : 4 * col_width].reshape(-1, 4, col_width)
    out_grad = term_sum[:, 4 * col_width :].T

    back_src = jnp.minimum(recv_start[:, None] + places[None, :], owned_rows - 1)
    back_send = pick_rows(back_src.reshape(-1), token_rows).reshape(dp_count, MAXLEN, col_width)
    back_grads = lax.all_to_all(back_send, "dp", split_axis=0, concat_axis=0, tiled=True)
    back_grads = back_grads.reshape(dp_count * MAXLEN, col_width)
    load_ids = jnp.arange(load_rows, dtype=jnp.int32)
    seq_of = jnp.sum((load_ids[:, None] >= my_starts[None, :]).astype(jnp.int32), axis=1) - 1
    seq_pick = seq_of[:, None] == seq_ids[None, :]
    owner_of = jnp.sum(jnp.where(seq_pick, my_owners[None, :], 0), axis=1)
    start_of = jnp.sum(jnp.where(seq_pick, my_starts[None, :], 0), axis=1)
    back_ids = owner_of * MAXLEN + jnp.minimum(load_ids - start_of, MAXLEN - 1)
    row_used = load_ids < jnp.sum(my_lengths)
    token_grad = pick_rows(jnp.where(row_used, back_ids, -1), back_grads)
    return (mixed_out, token_grad, proj_grad, out_grad)


def solution(mesh):
    in_specs = (P("dp", "tensor"), P("dp", "tensor"), P(), P(), P(), P(), P())
    out_specs = (P("dp", "tensor"), P("dp", "tensor"), P("dp", None, "tensor"), P("tensor", "dp"))
    return jax.shard_map(local, mesh=mesh, in_specs=in_specs, out_specs=out_specs, check_vma=False)
```

```python
import math

import jax
import jax.numpy as jnp
from jax import lax
from jax.sharding import PartitionSpec as P

D = 1024
H = 8
MAXLEN = 192


norm_eps = 1e-05


def silu_slope(argument):
    sigmoid_val = jax.nn.sigmoid(argument)
    return sigmoid_val * (1.0 + argument * (1.0 - sigmoid_val))


def exclusive_sum(counts):
    return jnp.cumsum(counts) - counts


def local(tokens, cotangent, lengths, owners, proj_weight, norm_gain, out_weight):
    f32 = jnp.float32
    bf16 = jnp.bfloat16
    dp_count = lax.axis_size("dp")
    tensor_count = lax.axis_size("tensor")
    dp_index = lax.axis_index("dp")
    tensor_index = lax.axis_index("tensor")
    col_width = tokens.shape[1]
    load_rows = tokens.shape[0]
    head_dim = D // H
    score_scale = 1.0 / math.sqrt(head_dim)
    owned_rows = dp_count * (9 * MAXLEN // 16)
    places = jnp.arange(MAXLEN, dtype=jnp.int32)
    peer_ids = jnp.arange(dp_count, dtype=jnp.int32)
    seq_ids = jnp.arange(lengths.shape[1], dtype=jnp.int32)

    my_lengths = lengths[dp_index]
    my_owners = owners[dp_index]
    my_starts = exclusive_sum(my_lengths)
    sent_to = my_owners[None, :] == peer_ids[:, None]
    send_start = jnp.sum(jnp.where(sent_to, my_starts[None, :], 0), axis=1)
    send_ids = jnp.minimum(send_start[:, None] + places[None, :], load_rows - 1)
    def pick_rows(row_ids, source):
        one_hot = (row_ids[:, None] == jnp.arange(source.shape[0], dtype=jnp.int32)[None, :]).astype(bf16)
        return jnp.dot(one_hot, source, preferred_element_type=f32).astype(bf16)

    flat_send = send_ids.reshape(-1)
    send_both = jnp.concatenate(
        [pick_rows(flat_send, tokens), pick_rows(flat_send, cotangent)], axis=1
    ).reshape(dp_count, MAXLEN, 2 * col_width)
    recv_both = lax.all_to_all(send_both, "dp", split_axis=0, concat_axis=0, tiled=True)

    half_count = tensor_count // 2
    core = tensor_index % 2

    def by_core(weight, axis):
        split = weight.reshape(weight.shape[:axis] + (half_count, 2) + weight.shape[axis + 1 :])
        return (
            lax.dynamic_index_in_dim(split, core, axis + 1, keepdims=False),
            lax.dynamic_index_in_dim(split, 1 - core, axis + 1, keepdims=False),
        )

    head_start = tensor_index * H // tensor_count * head_dim
    own_start = tensor_index * col_width
    inner_start = own_start - head_start
    head_proj = lax.dynamic_slice_in_dim(proj_weight, head_start, head_dim, 2).reshape(
        tensor_count, col_width, 4 * head_dim
    )
    sib_start = (tensor_index ^ 1) * col_width
    dest_proj = by_core(proj_weight.reshape(tensor_count, col_width, 4, D), 0)[0]
    pair_proj = jnp.stack(
        [
            lax.dynamic_slice_in_dim(dest_proj, start, col_width, 3).reshape(
                half_count, col_width, 4 * col_width
            )
            for start in (own_start, sib_start)
        ]
    )
    head_out = lax.dynamic_slice_in_dim(out_weight, head_start, head_dim, 0).reshape(
        head_dim, tensor_count, col_width
    )
    head_gain = lax.dynamic_slice_in_dim(norm_gain, head_start, head_dim, 0)

    proj_mine, proj_other = by_core(head_proj, 0)
    out_mine, out_other = by_core(head_out, 1)
    dest_out = by_core(out_weight.reshape(D, tensor_count, col_width), 1)[0]
    pair_out = jnp.stack(
        [lax.dynamic_slice_in_dim(dest_out, start, col_width, 0) for start in (own_start, sib_start)]
    )
    weight_pack = (proj_mine, proj_other, out_mine, out_other, pair_proj, pair_out, head_gain)
    recv_both, weight_pack = lax.optimization_barrier((recv_both, weight_pack))
    proj_mine, proj_other, out_mine, out_other, pair_proj, pair_out, head_gain = weight_pack

    recv_len = jnp.sum(jnp.where(owners == dp_index, lengths, 0), axis=1)
    recv_start = exclusive_sum(recv_len)
    compact_ids = jnp.arange(owned_rows, dtype=jnp.int32)
    compact_slot = (
        jnp.sum((compact_ids[:, None] >= recv_start[None, :]).astype(jnp.int32), axis=1) - 1
    )
    slot_pick = compact_slot[:, None] == peer_ids[None, :]
    compact_start = jnp.sum(jnp.where(slot_pick, recv_start[None, :], 0), axis=1)
    gather_ids = compact_slot * MAXLEN + compact_ids - compact_start
    own_both = pick_rows(gather_ids, recv_both.reshape(dp_count * MAXLEN, 2 * col_width))
    own_tokens = own_both[:, :col_width]
    own_cotan = own_both[:, col_width:]

    same_core = [[2 * z + c for z in range(half_count)] for c in range(2)]
    sibling = [(t, t ^ 1) for t in range(tensor_count)]
    mine = lax.all_gather(own_both, "tensor", axis=0, tiled=False, axis_index_groups=same_core)
    other = lax.ppermute(mine, "tensor", sibling)
    mine_tok, mine_cot = mine[..., :col_width], mine[..., col_width:]
    other_tok, other_cot = other[..., :col_width], other[..., col_width:]

    def reduce_blocks(part):
        pieces = lax.all_to_all(part, "tensor", 0, 0, tiled=True, axis_index_groups=same_core)
        return jnp.sum(pieces.astype(f32), axis=0)

    projected = jnp.einsum(
        "trc,tcn->rn", mine_tok, proj_mine, preferred_element_type=f32
    ) + jnp.einsum("trc,tcn->rn", other_tok, proj_other, preferred_element_type=f32)
    down_grad = jnp.einsum(
        "trc,dtc->rd", mine_cot, out_mine, preferred_element_type=f32
    ) + jnp.einsum("trc,dtc->rd", other_cot, out_other, preferred_element_type=f32)
    proj4 = projected.reshape(owned_rows, 4, head_dim)
    activated = jax.nn.silu(proj4).astype(bf16)
    gating = activated[:, 0]
    values = activated[:, 1]
    queries = activated[:, 2]
    keys_head = activated[:, 3]
    scores = jnp.einsum("md,nd->mn", queries, keys_head, preferred_element_type=f32)
    allowed = (compact_slot[:, None] == compact_slot[None, :]) & (
        compact_ids[:, None] >= compact_ids[None, :]
    )
    weights = jnp.where(allowed, jax.nn.silu(scores * score_scale) / MAXLEN, 0.0).astype(bf16)
    attended = jnp.einsum("mn,nd->md", weights, values, preferred_element_type=f32)
    inv_rms = lax.rsqrt(jnp.mean(attended * attended, axis=-1, keepdims=True) + norm_eps)
    normed = attended * inv_rms * head_gain
    gated = (normed * gating).astype(bf16)
    own_gated = lax.dynamic_slice_in_dim(gated, inner_start, col_width, 1)
    pair_gated = jnp.stack([own_gated, lax.ppermute(own_gated, "tensor", sibling)])
    out_part = jnp.einsum("src,sczk->zrk", pair_gated, pair_out, preferred_element_type=f32)

    d_normed = down_grad * gating
    d_gating = down_grad * normed
    scaled = head_gain * d_normed
    d_attended = (
        inv_rms * scaled
        - attended * inv_rms**3 * jnp.mean(attended * scaled, axis=-1, keepdims=True)
    ).astype(bf16)
    d_weights = jnp.einsum("md,nd->mn", d_attended, values, preferred_element_type=f32)
    d_values = jnp.einsum("mn,md->nd", weights, d_attended, preferred_element_type=f32)
    d_scores = jnp.where(
        allowed, d_weights * silu_slope(scores * score_scale) * (score_scale / MAXLEN), 0.0
    ).astype(bf16)
    d_queries = jnp.einsum("mn,nd->md", d_scores, keys_head, preferred_element_type=f32)
    d_keys = jnp.einsum("mn,md->nd", d_scores, queries, preferred_element_type=f32)
    d_activated = jnp.stack([d_gating, d_values, d_queries, d_keys], axis=1)
    d_projected = (d_activated * silu_slope(proj4)).astype(bf16)
    own_grad = lax.dynamic_slice_in_dim(d_projected, inner_start, col_width, 2).reshape(
        owned_rows, 4 * col_width
    )
    pair_grad = jnp.stack([own_grad, lax.ppermute(own_grad, "tensor", sibling)])
    grad_part = jnp.einsum("srn,szkn->zrk", pair_grad, pair_proj, preferred_element_type=f32)
    both_sum = reduce_blocks(jnp.concatenate([out_part, grad_part], axis=2).astype(bf16))
    out_sum = both_sum[:, :col_width]
    grad_sum = both_sum[:, col_width:]
    mixed_out = (own_tokens.astype(f32) + out_sum).astype(bf16)
    token_rows = (own_cotan.astype(f32) + grad_sum).astype(bf16)

    def by_rows(term_mine, term_other):
        pair = jnp.stack([term_mine, term_other], axis=1)
        pair = jnp.where(core == 0, pair, pair[:, ::-1])
        return pair.reshape((D,) + term_mine.shape[2:])

    proj_term = by_rows(
        jnp.einsum("trc,rn->tcn", mine_tok, own_grad, preferred_element_type=f32),
        jnp.einsum("trc,rn->tcn", other_tok, own_grad, preferred_element_type=f32),
    )
    out_term = by_rows(
        jnp.einsum("trc,rd->tcd", mine_cot, own_gated, preferred_element_type=f32),
        jnp.einsum("trc,rd->tcd", other_cot, own_gated, preferred_element_type=f32),
    )
    terms = jnp.concatenate([proj_term, out_term], axis=1).astype(bf16)
    bit_count = dp_count.bit_length() - 1
    term_sum = terms.reshape((2,) * bit_count + (D // dp_count,) + terms.shape[1:]).astype(f32)
    for level in range(bit_count - 1, -1, -1):
        my_bit = (dp_index >> level) & 1
        keep = lax.dynamic_index_in_dim(term_sum, my_bit, 0, keepdims=False)
        send = lax.dynamic_index_in_dim(term_sum, 1 - my_bit, 0, keepdims=False)
        partners = [(d, d ^ (1 << level)) for d in range(dp_count)]
        term_sum = keep + lax.ppermute(send.astype(bf16), "dp", partners).astype(f32)
    proj_grad = term_sum[:, : 4 * col_width].reshape(-1, 4, col_width)
    out_grad = term_sum[:, 4 * col_width :].T

    back_src = jnp.minimum(recv_start[:, None] + places[None, :], owned_rows - 1)
    back_send = pick_rows(back_src.reshape(-1), token_rows).reshape(dp_count, MAXLEN, col_width)
    back_grads = lax.all_to_all(back_send, "dp", split_axis=0, concat_axis=0, tiled=True)
    back_grads = back_grads.reshape(dp_count * MAXLEN, col_width)
    load_ids = jnp.arange(load_rows, dtype=jnp.int32)
    seq_of = jnp.sum((load_ids[:, None] >= my_starts[None, :]).astype(jnp.int32), axis=1) - 1
    seq_pick = seq_of[:, None] == seq_ids[None, :]
    owner_of = jnp.sum(jnp.where(seq_pick, my_owners[None, :], 0), axis=1)
    start_of = jnp.sum(jnp.where(seq_pick, my_starts[None, :], 0), axis=1)
    back_ids = owner_of * MAXLEN + jnp.minimum(load_ids - start_of, MAXLEN - 1)
    row_used = load_ids < jnp.sum(my_lengths)
    token_grad = pick_rows(jnp.where(row_used, back_ids, -1), back_grads)
    return (mixed_out, token_grad, proj_grad, out_grad)


def solution(mesh):
    in_specs = (P("dp", "tensor"), P("dp", "tensor"), P(), P(), P(), P(), P())
    out_specs = (P("dp", "tensor"), P("dp", "tensor"), P("dp", None, "tensor"), P("tensor", "dp"))
    return jax.shard_map(local, mesh=mesh, in_specs=in_specs, out_specs=out_specs, check_vma=False)
```

```python
import math

import jax
import jax.numpy as jnp
from jax import lax
from jax.sharding import PartitionSpec as P

D = 1024
H = 8
MAXLEN = 192


norm_eps = 1e-05


def silu_slope(argument):
    sigmoid_val = jax.nn.sigmoid(argument)
    return sigmoid_val * (1.0 + argument * (1.0 - sigmoid_val))


def exclusive_sum(counts):
    return jnp.cumsum(counts) - counts


def local(tokens, cotangent, lengths, owners, proj_weight, norm_gain, out_weight):
    f32 = jnp.float32
    bf16 = jnp.bfloat16
    dp_count = lax.axis_size("dp")
    tensor_count = lax.axis_size("tensor")
    dp_index = lax.axis_index("dp")
    tensor_index = lax.axis_index("tensor")
    col_width = tokens.shape[1]
    load_rows = tokens.shape[0]
    head_dim = D // H
    score_scale = 1.0 / math.sqrt(head_dim)
    owned_rows = dp_count * (9 * MAXLEN // 16)
    places = jnp.arange(MAXLEN, dtype=jnp.int32)
    peer_ids = jnp.arange(dp_count, dtype=jnp.int32)
    seq_ids = jnp.arange(lengths.shape[1], dtype=jnp.int32)

    my_lengths = lengths[dp_index]
    my_owners = owners[dp_index]
    my_starts = exclusive_sum(my_lengths)
    sent_to = my_owners[None, :] == peer_ids[:, None]
    send_start = jnp.sum(jnp.where(sent_to, my_starts[None, :], 0), axis=1)
    send_ids = jnp.minimum(send_start[:, None] + places[None, :], load_rows - 1)
    def exchange(blocks):
        pieces = [lax.dynamic_index_in_dim(blocks, dp_index, 0, keepdims=False)]
        for k in range(1, dp_count):
            outgoing = lax.dynamic_index_in_dim(blocks, dp_index ^ k, 0, keepdims=False)
            pieces.append(lax.ppermute(outgoing, "dp", [(d, d ^ k) for d in range(dp_count)]))
        return jnp.stack(pieces)

    def pick_rows(row_ids, source):
        one_hot = (row_ids[:, None] == jnp.arange(source.shape[0], dtype=jnp.int32)[None, :]).astype(bf16)
        return jnp.dot(one_hot, source, preferred_element_type=f32).astype(bf16)

    flat_send = send_ids.reshape(-1)
    send_both = jnp.concatenate(
        [pick_rows(flat_send, tokens), pick_rows(flat_send, cotangent)], axis=1
    ).reshape(dp_count, MAXLEN, 2 * col_width)
    recv_both = exchange(send_both)

    half_count = tensor_count // 2
    core = tensor_index % 2

    def by_core(weight, axis):
        split = weight.reshape(weight.shape[:axis] + (half_count, 2) + weight.shape[axis + 1 :])
        return (
            lax.dynamic_index_in_dim(split, core, axis + 1, keepdims=False),
            lax.dynamic_index_in_dim(split, 1 - core, axis + 1, keepdims=False),
        )

    head_start = tensor_index * H // tensor_count * head_dim
    own_start = tensor_index * col_width
    inner_start = own_start - head_start
    head_proj = lax.dynamic_slice_in_dim(proj_weight, head_start, head_dim, 2).reshape(
        tensor_count, col_width, 4 * head_dim
    )
    own_proj = lax.dynamic_slice_in_dim(proj_weight, own_start, col_width, 2).reshape(
        tensor_count, col_width, 4 * col_width
    )
    head_out = lax.dynamic_slice_in_dim(out_weight, head_start, head_dim, 0).reshape(
        head_dim, tensor_count, col_width
    )
    head_gain = lax.dynamic_slice_in_dim(norm_gain, head_start, head_dim, 0)

    proj_mine, proj_other = by_core(head_proj, 0)
    out_mine, out_other = by_core(head_out, 1)
    own_out = lax.dynamic_slice_in_dim(out_weight, own_start, col_width, 0).reshape(
        col_width, tensor_count, col_width
    )
    weight_pack = (proj_mine, proj_other, out_mine, out_other, own_proj, own_out, head_gain)
    recv_both, weight_pack = lax.optimization_barrier((recv_both, weight_pack))
    proj_mine, proj_other, out_mine, out_other, own_proj, own_out, head_gain = weight_pack

    recv_len = jnp.sum(jnp.where(owners == dp_index, lengths, 0), axis=1)
    recv_start = exclusive_sum(recv_len)
    compact_ids = jnp.arange(owned_rows, dtype=jnp.int32)
    compact_slot = (
        jnp.sum((compact_ids[:, None] >= recv_start[None, :]).astype(jnp.int32), axis=1) - 1
    )
    slot_pick = compact_slot[:, None] == peer_ids[None, :]
    compact_start = jnp.sum(jnp.where(slot_pick, recv_start[None, :], 0), axis=1)
    gather_ids = (compact_slot ^ dp_index) * MAXLEN + compact_ids - compact_start
    own_both = pick_rows(gather_ids, recv_both.reshape(dp_count * MAXLEN, 2 * col_width))
    own_tokens = own_both[:, :col_width]
    own_cotan = own_both[:, col_width:]

    same_core = [[2 * z + c for z in range(half_count)] for c in range(2)]
    sibling = [(t, t ^ 1) for t in range(tensor_count)]
    mine = lax.all_gather(own_both, "tensor", axis=0, tiled=False, axis_index_groups=same_core)
    other = lax.ppermute(mine, "tensor", sibling)
    mine_tok, mine_cot = mine[..., :col_width], mine[..., col_width:]
    other_tok, other_cot = other[..., :col_width], other[..., col_width:]

    def reduce_blocks(part):
        keep, send = by_core(part, 0)
        pair_sum = (keep.astype(f32) + lax.ppermute(send, "tensor", sibling).astype(f32)).astype(bf16)
        pieces = lax.all_to_all(pair_sum, "tensor", 0, 0, tiled=True, axis_index_groups=same_core)
        return jnp.sum(pieces.astype(f32), axis=0)

    projected = jnp.einsum(
        "trc,tcn->rn", mine_tok, proj_mine, preferred_element_type=f32
    ) + jnp.einsum("trc,tcn->rn", other_tok, proj_other, preferred_element_type=f32)
    down_grad = jnp.einsum(
        "trc,dtc->rd", mine_cot, out_mine, preferred_element_type=f32
    ) + jnp.einsum("trc,dtc->rd", other_cot, out_other, preferred_element_type=f32)
    proj4 = projected.reshape(owned_rows, 4, head_dim)
    activated = jax.nn.silu(proj4).astype(bf16)
    gating = activated[:, 0]
    values = activated[:, 1]
    queries = activated[:, 2]
    keys_head = activated[:, 3]
    scores = jnp.einsum("md,nd->mn", queries, keys_head, preferred_element_type=f32)
    allowed = (compact_slot[:, None] == compact_slot[None, :]) & (
        compact_ids[:, None] >= compact_ids[None, :]
    )
    weights = jnp.where(allowed, jax.nn.silu(scores * score_scale) / MAXLEN, 0.0).astype(bf16)
    attended = jnp.einsum("mn,nd->md", weights, values, preferred_element_type=f32)
    inv_rms = lax.rsqrt(jnp.mean(attended * attended, axis=-1, keepdims=True) + norm_eps)
    normed = attended * inv_rms * head_gain
    gated = (normed * gating).astype(bf16)
    own_gated = lax.dynamic_slice_in_dim(gated, inner_start, col_width, 1)
    out_part = jnp.einsum("rc,ctk->trk", own_gated, own_out, preferred_element_type=f32)

    d_normed = down_grad * gating
    d_gating = down_grad * normed
    scaled = head_gain * d_normed
    d_attended = (
        inv_rms * scaled
        - attended * inv_rms**3 * jnp.mean(attended * scaled, axis=-1, keepdims=True)
    ).astype(bf16)
    d_weights = jnp.einsum("md,nd->mn", d_attended, values, preferred_element_type=f32)
    d_values = jnp.einsum("mn,md->nd", weights, d_attended, preferred_element_type=f32)
    d_scores = jnp.where(
        allowed, d_weights * silu_slope(scores * score_scale) * (score_scale / MAXLEN), 0.0
    ).astype(bf16)
    d_queries = jnp.einsum("mn,nd->md", d_scores, keys_head, preferred_element_type=f32)
    d_keys = jnp.einsum("mn,md->nd", d_scores, queries, preferred_element_type=f32)
    d_activated = jnp.stack([d_gating, d_values, d_queries, d_keys], axis=1)
    d_projected = (d_activated * silu_slope(proj4)).astype(bf16)
    own_grad = lax.dynamic_slice_in_dim(d_projected, inner_start, col_width, 2).reshape(
        owned_rows, 4 * col_width
    )
    grad_part = jnp.einsum("rn,tkn->trk", own_grad, own_proj, preferred_element_type=f32)
    both_sum = reduce_blocks(jnp.concatenate([out_part, grad_part], axis=2).astype(bf16))
    out_sum = both_sum[:, :col_width]
    grad_sum = both_sum[:, col_width:]
    mixed_out = (own_tokens.astype(f32) + out_sum).astype(bf16)
    token_rows = (own_cotan.astype(f32) + grad_sum).astype(bf16)

    def by_rows(term_mine, term_other):
        pair = jnp.stack([term_mine, term_other], axis=1)
        pair = jnp.where(core == 0, pair, pair[:, ::-1])
        return pair.reshape((D,) + term_mine.shape[2:])

    proj_term = by_rows(
        jnp.einsum("trc,rn->tcn", mine_tok, own_grad, preferred_element_type=f32),
        jnp.einsum("trc,rn->tcn", other_tok, own_grad, preferred_element_type=f32),
    )
    out_term = by_rows(
        jnp.einsum("trc,rd->tcd", mine_cot, own_gated, preferred_element_type=f32),
        jnp.einsum("trc,rd->tcd", other_cot, own_gated, preferred_element_type=f32),
    )
    terms = jnp.concatenate([proj_term, out_term], axis=1).astype(bf16)
    bit_count = dp_count.bit_length() - 1
    term_sum = terms.reshape((2,) * bit_count + (D // dp_count,) + terms.shape[1:]).astype(f32)
    for level in range(bit_count - 1, -1, -1):
        my_bit = (dp_index >> level) & 1
        keep = lax.dynamic_index_in_dim(term_sum, my_bit, 0, keepdims=False)
        send = lax.dynamic_index_in_dim(term_sum, 1 - my_bit, 0, keepdims=False)
        partners = [(d, d ^ (1 << level)) for d in range(dp_count)]
        term_sum = keep + lax.ppermute(send.astype(bf16), "dp", partners).astype(f32)
    proj_grad = term_sum[:, : 4 * col_width].reshape(-1, 4, col_width)
    out_grad = term_sum[:, 4 * col_width :].T

    back_src = jnp.minimum(recv_start[:, None] + places[None, :], owned_rows - 1)
    back_send = pick_rows(back_src.reshape(-1), token_rows).reshape(dp_count, MAXLEN, col_width)
    back_grads = exchange(back_send)
    back_grads = back_grads.reshape(dp_count * MAXLEN, col_width)
    load_ids = jnp.arange(load_rows, dtype=jnp.int32)
    seq_of = jnp.sum((load_ids[:, None] >= my_starts[None, :]).astype(jnp.int32), axis=1) - 1
    seq_pick = seq_of[:, None] == seq_ids[None, :]
    owner_of = jnp.sum(jnp.where(seq_pick, my_owners[None, :], 0), axis=1)
    start_of = jnp.sum(jnp.where(seq_pick, my_starts[None, :], 0), axis=1)
    back_ids = (owner_of ^ dp_index) * MAXLEN + jnp.minimum(load_ids - start_of, MAXLEN - 1)
    row_used = load_ids < jnp.sum(my_lengths)
    token_grad = pick_rows(jnp.where(row_used, back_ids, -1), back_grads)
    return (mixed_out, token_grad, proj_grad, out_grad)


def solution(mesh):
    in_specs = (P("dp", "tensor"), P("dp", "tensor"), P(), P(), P(), P(), P())
    out_specs = (P("dp", "tensor"), P("dp", "tensor"), P("dp", None, "tensor"), P("tensor", "dp"))
    return jax.shard_map(local, mesh=mesh, in_specs=in_specs, out_specs=out_specs, check_vma=False)
```

```python
import math

import jax
import jax.numpy as jnp
from jax import lax
from jax.sharding import PartitionSpec as P

D = 1024
H = 8
MAXLEN = 192


norm_eps = 1e-05


def silu_slope(argument):
    sigmoid_val = jax.nn.sigmoid(argument)
    return sigmoid_val * (1.0 + argument * (1.0 - sigmoid_val))


def exclusive_sum(counts):
    return jnp.cumsum(counts) - counts


def local(tokens, cotangent, lengths, owners, proj_weight, norm_gain, out_weight):
    f32 = jnp.float32
    bf16 = jnp.bfloat16
    dp_count = lax.axis_size("dp")
    tensor_count = lax.axis_size("tensor")
    dp_index = lax.axis_index("dp")
    tensor_index = lax.axis_index("tensor")
    col_width = tokens.shape[1]
    load_rows = tokens.shape[0]
    head_dim = D // H
    score_scale = 1.0 / math.sqrt(head_dim)
    owned_rows = dp_count * (9 * MAXLEN // 16)
    places = jnp.arange(MAXLEN, dtype=jnp.int32)
    peer_ids = jnp.arange(dp_count, dtype=jnp.int32)
    seq_ids = jnp.arange(lengths.shape[1], dtype=jnp.int32)

    my_lengths = lengths[dp_index]
    my_owners = owners[dp_index]
    my_starts = exclusive_sum(my_lengths)
    sent_to = my_owners[None, :] == peer_ids[:, None]
    send_start = jnp.sum(jnp.where(sent_to, my_starts[None, :], 0), axis=1)
    send_ids = jnp.minimum(send_start[:, None] + places[None, :], load_rows - 1)
    def exchange(blocks):
        pieces = [lax.dynamic_index_in_dim(blocks, dp_index, 0, keepdims=False)]
        for k in range(1, dp_count):
            outgoing = lax.dynamic_index_in_dim(blocks, dp_index ^ k, 0, keepdims=False)
            pieces.append(lax.ppermute(outgoing, "dp", [(d, d ^ k) for d in range(dp_count)]))
        return jnp.stack(pieces)

    def pick_rows(row_ids, source):
        one_hot = (row_ids[:, None] == jnp.arange(source.shape[0], dtype=jnp.int32)[None, :]).astype(bf16)
        return jnp.dot(one_hot, source, preferred_element_type=f32).astype(bf16)

    flat_send = send_ids.reshape(-1)
    send_both = jnp.concatenate(
        [pick_rows(flat_send, tokens), pick_rows(flat_send, cotangent)], axis=1
    ).reshape(dp_count, MAXLEN, 2 * col_width)
    recv_both = exchange(send_both)

    half_count = tensor_count // 2
    core = tensor_index % 2

    def by_core(weight, axis):
        split = weight.reshape(weight.shape[:axis] + (half_count, 2) + weight.shape[axis + 1 :])
        return (
            lax.dynamic_index_in_dim(split, core, axis + 1, keepdims=False),
            lax.dynamic_index_in_dim(split, 1 - core, axis + 1, keepdims=False),
        )

    head_start = tensor_index * H // tensor_count * head_dim
    own_start = tensor_index * col_width
    inner_start = own_start - head_start
    head_proj = lax.dynamic_slice_in_dim(proj_weight, head_start, head_dim, 2).reshape(
        tensor_count, col_width, 4 * head_dim
    )
    own_proj = lax.dynamic_slice_in_dim(proj_weight, own_start, col_width, 2).reshape(
        tensor_count, col_width, 4 * col_width
    )
    head_out = lax.dynamic_slice_in_dim(out_weight, head_start, head_dim, 0).reshape(
        head_dim, tensor_count, col_width
    )
    head_gain = lax.dynamic_slice_in_dim(norm_gain, head_start, head_dim, 0)

    proj_mine, proj_other = by_core(head_proj, 0)
    out_mine, out_other = by_core(head_out, 1)
    own_out = lax.dynamic_slice_in_dim(out_weight, own_start, col_width, 0).reshape(
        col_width, tensor_count, col_width
    )
    weight_pack = (proj_mine, proj_other, out_mine, out_other, own_proj, own_out, head_gain)
    recv_both, weight_pack = lax.optimization_barrier((recv_both, weight_pack))
    proj_mine, proj_other, out_mine, out_other, own_proj, own_out, head_gain = weight_pack

    recv_len = jnp.sum(jnp.where(owners == dp_index, lengths, 0), axis=1)
    recv_start = exclusive_sum(recv_len)
    compact_ids = jnp.arange(owned_rows, dtype=jnp.int32)
    compact_slot = (
        jnp.sum((compact_ids[:, None] >= recv_start[None, :]).astype(jnp.int32), axis=1) - 1
    )
    slot_pick = compact_slot[:, None] == peer_ids[None, :]
    compact_start = jnp.sum(jnp.where(slot_pick, recv_start[None, :], 0), axis=1)
    gather_ids = (compact_slot ^ dp_index) * MAXLEN + compact_ids - compact_start
    own_both = pick_rows(gather_ids, recv_both.reshape(dp_count * MAXLEN, 2 * col_width))
    own_tokens = own_both[:, :col_width]
    own_cotan = own_both[:, col_width:]

    same_core = [[2 * z + c for z in range(half_count)] for c in range(2)]
    sibling = [(t, t ^ 1) for t in range(tensor_count)]
    mine = lax.all_gather(own_both, "tensor", axis=0, tiled=False, axis_index_groups=same_core)
    other = lax.ppermute(mine, "tensor", sibling)
    mine_tok, mine_cot = mine[..., :col_width], mine[..., col_width:]
    other_tok, other_cot = other[..., :col_width], other[..., col_width:]

    def reduce_blocks(part):
        keep, send = by_core(part, 0)
        pair_sum = (keep.astype(f32) + lax.ppermute(send, "tensor", sibling).astype(f32)).astype(bf16)
        chip = tensor_index // 2
        total = lax.dynamic_index_in_dim(pair_sum, chip, 0, keepdims=False).astype(f32)
        for k in range(1, half_count):
            outgoing = lax.dynamic_index_in_dim(pair_sum, chip ^ k, 0, keepdims=False)
            partners = [(t, ((t // 2) ^ k) * 2 + t % 2) for t in range(tensor_count)]
            total = total + lax.ppermute(outgoing, "tensor", partners).astype(f32)
        return total

    projected = jnp.einsum(
        "trc,tcn->rn", mine_tok, proj_mine, preferred_element_type=f32
    ) + jnp.einsum("trc,tcn->rn", other_tok, proj_other, preferred_element_type=f32)
    down_grad = jnp.einsum(
        "trc,dtc->rd", mine_cot, out_mine, preferred_element_type=f32
    ) + jnp.einsum("trc,dtc->rd", other_cot, out_other, preferred_element_type=f32)
    proj4 = projected.reshape(owned_rows, 4, head_dim)
    activated = jax.nn.silu(proj4).astype(bf16)
    gating = activated[:, 0]
    values = activated[:, 1]
    queries = activated[:, 2]
    keys_head = activated[:, 3]
    scores = jnp.einsum("md,nd->mn", queries, keys_head, preferred_element_type=f32)
    allowed = (compact_slot[:, None] == compact_slot[None, :]) & (
        compact_ids[:, None] >= compact_ids[None, :]
    )
    weights = jnp.where(allowed, jax.nn.silu(scores * score_scale) / MAXLEN, 0.0).astype(bf16)
    attended = jnp.einsum("mn,nd->md", weights, values, preferred_element_type=f32)
    inv_rms = lax.rsqrt(jnp.mean(attended * attended, axis=-1, keepdims=True) + norm_eps)
    normed = attended * inv_rms * head_gain
    gated = (normed * gating).astype(bf16)
    own_gated = lax.dynamic_slice_in_dim(gated, inner_start, col_width, 1)
    out_part = jnp.einsum("rc,ctk->trk", own_gated, own_out, preferred_element_type=f32)

    d_normed = down_grad * gating
    d_gating = down_grad * normed
    scaled = head_gain * d_normed
    d_attended = (
        inv_rms * scaled
        - attended * inv_rms**3 * jnp.mean(attended * scaled, axis=-1, keepdims=True)
    ).astype(bf16)
    d_weights = jnp.einsum("md,nd->mn", d_attended, values, preferred_element_type=f32)
    d_values = jnp.einsum("mn,md->nd", weights, d_attended, preferred_element_type=f32)
    d_scores = jnp.where(
        allowed, d_weights * silu_slope(scores * score_scale) * (score_scale / MAXLEN), 0.0
    ).astype(bf16)
    d_queries = jnp.einsum("mn,nd->md", d_scores, keys_head, preferred_element_type=f32)
    d_keys = jnp.einsum("mn,md->nd", d_scores, queries, preferred_element_type=f32)
    d_activated = jnp.stack([d_gating, d_values, d_queries, d_keys], axis=1)
    d_projected = (d_activated * silu_slope(proj4)).astype(bf16)
    own_grad = lax.dynamic_slice_in_dim(d_projected, inner_start, col_width, 2).reshape(
        owned_rows, 4 * col_width
    )
    grad_part = jnp.einsum("rn,tkn->trk", own_grad, own_proj, preferred_element_type=f32)
    both_sum = reduce_blocks(jnp.concatenate([out_part, grad_part], axis=2).astype(bf16))
    out_sum = both_sum[:, :col_width]
    grad_sum = both_sum[:, col_width:]
    mixed_out = (own_tokens.astype(f32) + out_sum).astype(bf16)
    token_rows = (own_cotan.astype(f32) + grad_sum).astype(bf16)

    def by_rows(term_mine, term_other):
        pair = jnp.stack([term_mine, term_other], axis=1)
        pair = jnp.where(core == 0, pair, pair[:, ::-1])
        return pair.reshape((D,) + term_mine.shape[2:])

    proj_term = by_rows(
        jnp.einsum("trc,rn->tcn", mine_tok, own_grad, preferred_element_type=f32),
        jnp.einsum("trc,rn->tcn", other_tok, own_grad, preferred_element_type=f32),
    )
    out_term = by_rows(
        jnp.einsum("trc,rd->tcd", mine_cot, own_gated, preferred_element_type=f32),
        jnp.einsum("trc,rd->tcd", other_cot, own_gated, preferred_element_type=f32),
    )
    terms = jnp.concatenate([proj_term, out_term], axis=1).astype(bf16)
    bit_count = dp_count.bit_length() - 1
    term_sum = terms.reshape((2,) * bit_count + (D // dp_count,) + terms.shape[1:]).astype(f32)
    for level in range(bit_count - 1, -1, -1):
        my_bit = (dp_index >> level) & 1
        keep = lax.dynamic_index_in_dim(term_sum, my_bit, 0, keepdims=False)
        send = lax.dynamic_index_in_dim(term_sum, 1 - my_bit, 0, keepdims=False)
        partners = [(d, d ^ (1 << level)) for d in range(dp_count)]
        term_sum = keep + lax.ppermute(send.astype(bf16), "dp", partners).astype(f32)
    proj_grad = term_sum[:, : 4 * col_width].reshape(-1, 4, col_width)
    out_grad = term_sum[:, 4 * col_width :].T

    back_src = jnp.minimum(recv_start[:, None] + places[None, :], owned_rows - 1)
    back_send = pick_rows(back_src.reshape(-1), token_rows).reshape(dp_count, MAXLEN, col_width)
    back_grads = exchange(back_send)
    back_grads = back_grads.reshape(dp_count * MAXLEN, col_width)
    load_ids = jnp.arange(load_rows, dtype=jnp.int32)
    seq_of = jnp.sum((load_ids[:, None] >= my_starts[None, :]).astype(jnp.int32), axis=1) - 1
    seq_pick = seq_of[:, None] == seq_ids[None, :]
    owner_of = jnp.sum(jnp.where(seq_pick, my_owners[None, :], 0), axis=1)
    start_of = jnp.sum(jnp.where(seq_pick, my_starts[None, :], 0), axis=1)
    back_ids = (owner_of ^ dp_index) * MAXLEN + jnp.minimum(load_ids - start_of, MAXLEN - 1)
    row_used = load_ids < jnp.sum(my_lengths)
    token_grad = pick_rows(jnp.where(row_used, back_ids, -1), back_grads)
    return (mixed_out, token_grad, proj_grad, out_grad)


def solution(mesh):
    in_specs = (P("dp", "tensor"), P("dp", "tensor"), P(), P(), P(), P(), P())
    out_specs = (P("dp", "tensor"), P("dp", "tensor"), P("dp", None, "tensor"), P("tensor", "dp"))
    return jax.shard_map(local, mesh=mesh, in_specs=in_specs, out_specs=out_specs, check_vma=False)
```

```python
import math

import jax
import jax.numpy as jnp
from jax import lax
from jax.sharding import PartitionSpec as P

D = 1024
H = 8
MAXLEN = 192


norm_eps = 1e-05


def silu_slope(argument):
    sigmoid_val = jax.nn.sigmoid(argument)
    return sigmoid_val * (1.0 + argument * (1.0 - sigmoid_val))


def exclusive_sum(counts):
    return jnp.cumsum(counts) - counts


def local(tokens, cotangent, lengths, owners, proj_weight, norm_gain, out_weight):
    f32 = jnp.float32
    bf16 = jnp.bfloat16
    dp_count = lax.axis_size("dp")
    tensor_count = lax.axis_size("tensor")
    dp_index = lax.axis_index("dp")
    tensor_index = lax.axis_index("tensor")
    col_width = tokens.shape[1]
    load_rows = tokens.shape[0]
    head_dim = D // H
    score_scale = 1.0 / math.sqrt(head_dim)
    owned_rows = dp_count * (9 * MAXLEN // 16)
    places = jnp.arange(MAXLEN, dtype=jnp.int32)
    peer_ids = jnp.arange(dp_count, dtype=jnp.int32)
    seq_ids = jnp.arange(lengths.shape[1], dtype=jnp.int32)

    my_lengths = lengths[dp_index]
    my_owners = owners[dp_index]
    my_starts = exclusive_sum(my_lengths)
    sent_to = my_owners[None, :] == peer_ids[:, None]
    send_start = jnp.sum(jnp.where(sent_to, my_starts[None, :], 0), axis=1)
    send_ids = jnp.minimum(send_start[:, None] + places[None, :], load_rows - 1)
    def exchange(blocks):
        pieces = [lax.dynamic_index_in_dim(blocks, dp_index, 0, keepdims=False)]
        for k in range(1, dp_count):
            outgoing = lax.dynamic_index_in_dim(blocks, dp_index ^ k, 0, keepdims=False)
            pieces.append(lax.ppermute(outgoing, "dp", [(d, d ^ k) for d in range(dp_count)]))
        return jnp.stack(pieces)

    def pick_rows(row_ids, source):
        one_hot = (row_ids[:, None] == jnp.arange(source.shape[0], dtype=jnp.int32)[None, :]).astype(bf16)
        return jnp.dot(one_hot, source, preferred_element_type=f32).astype(bf16)

    flat_send = send_ids.reshape(-1)
    send_both = jnp.concatenate(
        [pick_rows(flat_send, tokens), pick_rows(flat_send, cotangent)], axis=1
    ).reshape(dp_count, MAXLEN, 2 * col_width)
    recv_both = exchange(send_both)

    half_count = tensor_count // 2
    core = tensor_index % 2

    def by_core(weight, axis):
        split = weight.reshape(weight.shape[:axis] + (half_count, 2) + weight.shape[axis + 1 :])
        return (
            lax.dynamic_index_in_dim(split, core, axis + 1, keepdims=False),
            lax.dynamic_index_in_dim(split, 1 - core, axis + 1, keepdims=False),
        )

    head_start = tensor_index * H // tensor_count * head_dim
    own_start = tensor_index * col_width
    inner_start = own_start - head_start
    head_proj = lax.dynamic_slice_in_dim(proj_weight, head_start, head_dim, 2).reshape(
        tensor_count, col_width, 4 * head_dim
    )
    own_proj = lax.dynamic_slice_in_dim(proj_weight, own_start, col_width, 2).reshape(
        tensor_count, col_width, 4 * col_width
    )
    head_out = lax.dynamic_slice_in_dim(out_weight, head_start, head_dim, 0).reshape(
        head_dim, tensor_count, col_width
    )
    head_gain = lax.dynamic_slice_in_dim(norm_gain, head_start, head_dim, 0)

    proj_mine, proj_other = by_core(head_proj, 0)
    out_mine, out_other = by_core(head_out, 1)
    own_out = lax.dynamic_slice_in_dim(out_weight, own_start, col_width, 0).reshape(
        col_width, tensor_count, col_width
    )
    recv_len = jnp.sum(jnp.where(owners == dp_index, lengths, 0), axis=1)
    recv_start = exclusive_sum(recv_len)
    back_src = jnp.minimum(recv_start[:, None] + places[None, :], owned_rows - 1)
    back_pick = (
        back_src.reshape(-1)[:, None] == jnp.arange(owned_rows, dtype=jnp.int32)[None, :]
    ).astype(bf16)
    load_ids = jnp.arange(load_rows, dtype=jnp.int32)
    seq_of = jnp.sum((load_ids[:, None] >= my_starts[None, :]).astype(jnp.int32), axis=1) - 1
    seq_pick = seq_of[:, None] == seq_ids[None, :]
    owner_of = jnp.sum(jnp.where(seq_pick, my_owners[None, :], 0), axis=1)
    start_of = jnp.sum(jnp.where(seq_pick, my_starts[None, :], 0), axis=1)
    back_ids = (owner_of ^ dp_index) * MAXLEN + jnp.minimum(load_ids - start_of, MAXLEN - 1)
    row_used = load_ids < jnp.sum(my_lengths)
    final_ids = jnp.where(row_used, back_ids, -1)
    final_pick = (
        final_ids[:, None] == jnp.arange(dp_count * MAXLEN, dtype=jnp.int32)[None, :]
    ).astype(bf16)
    weight_pack = (
        proj_mine, proj_other, out_mine, out_other, own_proj, own_out, head_gain, back_pick, final_pick
    )
    recv_both, weight_pack = lax.optimization_barrier((recv_both, weight_pack))
    (
        proj_mine, proj_other, out_mine, out_other, own_proj, own_out, head_gain, back_pick, final_pick
    ) = weight_pack

    compact_ids = jnp.arange(owned_rows, dtype=jnp.int32)
    compact_slot = (
        jnp.sum((compact_ids[:, None] >= recv_start[None, :]).astype(jnp.int32), axis=1) - 1
    )
    slot_pick = compact_slot[:, None] == peer_ids[None, :]
    compact_start = jnp.sum(jnp.where(slot_pick, recv_start[None, :], 0), axis=1)
    gather_ids = (compact_slot ^ dp_index) * MAXLEN + compact_ids - compact_start
    own_both = pick_rows(gather_ids, recv_both.reshape(dp_count * MAXLEN, 2 * col_width))
    own_tokens = own_both[:, :col_width]
    own_cotan = own_both[:, col_width:]

    same_core = [[2 * z + c for z in range(half_count)] for c in range(2)]
    sibling = [(t, t ^ 1) for t in range(tensor_count)]
    mine = lax.all_gather(own_both, "tensor", axis=0, tiled=False, axis_index_groups=same_core)
    other = lax.ppermute(mine, "tensor", sibling)
    mine_tok, mine_cot = mine[..., :col_width], mine[..., col_width:]
    other_tok, other_cot = other[..., :col_width], other[..., col_width:]

    def sibling_sum(part):
        keep, send = by_core(part, 0)
        return (keep.astype(f32) + lax.ppermute(send, "tensor", sibling).astype(f32)).astype(bf16)

    def reduce_blocks(pair_sum):
        pieces = lax.all_to_all(pair_sum, "tensor", 0, 0, tiled=True, axis_index_groups=same_core)
        return jnp.sum(pieces.astype(f32), axis=0)

    projected = jnp.einsum(
        "trc,tcn->rn", mine_tok, proj_mine, preferred_element_type=f32
    ) + jnp.einsum("trc,tcn->rn", other_tok, proj_other, preferred_element_type=f32)
    down_grad = jnp.einsum(
        "trc,dtc->rd", mine_cot, out_mine, preferred_element_type=f32
    ) + jnp.einsum("trc,dtc->rd", other_cot, out_other, preferred_element_type=f32)
    proj4 = projected.reshape(owned_rows, 4, head_dim)
    activated = jax.nn.silu(proj4).astype(bf16)
    gating = activated[:, 0]
    values = activated[:, 1]
    queries = activated[:, 2]
    keys_head = activated[:, 3]
    scores = jnp.einsum("md,nd->mn", queries, keys_head, preferred_element_type=f32)
    allowed = (compact_slot[:, None] == compact_slot[None, :]) & (
        compact_ids[:, None] >= compact_ids[None, :]
    )
    weights = jnp.where(allowed, jax.nn.silu(scores * score_scale) / MAXLEN, 0.0).astype(bf16)
    attended = jnp.einsum("mn,nd->md", weights, values, preferred_element_type=f32)
    inv_rms = lax.rsqrt(jnp.mean(attended * attended, axis=-1, keepdims=True) + norm_eps)
    normed = attended * inv_rms * head_gain
    gated = (normed * gating).astype(bf16)
    own_gated = lax.dynamic_slice_in_dim(gated, inner_start, col_width, 1)
    out_part = jnp.einsum("rc,ctk->trk", own_gated, own_out, preferred_element_type=f32)

    d_normed = down_grad * gating
    d_gating = down_grad * normed
    scaled = head_gain * d_normed
    d_attended = (
        inv_rms * scaled
        - attended * inv_rms**3 * jnp.mean(attended * scaled, axis=-1, keepdims=True)
    ).astype(bf16)
    d_weights = jnp.einsum("md,nd->mn", d_attended, values, preferred_element_type=f32)
    d_values = jnp.einsum("mn,md->nd", weights, d_attended, preferred_element_type=f32)
    d_scores = jnp.where(
        allowed, d_weights * silu_slope(scores * score_scale) * (score_scale / MAXLEN), 0.0
    ).astype(bf16)
    d_queries = jnp.einsum("mn,nd->md", d_scores, keys_head, preferred_element_type=f32)
    d_keys = jnp.einsum("mn,md->nd", d_scores, queries, preferred_element_type=f32)
    d_activated = jnp.stack([d_gating, d_values, d_queries, d_keys], axis=1)
    d_projected = (d_activated * silu_slope(proj4)).astype(bf16)
    own_grad = lax.dynamic_slice_in_dim(d_projected, inner_start, col_width, 2).reshape(
        owned_rows, 4 * col_width
    )
    grad_part = jnp.einsum("rn,tkn->trk", own_grad, own_proj, preferred_element_type=f32)
    both_sum = reduce_blocks(
        jnp.concatenate([sibling_sum(out_part.astype(bf16)), sibling_sum(grad_part.astype(bf16))], axis=2)
    )
    out_sum = both_sum[:, :col_width]
    grad_sum = both_sum[:, col_width:]
    mixed_out = (own_tokens.astype(f32) + out_sum).astype(bf16)
    token_rows = (own_cotan.astype(f32) + grad_sum).astype(bf16)

    def by_rows(term_mine, term_other):
        pair = jnp.stack([term_mine, term_other], axis=1)
        pair = jnp.where(core == 0, pair, pair[:, ::-1])
        return pair.reshape((D,) + term_mine.shape[2:])

    proj_term = by_rows(
        jnp.einsum("trc,rn->tcn", mine_tok, own_grad, preferred_element_type=f32),
        jnp.einsum("trc,rn->tcn", other_tok, own_grad, preferred_element_type=f32),
    )
    out_term = by_rows(
        jnp.einsum("trc,rd->tcd", mine_cot, own_gated, preferred_element_type=f32),
        jnp.einsum("trc,rd->tcd", other_cot, own_gated, preferred_element_type=f32),
    )
    terms = jnp.concatenate([proj_term, out_term], axis=1).astype(bf16)
    bit_count = dp_count.bit_length() - 1
    term_sum = terms.reshape((2,) * bit_count + (D // dp_count,) + terms.shape[1:]).astype(f32)
    for level in range(bit_count - 1, -1, -1):
        my_bit = (dp_index >> level) & 1
        keep = lax.dynamic_index_in_dim(term_sum, my_bit, 0, keepdims=False)
        send = lax.dynamic_index_in_dim(term_sum, 1 - my_bit, 0, keepdims=False)
        partners = [(d, d ^ (1 << level)) for d in range(dp_count)]
        term_sum = keep + lax.ppermute(send.astype(bf16), "dp", partners).astype(f32)
    proj_grad = term_sum[:, : 4 * col_width].reshape(-1, 4, col_width)
    out_grad = term_sum[:, 4 * col_width :].T

    back_send = jnp.dot(back_pick, token_rows, preferred_element_type=f32).astype(bf16)
    back_grads = exchange(back_send.reshape(dp_count, MAXLEN, col_width))
    back_grads = back_grads.reshape(dp_count * MAXLEN, col_width)
    token_grad = jnp.dot(final_pick, back_grads, preferred_element_type=f32).astype(bf16)
    return (mixed_out, token_grad, proj_grad, out_grad)


def solution(mesh):
    in_specs = (P("dp", "tensor"), P("dp", "tensor"), P(), P(), P(), P(), P())
    out_specs = (P("dp", "tensor"), P("dp", "tensor"), P("dp", None, "tensor"), P("tensor", "dp"))
    return jax.shard_map(local, mesh=mesh, in_specs=in_specs, out_specs=out_specs, check_vma=False)
```

```python
import math

import jax
import jax.numpy as jnp
from jax import lax
from jax.sharding import PartitionSpec as P

D = 1024
H = 8
MAXLEN = 192


norm_eps = 1e-05


def silu_slope(argument):
    sigmoid_val = jax.nn.sigmoid(argument)
    return sigmoid_val * (1.0 + argument * (1.0 - sigmoid_val))


def exclusive_sum(counts):
    return jnp.cumsum(counts) - counts


def local(tokens, cotangent, lengths, owners, proj_weight, norm_gain, out_weight):
    f32 = jnp.float32
    bf16 = jnp.bfloat16
    dp_count = lax.axis_size("dp")
    tensor_count = lax.axis_size("tensor")
    dp_index = lax.axis_index("dp")
    tensor_index = lax.axis_index("tensor")
    col_width = tokens.shape[1]
    load_rows = tokens.shape[0]
    head_dim = D // H
    score_scale = 1.0 / math.sqrt(head_dim)
    owned_rows = dp_count * (9 * MAXLEN // 16)
    places = jnp.arange(MAXLEN, dtype=jnp.int32)
    peer_ids = jnp.arange(dp_count, dtype=jnp.int32)
    seq_ids = jnp.arange(lengths.shape[1], dtype=jnp.int32)

    my_lengths = lengths[dp_index]
    my_owners = owners[dp_index]
    my_starts = exclusive_sum(my_lengths)
    sent_to = my_owners[None, :] == peer_ids[:, None]
    send_start = jnp.sum(jnp.where(sent_to, my_starts[None, :], 0), axis=1)
    send_ids = jnp.minimum(send_start[:, None] + places[None, :], load_rows - 1)
    def exchange(blocks):
        pieces = [lax.dynamic_index_in_dim(blocks, dp_index, 0, keepdims=False)]
        for k in range(1, dp_count):
            outgoing = lax.dynamic_index_in_dim(blocks, dp_index ^ k, 0, keepdims=False)
            pieces.append(lax.ppermute(outgoing, "dp", [(d, d ^ k) for d in range(dp_count)]))
        return jnp.stack(pieces)

    def pick_rows(row_ids, source):
        one_hot = (row_ids[:, None] == jnp.arange(source.shape[0], dtype=jnp.int32)[None, :]).astype(bf16)
        return jnp.dot(one_hot, source, preferred_element_type=f32).astype(bf16)

    flat_send = send_ids.reshape(-1)
    send_both = jnp.concatenate(
        [pick_rows(flat_send, tokens), pick_rows(flat_send, cotangent)], axis=1
    ).reshape(dp_count, MAXLEN, 2 * col_width)
    recv_both = exchange(send_both)

    half_count = tensor_count // 2
    core = tensor_index % 2

    def by_core(weight, axis):
        split = weight.reshape(weight.shape[:axis] + (half_count, 2) + weight.shape[axis + 1 :])
        return (
            lax.dynamic_index_in_dim(split, core, axis + 1, keepdims=False),
            lax.dynamic_index_in_dim(split, 1 - core, axis + 1, keepdims=False),
        )

    head_start = tensor_index * H // tensor_count * head_dim
    own_start = tensor_index * col_width
    inner_start = own_start - head_start
    head_proj = lax.dynamic_slice_in_dim(proj_weight, head_start, head_dim, 2).reshape(
        tensor_count, col_width, 4 * head_dim
    )
    own_proj = lax.dynamic_slice_in_dim(proj_weight, own_start, col_width, 2).reshape(
        tensor_count, col_width, 4 * col_width
    )
    head_out = lax.dynamic_slice_in_dim(out_weight, head_start, head_dim, 0).reshape(
        head_dim, tensor_count, col_width
    )
    head_gain = lax.dynamic_slice_in_dim(norm_gain, head_start, head_dim, 0)

    proj_mine, proj_other = by_core(head_proj, 0)
    out_mine, out_other = by_core(head_out, 1)
    own_out = lax.dynamic_slice_in_dim(out_weight, own_start, col_width, 0).reshape(
        col_width, tensor_count, col_width
    )
    weight_pack = (proj_mine, proj_other, out_mine, out_other, own_proj, own_out, head_gain)
    recv_both, weight_pack = lax.optimization_barrier((recv_both, weight_pack))
    proj_mine, proj_other, out_mine, out_other, own_proj, own_out, head_gain = weight_pack

    recv_len = jnp.sum(jnp.where(owners == dp_index, lengths, 0), axis=1)
    recv_start = exclusive_sum(recv_len)
    compact_ids = jnp.arange(owned_rows, dtype=jnp.int32)
    compact_slot = (
        jnp.sum((compact_ids[:, None] >= recv_start[None, :]).astype(jnp.int32), axis=1) - 1
    )
    slot_pick = compact_slot[:, None] == peer_ids[None, :]
    compact_start = jnp.sum(jnp.where(slot_pick, recv_start[None, :], 0), axis=1)
    gather_ids = (compact_slot ^ dp_index) * MAXLEN + compact_ids - compact_start
    own_both = pick_rows(gather_ids, recv_both.reshape(dp_count * MAXLEN, 2 * col_width))
    own_tokens = own_both[:, :col_width]
    own_cotan = own_both[:, col_width:]

    same_core = [[2 * z + c for z in range(half_count)] for c in range(2)]
    sibling = [(t, t ^ 1) for t in range(tensor_count)]
    mine = lax.all_gather(own_both, "tensor", axis=0, tiled=False, axis_index_groups=same_core)
    other = lax.ppermute(mine, "tensor", sibling)
    mine_tok, mine_cot = mine[..., :col_width], mine[..., col_width:]
    other_tok, other_cot = other[..., :col_width], other[..., col_width:]

    def sibling_sum(part):
        keep, send = by_core(part, 0)
        return (keep.astype(f32) + lax.ppermute(send, "tensor", sibling).astype(f32)).astype(bf16)

    def reduce_blocks(pair_sum):
        pieces = lax.all_to_all(pair_sum, "tensor", 0, 0, tiled=True, axis_index_groups=same_core)
        return jnp.sum(pieces.astype(f32), axis=0)

    projected = jnp.einsum(
        "trc,tcn->rn", mine_tok, proj_mine, preferred_element_type=f32
    ) + jnp.einsum("trc,tcn->rn", other_tok, proj_other, preferred_element_type=f32)
    down_grad = jnp.einsum(
        "trc,dtc->rd", mine_cot, out_mine, preferred_element_type=f32
    ) + jnp.einsum("trc,dtc->rd", other_cot, out_other, preferred_element_type=f32)
    proj4 = projected.reshape(owned_rows, 4, head_dim)
    activated = jax.nn.silu(proj4).astype(bf16)
    gating = activated[:, 0]
    values = activated[:, 1]
    queries = activated[:, 2]
    keys_head = activated[:, 3]
    scores = jnp.einsum("md,nd->mn", queries, keys_head, preferred_element_type=f32)
    allowed = (compact_slot[:, None] == compact_slot[None, :]) & (
        compact_ids[:, None] >= compact_ids[None, :]
    )
    weights = jnp.where(allowed, jax.nn.silu(scores * score_scale) / MAXLEN, 0.0).astype(bf16)
    attended = jnp.einsum("mn,nd->md", weights, values, preferred_element_type=f32)
    inv_rms = lax.rsqrt(jnp.mean(attended * attended, axis=-1, keepdims=True) + norm_eps)
    normed = attended * inv_rms * head_gain
    gated = (normed * gating).astype(bf16)
    own_gated = lax.dynamic_slice_in_dim(gated, inner_start, col_width, 1)
    out_part = jnp.einsum("rc,ctk->trk", own_gated, own_out, preferred_element_type=f32)

    d_normed = down_grad * gating
    d_gating = down_grad * normed
    scaled = head_gain * d_normed
    d_attended = (
        inv_rms * scaled
        - attended * inv_rms**3 * jnp.mean(attended * scaled, axis=-1, keepdims=True)
    ).astype(bf16)
    d_weights = jnp.einsum("md,nd->mn", d_attended, values, preferred_element_type=f32)
    d_values = jnp.einsum("mn,md->nd", weights, d_attended, preferred_element_type=f32)
    d_scores = jnp.where(
        allowed, d_weights * silu_slope(scores * score_scale) * (score_scale / MAXLEN), 0.0
    ).astype(bf16)
    d_queries = jnp.einsum("mn,nd->md", d_scores, keys_head, preferred_element_type=f32)
    d_keys = jnp.einsum("mn,md->nd", d_scores, queries, preferred_element_type=f32)
    d_activated = jnp.stack([d_gating, d_values, d_queries, d_keys], axis=1)
    d_projected = (d_activated * silu_slope(proj4)).astype(bf16)
    own_grad = lax.dynamic_slice_in_dim(d_projected, inner_start, col_width, 2).reshape(
        owned_rows, 4 * col_width
    )
    grad_part = jnp.einsum("rn,tkn->trk", own_grad, own_proj, preferred_element_type=f32)
    both_sum = reduce_blocks(
        jnp.concatenate([sibling_sum(out_part.astype(bf16)), sibling_sum(grad_part.astype(bf16))], axis=2)
    )
    out_sum = both_sum[:, :col_width]
    grad_sum = both_sum[:, col_width:]
    mixed_out = (own_tokens.astype(f32) + out_sum).astype(bf16)
    token_rows = (own_cotan.astype(f32) + grad_sum).astype(bf16)

    def by_rows(term_mine, term_other):
        pair = jnp.stack([term_mine, term_other], axis=1)
        pair = jnp.where(core == 0, pair, pair[:, ::-1])
        return pair.reshape((D,) + term_mine.shape[2:])

    proj_term = by_rows(
        jnp.einsum("trc,rn->tcn", mine_tok, own_grad, preferred_element_type=f32),
        jnp.einsum("trc,rn->tcn", other_tok, own_grad, preferred_element_type=f32),
    )
    out_term = by_rows(
        jnp.einsum("trc,rd->tcd", mine_cot, own_gated, preferred_element_type=f32),
        jnp.einsum("trc,rd->tcd", other_cot, own_gated, preferred_element_type=f32),
    )
    terms = jnp.concatenate([proj_term, out_term], axis=1).astype(bf16)
    bit_count = dp_count.bit_length() - 1
    term_sum = terms.reshape((2,) * bit_count + (D // dp_count,) + terms.shape[1:]).astype(f32)
    for level in range(bit_count - 1, -1, -1):
        my_bit = (dp_index >> level) & 1
        keep = lax.dynamic_index_in_dim(term_sum, my_bit, 0, keepdims=False)
        send = lax.dynamic_index_in_dim(term_sum, 1 - my_bit, 0, keepdims=False)
        partners = [(d, d ^ (1 << level)) for d in range(dp_count)]
        term_sum = keep + lax.ppermute(send.astype(bf16), "dp", partners).astype(f32)
    proj_grad = term_sum[:, : 4 * col_width].reshape(-1, 4, col_width)
    out_grad = term_sum[:, 4 * col_width :].T

    back_src = jnp.minimum(recv_start[:, None] + places[None, :], owned_rows - 1)
    back_send = pick_rows(back_src.reshape(-1), token_rows).reshape(dp_count, MAXLEN, col_width)
    back_grads = exchange(back_send)
    back_grads = back_grads.reshape(dp_count * MAXLEN, col_width)
    load_ids = jnp.arange(load_rows, dtype=jnp.int32)
    seq_of = jnp.sum((load_ids[:, None] >= my_starts[None, :]).astype(jnp.int32), axis=1) - 1
    seq_pick = seq_of[:, None] == seq_ids[None, :]
    owner_of = jnp.sum(jnp.where(seq_pick, my_owners[None, :], 0), axis=1)
    start_of = jnp.sum(jnp.where(seq_pick, my_starts[None, :], 0), axis=1)
    back_ids = (owner_of ^ dp_index) * MAXLEN + jnp.minimum(load_ids - start_of, MAXLEN - 1)
    row_used = load_ids < jnp.sum(my_lengths)
    token_grad = pick_rows(jnp.where(row_used, back_ids, -1), back_grads)
    return (mixed_out, token_grad, proj_grad, out_grad)


def solution(mesh):
    in_specs = (P("dp", "tensor"), P("dp", "tensor"), P(), P(), P(), P(), P())
    out_specs = (P("dp", "tensor"), P("dp", "tensor"), P("dp", None, "tensor"), P("tensor", "dp"))
    return jax.shard_map(local, mesh=mesh, in_specs=in_specs, out_specs=out_specs, check_vma=False)
```

```python
import math

import jax
import jax.numpy as jnp
from jax import lax
from jax.sharding import PartitionSpec as P

D = 1024
H = 8
MAXLEN = 192


norm_eps = 1e-05


def silu_slope(argument):
    sigmoid_val = jax.nn.sigmoid(argument)
    return sigmoid_val * (1.0 + argument * (1.0 - sigmoid_val))


def exclusive_sum(counts):
    return jnp.cumsum(counts) - counts


def local(tokens, cotangent, lengths, owners, proj_weight, norm_gain, out_weight):
    f32 = jnp.float32
    bf16 = jnp.bfloat16
    dp_count = lax.axis_size("dp")
    tensor_count = lax.axis_size("tensor")
    dp_index = lax.axis_index("dp")
    tensor_index = lax.axis_index("tensor")
    col_width = tokens.shape[1]
    load_rows = tokens.shape[0]
    head_dim = D // H
    score_scale = 1.0 / math.sqrt(head_dim)
    owned_rows = dp_count * (9 * MAXLEN // 16)
    places = jnp.arange(MAXLEN, dtype=jnp.int32)
    peer_ids = jnp.arange(dp_count, dtype=jnp.int32)
    seq_ids = jnp.arange(lengths.shape[1], dtype=jnp.int32)

    my_lengths = lengths[dp_index]
    my_owners = owners[dp_index]
    my_starts = exclusive_sum(my_lengths)
    sent_to = my_owners[None, :] == peer_ids[:, None]
    send_start = jnp.sum(jnp.where(sent_to, my_starts[None, :], 0), axis=1)
    send_ids = jnp.minimum(send_start[:, None] + places[None, :], load_rows - 1)
    def exchange(blocks):
        pieces = [lax.dynamic_index_in_dim(blocks, dp_index, 0, keepdims=False)]
        for k in range(1, dp_count):
            outgoing = lax.dynamic_index_in_dim(blocks, dp_index ^ k, 0, keepdims=False)
            pieces.append(lax.ppermute(outgoing, "dp", [(d, d ^ k) for d in range(dp_count)]))
        return jnp.stack(pieces)

    def pick_rows(row_ids, source):
        one_hot = (row_ids[:, None] == jnp.arange(source.shape[0], dtype=jnp.int32)[None, :]).astype(bf16)
        return jnp.dot(one_hot, source, preferred_element_type=f32).astype(bf16)

    flat_send = send_ids.reshape(-1)
    send_both = jnp.concatenate(
        [pick_rows(flat_send, tokens), pick_rows(flat_send, cotangent)], axis=1
    ).reshape(dp_count, MAXLEN, 2 * col_width)
    recv_both = exchange(send_both)

    half_count = tensor_count // 2
    core = tensor_index % 2

    def by_core(weight, axis):
        split = weight.reshape(weight.shape[:axis] + (half_count, 2) + weight.shape[axis + 1 :])
        return (
            lax.dynamic_index_in_dim(split, core, axis + 1, keepdims=False),
            lax.dynamic_index_in_dim(split, 1 - core, axis + 1, keepdims=False),
        )

    head_start = tensor_index * H // tensor_count * head_dim
    own_start = tensor_index * col_width
    inner_start = own_start - head_start
    head_proj = lax.dynamic_slice_in_dim(proj_weight, head_start, head_dim, 2).reshape(
        tensor_count, col_width, 4 * head_dim
    )
    own_proj = lax.dynamic_slice_in_dim(proj_weight, own_start, col_width, 2).reshape(
        tensor_count, col_width, 4 * col_width
    )
    head_out = lax.dynamic_slice_in_dim(out_weight, head_start, head_dim, 0).reshape(
        head_dim, tensor_count, col_width
    )
    head_gain = lax.dynamic_slice_in_dim(norm_gain, head_start, head_dim, 0)

    proj_mine, proj_other = by_core(head_proj, 0)
    out_mine, out_other = by_core(head_out, 1)
    own_out = lax.dynamic_slice_in_dim(out_weight, own_start, col_width, 0).reshape(
        col_width, tensor_count, col_width
    )
    weight_pack = (proj_mine, proj_other, out_mine, out_other, own_proj, own_out, head_gain)
    recv_both, weight_pack = lax.optimization_barrier((recv_both, weight_pack))
    proj_mine, proj_other, out_mine, out_other, own_proj, own_out, head_gain = weight_pack

    recv_len = jnp.sum(jnp.where(owners == dp_index, lengths, 0), axis=1)
    recv_start = exclusive_sum(recv_len)
    compact_ids = jnp.arange(owned_rows, dtype=jnp.int32)
    compact_slot = (
        jnp.sum((compact_ids[:, None] >= recv_start[None, :]).astype(jnp.int32), axis=1) - 1
    )
    slot_pick = compact_slot[:, None] == peer_ids[None, :]
    compact_start = jnp.sum(jnp.where(slot_pick, recv_start[None, :], 0), axis=1)
    gather_ids = (compact_slot ^ dp_index) * MAXLEN + compact_ids - compact_start
    own_both = pick_rows(gather_ids, recv_both.reshape(dp_count * MAXLEN, 2 * col_width))
    own_tokens = own_both[:, :col_width]
    own_cotan = own_both[:, col_width:]

    same_core = [[2 * z + c for z in range(half_count)] for c in range(2)]
    sibling = [(t, t ^ 1) for t in range(tensor_count)]
    mine = lax.all_gather(own_both, "tensor", axis=0, tiled=False, axis_index_groups=same_core)
    other = lax.ppermute(mine, "tensor", sibling)
    mine_tok, mine_cot = mine[..., :col_width], mine[..., col_width:]
    other_tok, other_cot = other[..., :col_width], other[..., col_width:]

    def sibling_sum(part):
        keep, send = by_core(part, 0)
        return (keep.astype(f32) + lax.ppermute(send, "tensor", sibling).astype(f32)).astype(bf16)

    def reduce_blocks(pair_sum):
        pieces = lax.all_to_all(pair_sum, "tensor", 0, 0, tiled=True, axis_index_groups=same_core)
        return jnp.sum(pieces.astype(f32), axis=0)

    projected = jnp.einsum(
        "trc,tcn->rn", mine_tok, proj_mine, preferred_element_type=f32
    ) + jnp.einsum("trc,tcn->rn", other_tok, proj_other, preferred_element_type=f32)
    down_grad = jnp.einsum(
        "trc,dtc->rd", mine_cot, out_mine, preferred_element_type=f32
    ) + jnp.einsum("trc,dtc->rd", other_cot, out_other, preferred_element_type=f32)
    proj4 = projected.reshape(owned_rows, 4, head_dim)
    activated = jax.nn.silu(proj4).astype(bf16)
    gating = activated[:, 0]
    values = activated[:, 1]
    queries = activated[:, 2]
    keys_head = activated[:, 3]
    scores = jnp.einsum("md,nd->mn", queries, keys_head, preferred_element_type=f32)
    allowed = (compact_slot[:, None] == compact_slot[None, :]) & (
        compact_ids[:, None] >= compact_ids[None, :]
    )
    weights = jnp.where(allowed, jax.nn.silu(scores * score_scale) / MAXLEN, 0.0).astype(bf16)
    attended = jnp.einsum("mn,nd->md", weights, values, preferred_element_type=f32)
    inv_rms = lax.rsqrt(jnp.mean(attended * attended, axis=-1, keepdims=True) + norm_eps)
    normed = attended * inv_rms * head_gain
    gated = (normed * gating).astype(bf16)
    own_gated = lax.dynamic_slice_in_dim(gated, inner_start, col_width, 1)
    out_part = jnp.einsum("rc,ctk->trk", own_gated, own_out, preferred_element_type=f32)

    d_normed = down_grad * gating
    d_gating = down_grad * normed
    scaled = head_gain * d_normed
    d_attended = (
        inv_rms * scaled
        - attended * inv_rms**3 * jnp.mean(attended * scaled, axis=-1, keepdims=True)
    ).astype(bf16)
    d_weights = jnp.einsum("md,nd->mn", d_attended, values, preferred_element_type=f32)
    d_values = jnp.einsum("mn,md->nd", weights, d_attended, preferred_element_type=f32)
    d_scores = jnp.where(
        allowed, d_weights * silu_slope(scores * score_scale) * (score_scale / MAXLEN), 0.0
    ).astype(bf16)
    d_queries = jnp.einsum("mn,nd->md", d_scores, keys_head, preferred_element_type=f32)
    d_keys = jnp.einsum("mn,md->nd", d_scores, queries, preferred_element_type=f32)
    d_activated = jnp.stack([d_gating, d_values, d_queries, d_keys], axis=1)
    d_projected = (d_activated * silu_slope(proj4)).astype(bf16)
    own_grad = lax.dynamic_slice_in_dim(d_projected, inner_start, col_width, 2).reshape(
        owned_rows, 4 * col_width
    )
    grad_part = jnp.einsum("rn,tkn->trk", own_grad, own_proj, preferred_element_type=f32)
    both_sum = reduce_blocks(
        jnp.concatenate([sibling_sum(out_part.astype(bf16)), sibling_sum(grad_part.astype(bf16))], axis=2)
    )
    out_sum = both_sum[:, :col_width]
    grad_sum = both_sum[:, col_width:]
    mixed_out = (own_tokens.astype(f32) + out_sum).astype(bf16)
    token_rows = (own_cotan.astype(f32) + grad_sum).astype(bf16)

    def by_rows(term_mine, term_other):
        pair = jnp.stack([term_mine, term_other], axis=1)
        pair = jnp.where(core == 0, pair, pair[:, ::-1])
        return pair.reshape((D,) + term_mine.shape[2:])

    proj_term = by_rows(
        jnp.einsum("trc,rn->tcn", mine_tok, own_grad, preferred_element_type=f32),
        jnp.einsum("trc,rn->tcn", other_tok, own_grad, preferred_element_type=f32),
    )
    out_term = by_rows(
        jnp.einsum("trc,rd->tcd", mine_cot, own_gated, preferred_element_type=f32),
        jnp.einsum("trc,rd->tcd", other_cot, own_gated, preferred_element_type=f32),
    )
    terms = jnp.concatenate([proj_term, out_term], axis=1).astype(bf16)
    term_blocks = terms.reshape((dp_count, D // dp_count) + terms.shape[1:])
    term_sum = lax.dynamic_index_in_dim(term_blocks, dp_index, 0, keepdims=False).astype(f32)
    for k in range(1, dp_count):
        outgoing = lax.dynamic_index_in_dim(term_blocks, dp_index ^ k, 0, keepdims=False)
        partners = [(d, d ^ k) for d in range(dp_count)]
        term_sum = term_sum + lax.ppermute(outgoing, "dp", partners).astype(f32)
    proj_grad = term_sum[:, : 4 * col_width].reshape(-1, 4, col_width)
    out_grad = term_sum[:, 4 * col_width :].T

    back_src = jnp.minimum(recv_start[:, None] + places[None, :], owned_rows - 1)
    back_send = pick_rows(back_src.reshape(-1), token_rows).reshape(dp_count, MAXLEN, col_width)
    back_grads = exchange(back_send)
    back_grads = back_grads.reshape(dp_count * MAXLEN, col_width)
    load_ids = jnp.arange(load_rows, dtype=jnp.int32)
    seq_of = jnp.sum((load_ids[:, None] >= my_starts[None, :]).astype(jnp.int32), axis=1) - 1
    seq_pick = seq_of[:, None] == seq_ids[None, :]
    owner_of = jnp.sum(jnp.where(seq_pick, my_owners[None, :], 0), axis=1)
    start_of = jnp.sum(jnp.where(seq_pick, my_starts[None, :], 0), axis=1)
    back_ids = (owner_of ^ dp_index) * MAXLEN + jnp.minimum(load_ids - start_of, MAXLEN - 1)
    row_used = load_ids < jnp.sum(my_lengths)
    token_grad = pick_rows(jnp.where(row_used, back_ids, -1), back_grads)
    return (mixed_out, token_grad, proj_grad, out_grad)


def solution(mesh):
    in_specs = (P("dp", "tensor"), P("dp", "tensor"), P(), P(), P(), P(), P())
    out_specs = (P("dp", "tensor"), P("dp", "tensor"), P("dp", None, "tensor"), P("tensor", "dp"))
    return jax.shard_map(local, mesh=mesh, in_specs=in_specs, out_specs=out_specs, check_vma=False)
```

```python
import math

import jax
import jax.numpy as jnp
from jax import lax
from jax.sharding import PartitionSpec as P

D = 1024
H = 8
MAXLEN = 192


norm_eps = 1e-05


def silu_slope(argument):
    sigmoid_val = jax.nn.sigmoid(argument)
    return sigmoid_val * (1.0 + argument * (1.0 - sigmoid_val))


def exclusive_sum(counts):
    return jnp.cumsum(counts) - counts


def local(tokens, cotangent, lengths, owners, proj_weight, norm_gain, out_weight):
    f32 = jnp.float32
    bf16 = jnp.bfloat16
    dp_count = lax.axis_size("dp")
    tensor_count = lax.axis_size("tensor")
    dp_index = lax.axis_index("dp")
    tensor_index = lax.axis_index("tensor")
    col_width = tokens.shape[1]
    load_rows = tokens.shape[0]
    head_dim = D // H
    score_scale = 1.0 / math.sqrt(head_dim)
    owned_rows = dp_count * (9 * MAXLEN // 16)
    places = jnp.arange(MAXLEN, dtype=jnp.int32)
    peer_ids = jnp.arange(dp_count, dtype=jnp.int32)
    seq_ids = jnp.arange(lengths.shape[1], dtype=jnp.int32)

    my_lengths = lengths[dp_index]
    my_owners = owners[dp_index]
    my_starts = exclusive_sum(my_lengths)
    sent_to = my_owners[None, :] == peer_ids[:, None]
    send_start = jnp.sum(jnp.where(sent_to, my_starts[None, :], 0), axis=1)
    send_ids = jnp.minimum(send_start[:, None] + places[None, :], load_rows - 1)
    def exchange(blocks):
        pieces = [lax.dynamic_index_in_dim(blocks, dp_index, 0, keepdims=False)]
        for k in range(1, dp_count):
            outgoing = lax.dynamic_index_in_dim(blocks, dp_index ^ k, 0, keepdims=False)
            pieces.append(lax.ppermute(outgoing, "dp", [(d, d ^ k) for d in range(dp_count)]))
        return jnp.stack(pieces)

    def pick_rows(row_ids, source):
        one_hot = (row_ids[:, None] == jnp.arange(source.shape[0], dtype=jnp.int32)[None, :]).astype(bf16)
        return jnp.dot(one_hot, source, preferred_element_type=f32).astype(bf16)

    flat_send = send_ids.reshape(-1)
    send_both = jnp.concatenate(
        [pick_rows(flat_send, tokens), pick_rows(flat_send, cotangent)], axis=1
    ).reshape(dp_count, MAXLEN, 2 * col_width)
    recv_both = exchange(send_both)

    half_count = tensor_count // 2
    core = tensor_index % 2

    def by_core(weight, axis):
        split = weight.reshape(weight.shape[:axis] + (half_count, 2) + weight.shape[axis + 1 :])
        return (
            lax.dynamic_index_in_dim(split, core, axis + 1, keepdims=False),
            lax.dynamic_index_in_dim(split, 1 - core, axis + 1, keepdims=False),
        )

    head_start = tensor_index * H // tensor_count * head_dim
    own_start = tensor_index * col_width
    inner_start = own_start - head_start
    head_proj = lax.dynamic_slice_in_dim(proj_weight, head_start, head_dim, 2).reshape(
        tensor_count, col_width, 4 * head_dim
    )
    own_proj = lax.dynamic_slice_in_dim(proj_weight, own_start, col_width, 2).reshape(
        tensor_count, col_width, 4 * col_width
    )
    head_out = lax.dynamic_slice_in_dim(out_weight, head_start, head_dim, 0).reshape(
        head_dim, tensor_count, col_width
    )
    head_gain = lax.dynamic_slice_in_dim(norm_gain, head_start, head_dim, 0)

    proj_mine, proj_other = by_core(head_proj, 0)
    out_mine, out_other = by_core(head_out, 1)
    own_out = lax.dynamic_slice_in_dim(out_weight, own_start, col_width, 0).reshape(
        col_width, tensor_count, col_width
    )
    weight_pack = (proj_mine, proj_other, out_mine, out_other, head_gain)
    recv_both, weight_pack = lax.optimization_barrier((recv_both, weight_pack))
    proj_mine, proj_other, out_mine, out_other, head_gain = weight_pack

    recv_len = jnp.sum(jnp.where(owners == dp_index, lengths, 0), axis=1)
    recv_start = exclusive_sum(recv_len)
    compact_ids = jnp.arange(owned_rows, dtype=jnp.int32)
    compact_slot = (
        jnp.sum((compact_ids[:, None] >= recv_start[None, :]).astype(jnp.int32), axis=1) - 1
    )
    slot_pick = compact_slot[:, None] == peer_ids[None, :]
    compact_start = jnp.sum(jnp.where(slot_pick, recv_start[None, :], 0), axis=1)
    gather_ids = (compact_slot ^ dp_index) * MAXLEN + compact_ids - compact_start
    own_both = pick_rows(gather_ids, recv_both.reshape(dp_count * MAXLEN, 2 * col_width))
    own_tokens = own_both[:, :col_width]
    own_cotan = own_both[:, col_width:]

    same_core = [[2 * z + c for z in range(half_count)] for c in range(2)]
    sibling = [(t, t ^ 1) for t in range(tensor_count)]
    mine = lax.all_gather(own_both, "tensor", axis=0, tiled=False, axis_index_groups=same_core)
    other = lax.ppermute(mine, "tensor", sibling)
    mine_tok, mine_cot = mine[..., :col_width], mine[..., col_width:]
    other_tok, other_cot = other[..., :col_width], other[..., col_width:]

    def sibling_sum(part):
        keep, send = by_core(part, 0)
        return (keep.astype(f32) + lax.ppermute(send, "tensor", sibling).astype(f32)).astype(bf16)

    def reduce_blocks(pair_sum):
        pieces = lax.all_to_all(pair_sum, "tensor", 0, 0, tiled=True, axis_index_groups=same_core)
        return jnp.sum(pieces.astype(f32), axis=0)

    projected = jnp.einsum(
        "trc,tcn->rn", mine_tok, proj_mine, preferred_element_type=f32
    ) + jnp.einsum("trc,tcn->rn", other_tok, proj_other, preferred_element_type=f32)
    down_grad = jnp.einsum(
        "trc,dtc->rd", mine_cot, out_mine, preferred_element_type=f32
    ) + jnp.einsum("trc,dtc->rd", other_cot, out_other, preferred_element_type=f32)
    proj4 = projected.reshape(owned_rows, 4, head_dim)
    activated = jax.nn.silu(proj4).astype(bf16)
    gating = activated[:, 0]
    values = activated[:, 1]
    queries = activated[:, 2]
    keys_head = activated[:, 3]
    scores = jnp.einsum("md,nd->mn", queries, keys_head, preferred_element_type=f32)
    allowed = (compact_slot[:, None] == compact_slot[None, :]) & (
        compact_ids[:, None] >= compact_ids[None, :]
    )
    weights = jnp.where(allowed, jax.nn.silu(scores * score_scale) / MAXLEN, 0.0).astype(bf16)
    attended = jnp.einsum("mn,nd->md", weights, values, preferred_element_type=f32)
    inv_rms = lax.rsqrt(jnp.mean(attended * attended, axis=-1, keepdims=True) + norm_eps)
    normed = attended * inv_rms * head_gain
    gated = (normed * gating).astype(bf16)
    own_gated = lax.dynamic_slice_in_dim(gated, inner_start, col_width, 1)
    out_part = jnp.einsum("rc,ctk->trk", own_gated, own_out, preferred_element_type=f32)

    d_normed = down_grad * gating
    d_gating = down_grad * normed
    scaled = head_gain * d_normed
    d_attended = (
        inv_rms * scaled
        - attended * inv_rms**3 * jnp.mean(attended * scaled, axis=-1, keepdims=True)
    ).astype(bf16)
    d_weights = jnp.einsum("md,nd->mn", d_attended, values, preferred_element_type=f32)
    d_values = jnp.einsum("mn,md->nd", weights, d_attended, preferred_element_type=f32)
    d_scores = jnp.where(
        allowed, d_weights * silu_slope(scores * score_scale) * (score_scale / MAXLEN), 0.0
    ).astype(bf16)
    d_queries = jnp.einsum("mn,nd->md", d_scores, keys_head, preferred_element_type=f32)
    d_keys = jnp.einsum("mn,md->nd", d_scores, queries, preferred_element_type=f32)
    d_activated = jnp.stack([d_gating, d_values, d_queries, d_keys], axis=1)
    d_projected = (d_activated * silu_slope(proj4)).astype(bf16)
    own_grad = lax.dynamic_slice_in_dim(d_projected, inner_start, col_width, 2).reshape(
        owned_rows, 4 * col_width
    )
    grad_part = jnp.einsum("rn,tkn->trk", own_grad, own_proj, preferred_element_type=f32)
    both_sum = reduce_blocks(
        jnp.concatenate([sibling_sum(out_part.astype(bf16)), sibling_sum(grad_part.astype(bf16))], axis=2)
    )
    out_sum = both_sum[:, :col_width]
    grad_sum = both_sum[:, col_width:]
    mixed_out = (own_tokens.astype(f32) + out_sum).astype(bf16)
    token_rows = (own_cotan.astype(f32) + grad_sum).astype(bf16)

    def by_rows(term_mine, term_other):
        pair = jnp.stack([term_mine, term_other], axis=1)
        pair = jnp.where(core == 0, pair, pair[:, ::-1])
        return pair.reshape((D,) + term_mine.shape[2:])

    proj_term = by_rows(
        jnp.einsum("trc,rn->tcn", mine_tok, own_grad, preferred_element_type=f32),
        jnp.einsum("trc,rn->tcn", other_tok, own_grad, preferred_element_type=f32),
    )
    out_term = by_rows(
        jnp.einsum("trc,rd->tcd", mine_cot, own_gated, preferred_element_type=f32),
        jnp.einsum("trc,rd->tcd", other_cot, own_gated, preferred_element_type=f32),
    )
    terms = jnp.concatenate([proj_term, out_term], axis=1).astype(bf16)
    term_blocks = terms.reshape((dp_count, D // dp_count) + terms.shape[1:])
    term_sum = lax.dynamic_index_in_dim(term_blocks, dp_index, 0, keepdims=False).astype(f32)
    for k in range(1, dp_count):
        outgoing = lax.dynamic_index_in_dim(term_blocks, dp_index ^ k, 0, keepdims=False)
        partners = [(d, d ^ k) for d in range(dp_count)]
        term_sum = term_sum + lax.ppermute(outgoing, "dp", partners).astype(f32)
    proj_grad = term_sum[:, : 4 * col_width].reshape(-1, 4, col_width)
    out_grad = term_sum[:, 4 * col_width :].T

    back_src = jnp.minimum(recv_start[:, None] + places[None, :], owned_rows - 1)
    back_send = pick_rows(back_src.reshape(-1), token_rows).reshape(dp_count, MAXLEN, col_width)
    back_grads = exchange(back_send)
    back_grads = back_grads.reshape(dp_count * MAXLEN, col_width)
    load_ids = jnp.arange(load_rows, dtype=jnp.int32)
    seq_of = jnp.sum((load_ids[:, None] >= my_starts[None, :]).astype(jnp.int32), axis=1) - 1
    seq_pick = seq_of[:, None] == seq_ids[None, :]
    owner_of = jnp.sum(jnp.where(seq_pick, my_owners[None, :], 0), axis=1)
    start_of = jnp.sum(jnp.where(seq_pick, my_starts[None, :], 0), axis=1)
    back_ids = (owner_of ^ dp_index) * MAXLEN + jnp.minimum(load_ids - start_of, MAXLEN - 1)
    row_used = load_ids < jnp.sum(my_lengths)
    token_grad = pick_rows(jnp.where(row_used, back_ids, -1), back_grads)
    return (mixed_out, token_grad, proj_grad, out_grad)


def solution(mesh):
    in_specs = (P("dp", "tensor"), P("dp", "tensor"), P(), P(), P(), P(), P())
    out_specs = (P("dp", "tensor"), P("dp", "tensor"), P("dp", None, "tensor"), P("tensor", "dp"))
    return jax.shard_map(local, mesh=mesh, in_specs=in_specs, out_specs=out_specs, check_vma=False)
```

```python
import math

import jax
import jax.numpy as jnp
from jax import lax
from jax.sharding import PartitionSpec as P

D = 1024
H = 8
MAXLEN = 192


norm_eps = 1e-05


def silu_slope(argument):
    sigmoid_val = jax.nn.sigmoid(argument)
    return sigmoid_val * (1.0 + argument * (1.0 - sigmoid_val))


def exclusive_sum(counts):
    return jnp.cumsum(counts) - counts


def local(tokens, cotangent, lengths, owners, proj_weight, norm_gain, out_weight):
    f32 = jnp.float32
    bf16 = jnp.bfloat16
    dp_count = lax.axis_size("dp")
    tensor_count = lax.axis_size("tensor")
    dp_index = lax.axis_index("dp")
    tensor_index = lax.axis_index("tensor")
    col_width = tokens.shape[1]
    load_rows = tokens.shape[0]
    head_dim = D // H
    score_scale = 1.0 / math.sqrt(head_dim)
    owned_rows = dp_count * (9 * MAXLEN // 16)
    places = jnp.arange(MAXLEN, dtype=jnp.int32)
    peer_ids = jnp.arange(dp_count, dtype=jnp.int32)
    seq_ids = jnp.arange(lengths.shape[1], dtype=jnp.int32)

    my_lengths = lengths[dp_index]
    my_owners = owners[dp_index]
    my_starts = exclusive_sum(my_lengths)
    sent_to = my_owners[None, :] == peer_ids[:, None]
    send_start = jnp.sum(jnp.where(sent_to, my_starts[None, :], 0), axis=1)
    xor_peers = dp_index ^ peer_ids
    send_ids = jnp.minimum(jnp.take(send_start, xor_peers)[:, None] + places[None, :], load_rows - 1)
    def exchange(blocks):
        pieces = [blocks[0]]
        for k in range(1, dp_count):
            pieces.append(lax.ppermute(blocks[k], "dp", [(d, d ^ k) for d in range(dp_count)]))
        return jnp.stack(pieces)

    def pick_rows(row_ids, source):
        one_hot = (row_ids[:, None] == jnp.arange(source.shape[0], dtype=jnp.int32)[None, :]).astype(bf16)
        return jnp.dot(one_hot, source, preferred_element_type=f32).astype(bf16)

    flat_send = send_ids.reshape(-1)
    send_both = jnp.concatenate(
        [pick_rows(flat_send, tokens), pick_rows(flat_send, cotangent)], axis=1
    ).reshape(dp_count, MAXLEN, 2 * col_width)
    recv_both = exchange(send_both)

    half_count = tensor_count // 2
    core = tensor_index % 2

    def by_core(weight, axis):
        split = weight.reshape(weight.shape[:axis] + (half_count, 2) + weight.shape[axis + 1 :])
        return (
            lax.dynamic_index_in_dim(split, core, axis + 1, keepdims=False),
            lax.dynamic_index_in_dim(split, 1 - core, axis + 1, keepdims=False),
        )

    head_start = tensor_index * H // tensor_count * head_dim
    own_start = tensor_index * col_width
    inner_start = own_start - head_start
    head_proj = lax.dynamic_slice_in_dim(proj_weight, head_start, head_dim, 2).reshape(
        tensor_count, col_width, 4 * head_dim
    )
    own_proj = lax.dynamic_slice_in_dim(proj_weight, own_start, col_width, 2).reshape(
        tensor_count, col_width, 4 * col_width
    )
    head_out = lax.dynamic_slice_in_dim(out_weight, head_start, head_dim, 0).reshape(
        head_dim, tensor_count, col_width
    )
    head_gain = lax.dynamic_slice_in_dim(norm_gain, head_start, head_dim, 0)

    proj_mine, proj_other = by_core(head_proj, 0)
    out_mine, out_other = by_core(head_out, 1)
    own_out = lax.dynamic_slice_in_dim(out_weight, own_start, col_width, 0).reshape(
        col_width, tensor_count, col_width
    )
    weight_pack = (proj_mine, proj_other, out_mine, out_other, own_proj, own_out, head_gain)
    recv_both, weight_pack = lax.optimization_barrier((recv_both, weight_pack))
    proj_mine, proj_other, out_mine, out_other, own_proj, own_out, head_gain = weight_pack

    recv_len = jnp.sum(jnp.where(owners == dp_index, lengths, 0), axis=1)
    recv_start = exclusive_sum(recv_len)
    compact_ids = jnp.arange(owned_rows, dtype=jnp.int32)
    compact_slot = (
        jnp.sum((compact_ids[:, None] >= recv_start[None, :]).astype(jnp.int32), axis=1) - 1
    )
    slot_pick = compact_slot[:, None] == peer_ids[None, :]
    compact_start = jnp.sum(jnp.where(slot_pick, recv_start[None, :], 0), axis=1)
    gather_ids = (compact_slot ^ dp_index) * MAXLEN + compact_ids - compact_start
    own_both = pick_rows(gather_ids, recv_both.reshape(dp_count * MAXLEN, 2 * col_width))
    own_tokens = own_both[:, :col_width]
    own_cotan = own_both[:, col_width:]

    same_core = [[2 * z + c for z in range(half_count)] for c in range(2)]
    sibling = [(t, t ^ 1) for t in range(tensor_count)]
    mine = lax.all_gather(own_both, "tensor", axis=0, tiled=False, axis_index_groups=same_core)
    other = lax.ppermute(mine, "tensor", sibling)
    mine_tok, mine_cot = mine[..., :col_width], mine[..., col_width:]
    other_tok, other_cot = other[..., :col_width], other[..., col_width:]

    def sibling_sum(part):
        keep, send = by_core(part, 0)
        return (keep.astype(f32) + lax.ppermute(send, "tensor", sibling).astype(f32)).astype(bf16)

    def reduce_blocks(pair_sum):
        pieces = lax.all_to_all(pair_sum, "tensor", 0, 0, tiled=True, axis_index_groups=same_core)
        return jnp.sum(pieces.astype(f32), axis=0)

    projected = jnp.einsum(
        "trc,tcn->rn", mine_tok, proj_mine, preferred_element_type=f32
    ) + jnp.einsum("trc,tcn->rn", other_tok, proj_other, preferred_element_type=f32)
    down_grad = jnp.einsum(
        "trc,dtc->rd", mine_cot, out_mine, preferred_element_type=f32
    ) + jnp.einsum("trc,dtc->rd", other_cot, out_other, preferred_element_type=f32)
    proj4 = projected.reshape(owned_rows, 4, head_dim)
    activated = jax.nn.silu(proj4).astype(bf16)
    gating = activated[:, 0]
    values = activated[:, 1]
    queries = activated[:, 2]
    keys_head = activated[:, 3]
    scores = jnp.einsum("md,nd->mn", queries, keys_head, preferred_element_type=f32)
    allowed = (compact_slot[:, None] == compact_slot[None, :]) & (
        compact_ids[:, None] >= compact_ids[None, :]
    )
    weights = jnp.where(allowed, jax.nn.silu(scores * score_scale) / MAXLEN, 0.0).astype(bf16)
    attended = jnp.einsum("mn,nd->md", weights, values, preferred_element_type=f32)
    inv_rms = lax.rsqrt(jnp.mean(attended * attended, axis=-1, keepdims=True) + norm_eps)
    normed = attended * inv_rms * head_gain
    gated = (normed * gating).astype(bf16)
    own_gated = lax.dynamic_slice_in_dim(gated, inner_start, col_width, 1)
    out_part = jnp.einsum("rc,ctk->trk", own_gated, own_out, preferred_element_type=f32)

    d_normed = down_grad * gating
    d_gating = down_grad * normed
    scaled = head_gain * d_normed
    d_attended = (
        inv_rms * scaled
        - attended * inv_rms**3 * jnp.mean(attended * scaled, axis=-1, keepdims=True)
    ).astype(bf16)
    d_weights = jnp.einsum("md,nd->mn", d_attended, values, preferred_element_type=f32)
    d_values = jnp.einsum("mn,md->nd", weights, d_attended, preferred_element_type=f32)
    d_scores = jnp.where(
        allowed, d_weights * silu_slope(scores * score_scale) * (score_scale / MAXLEN), 0.0
    ).astype(bf16)
    d_queries = jnp.einsum("mn,nd->md", d_scores, keys_head, preferred_element_type=f32)
    d_keys = jnp.einsum("mn,md->nd", d_scores, queries, preferred_element_type=f32)
    d_activated = jnp.stack([d_gating, d_values, d_queries, d_keys], axis=1)
    d_projected = (d_activated * silu_slope(proj4)).astype(bf16)
    own_grad = lax.dynamic_slice_in_dim(d_projected, inner_start, col_width, 2).reshape(
        owned_rows, 4 * col_width
    )
    grad_part = jnp.einsum("rn,tkn->trk", own_grad, own_proj, preferred_element_type=f32)
    both_sum = reduce_blocks(
        jnp.concatenate([sibling_sum(out_part.astype(bf16)), sibling_sum(grad_part.astype(bf16))], axis=2)
    )
    out_sum = both_sum[:, :col_width]
    grad_sum = both_sum[:, col_width:]
    mixed_out = (own_tokens.astype(f32) + out_sum).astype(bf16)
    token_rows = (own_cotan.astype(f32) + grad_sum).astype(bf16)

    def by_rows(term_mine, term_other):
        pair = jnp.stack([term_mine, term_other], axis=1)
        pair = jnp.where(core == 0, pair, pair[:, ::-1])
        return pair.reshape((D,) + term_mine.shape[2:])

    proj_term = by_rows(
        jnp.einsum("trc,rn->tcn", mine_tok, own_grad, preferred_element_type=f32),
        jnp.einsum("trc,rn->tcn", other_tok, own_grad, preferred_element_type=f32),
    )
    out_term = by_rows(
        jnp.einsum("trc,rd->tcd", mine_cot, own_gated, preferred_element_type=f32),
        jnp.einsum("trc,rd->tcd", other_cot, own_gated, preferred_element_type=f32),
    )
    terms = jnp.concatenate([proj_term, out_term], axis=1).astype(bf16)
    term_blocks = terms.reshape((dp_count, D // dp_count) + terms.shape[1:])
    term_sum = lax.dynamic_index_in_dim(term_blocks, dp_index, 0, keepdims=False).astype(f32)
    for k in range(1, dp_count):
        outgoing = lax.dynamic_index_in_dim(term_blocks, dp_index ^ k, 0, keepdims=False)
        partners = [(d, d ^ k) for d in range(dp_count)]
        term_sum = term_sum + lax.ppermute(outgoing, "dp", partners).astype(f32)
    proj_grad = term_sum[:, : 4 * col_width].reshape(-1, 4, col_width)
    out_grad = term_sum[:, 4 * col_width :].T

    back_src = jnp.minimum(
        jnp.take(recv_start, xor_peers)[:, None] + places[None, :], owned_rows - 1
    )
    back_send = pick_rows(back_src.reshape(-1), token_rows).reshape(dp_count, MAXLEN, col_width)
    back_grads = exchange(back_send)
    back_grads = back_grads.reshape(dp_count * MAXLEN, col_width)
    load_ids = jnp.arange(load_rows, dtype=jnp.int32)
    seq_of = jnp.sum((load_ids[:, None] >= my_starts[None, :]).astype(jnp.int32), axis=1) - 1
    seq_pick = seq_of[:, None] == seq_ids[None, :]
    owner_of = jnp.sum(jnp.where(seq_pick, my_owners[None, :], 0), axis=1)
    start_of = jnp.sum(jnp.where(seq_pick, my_starts[None, :], 0), axis=1)
    back_ids = (owner_of ^ dp_index) * MAXLEN + jnp.minimum(load_ids - start_of, MAXLEN - 1)
    row_used = load_ids < jnp.sum(my_lengths)
    token_grad = pick_rows(jnp.where(row_used, back_ids, -1), back_grads)
    return (mixed_out, token_grad, proj_grad, out_grad)


def solution(mesh):
    in_specs = (P("dp", "tensor"), P("dp", "tensor"), P(), P(), P(), P(), P())
    out_specs = (P("dp", "tensor"), P("dp", "tensor"), P("dp", None, "tensor"), P("tensor", "dp"))
    return jax.shard_map(local, mesh=mesh, in_specs=in_specs, out_specs=out_specs, check_vma=False)
```

```python
import math

import jax
import jax.numpy as jnp
from jax import lax
from jax.sharding import PartitionSpec as P

D = 1024
H = 8
MAXLEN = 192


norm_eps = 1e-05


def silu_slope(argument):
    sigmoid_val = jax.nn.sigmoid(argument)
    return sigmoid_val * (1.0 + argument * (1.0 - sigmoid_val))


def exclusive_sum(counts):
    return jnp.cumsum(counts) - counts


def local(tokens, cotangent, lengths, owners, proj_weight, norm_gain, out_weight):
    f32 = jnp.float32
    bf16 = jnp.bfloat16
    dp_count = lax.axis_size("dp")
    tensor_count = lax.axis_size("tensor")
    dp_index = lax.axis_index("dp")
    tensor_index = lax.axis_index("tensor")
    col_width = tokens.shape[1]
    load_rows = tokens.shape[0]
    head_dim = D // H
    score_scale = 1.0 / math.sqrt(head_dim)
    owned_rows = dp_count * (9 * MAXLEN // 16)
    places = jnp.arange(MAXLEN, dtype=jnp.int32)
    peer_ids = jnp.arange(dp_count, dtype=jnp.int32)
    seq_ids = jnp.arange(lengths.shape[1], dtype=jnp.int32)

    my_lengths = lengths[dp_index]
    my_owners = owners[dp_index]
    my_starts = exclusive_sum(my_lengths)
    sent_to = my_owners[None, :] == peer_ids[:, None]
    send_start = jnp.sum(jnp.where(sent_to, my_starts[None, :], 0), axis=1)
    send_ids = jnp.minimum(send_start[:, None] + places[None, :], load_rows - 1)
    def exchange(blocks):
        pieces = [lax.dynamic_index_in_dim(blocks, dp_index, 0, keepdims=False)]
        for k in range(1, dp_count):
            outgoing = lax.dynamic_index_in_dim(blocks, dp_index ^ k, 0, keepdims=False)
            pieces.append(lax.ppermute(outgoing, "dp", [(d, d ^ k) for d in range(dp_count)]))
        return jnp.stack(pieces)

    def pick_rows(row_ids, source):
        one_hot = (row_ids[:, None] == jnp.arange(source.shape[0], dtype=jnp.int32)[None, :]).astype(bf16)
        return jnp.dot(one_hot, source, preferred_element_type=f32).astype(bf16)

    flat_send = send_ids.reshape(-1)
    send_both = jnp.concatenate(
        [pick_rows(flat_send, tokens), pick_rows(flat_send, cotangent)], axis=1
    ).reshape(dp_count, MAXLEN, 2 * col_width)
    recv_both = exchange(send_both)

    half_count = tensor_count // 2
    core = tensor_index % 2

    def by_core(weight, axis):
        split = weight.reshape(weight.shape[:axis] + (half_count, 2) + weight.shape[axis + 1 :])
        return (
            lax.dynamic_index_in_dim(split, core, axis + 1, keepdims=False),
            lax.dynamic_index_in_dim(split, 1 - core, axis + 1, keepdims=False),
        )

    head_start = tensor_index * H // tensor_count * head_dim
    own_start = tensor_index * col_width
    inner_start = own_start - head_start
    head_proj = lax.dynamic_slice_in_dim(proj_weight, head_start, head_dim, 2).reshape(
        tensor_count, col_width, 4 * head_dim
    )
    own_proj = lax.dynamic_slice_in_dim(proj_weight, own_start, col_width, 2).reshape(
        tensor_count, col_width, 4 * col_width
    )
    head_out = lax.dynamic_slice_in_dim(out_weight, head_start, head_dim, 0).reshape(
        head_dim, tensor_count, col_width
    )
    head_gain = lax.dynamic_slice_in_dim(norm_gain, head_start, head_dim, 0)

    proj_mine, proj_other = by_core(head_proj, 0)
    out_mine, out_other = by_core(head_out, 1)
    own_out = lax.dynamic_slice_in_dim(out_weight, own_start, col_width, 0).reshape(
        col_width, tensor_count, col_width
    )
    weight_pack = (proj_mine, proj_other, out_mine, out_other, own_proj, own_out, head_gain)
    recv_both, weight_pack = lax.optimization_barrier((recv_both, weight_pack))
    proj_mine, proj_other, out_mine, out_other, own_proj, own_out, head_gain = weight_pack

    recv_len = jnp.sum(jnp.where(owners == dp_index, lengths, 0), axis=1)
    recv_start = exclusive_sum(recv_len)
    compact_ids = jnp.arange(owned_rows, dtype=jnp.int32)
    compact_slot = (
        jnp.sum((compact_ids[:, None] >= recv_start[None, :]).astype(jnp.int32), axis=1) - 1
    )
    slot_pick = compact_slot[:, None] == peer_ids[None, :]
    compact_start = jnp.sum(jnp.where(slot_pick, recv_start[None, :], 0), axis=1)
    gather_ids = (compact_slot ^ dp_index) * MAXLEN + compact_ids - compact_start
    own_both = pick_rows(gather_ids, recv_both.reshape(dp_count * MAXLEN, 2 * col_width))
    own_tokens = own_both[:, :col_width]
    own_cotan = own_both[:, col_width:]

    same_core = [[2 * z + c for z in range(half_count)] for c in range(2)]
    sibling = [(t, t ^ 1) for t in range(tensor_count)]
    mine = lax.all_gather(own_both, "tensor", axis=0, tiled=False, axis_index_groups=same_core)
    other = lax.ppermute(mine, "tensor", sibling)
    mine_tok, mine_cot = mine[..., :col_width], mine[..., col_width:]
    other_tok, other_cot = other[..., :col_width], other[..., col_width:]

    def sibling_sum(part):
        keep, send = by_core(part, 0)
        return (keep.astype(f32) + lax.ppermute(send, "tensor", sibling).astype(f32)).astype(bf16)

    def reduce_by_permutes(pair_sum):
        chip = tensor_index // 2
        total = lax.dynamic_index_in_dim(pair_sum, chip, 0, keepdims=False).astype(f32)
        for k in range(1, half_count):
            outgoing = lax.dynamic_index_in_dim(pair_sum, chip ^ k, 0, keepdims=False)
            partners = [(t, ((t // 2) ^ k) * 2 + t % 2) for t in range(tensor_count)]
            total = total + lax.ppermute(outgoing, "tensor", partners).astype(f32)
        return total

    def reduce_blocks(pair_sum):
        pieces = lax.all_to_all(pair_sum, "tensor", 0, 0, tiled=True, axis_index_groups=same_core)
        return jnp.sum(pieces.astype(f32), axis=0)

    projected = jnp.einsum(
        "trc,tcn->rn", mine_tok, proj_mine, preferred_element_type=f32
    ) + jnp.einsum("trc,tcn->rn", other_tok, proj_other, preferred_element_type=f32)
    down_grad = jnp.einsum(
        "trc,dtc->rd", mine_cot, out_mine, preferred_element_type=f32
    ) + jnp.einsum("trc,dtc->rd", other_cot, out_other, preferred_element_type=f32)
    proj4 = projected.reshape(owned_rows, 4, head_dim)
    activated = jax.nn.silu(proj4).astype(bf16)
    gating = activated[:, 0]
    values = activated[:, 1]
    queries = activated[:, 2]
    keys_head = activated[:, 3]
    scores = jnp.einsum("md,nd->mn", queries, keys_head, preferred_element_type=f32)
    allowed = (compact_slot[:, None] == compact_slot[None, :]) & (
        compact_ids[:, None] >= compact_ids[None, :]
    )
    weights = jnp.where(allowed, jax.nn.silu(scores * score_scale) / MAXLEN, 0.0).astype(bf16)
    attended = jnp.einsum("mn,nd->md", weights, values, preferred_element_type=f32)
    inv_rms = lax.rsqrt(jnp.mean(attended * attended, axis=-1, keepdims=True) + norm_eps)
    normed = attended * inv_rms * head_gain
    gated = (normed * gating).astype(bf16)
    own_gated = lax.dynamic_slice_in_dim(gated, inner_start, col_width, 1)
    out_part = jnp.einsum("rc,ctk->trk", own_gated, own_out, preferred_element_type=f32)

    d_normed = down_grad * gating
    d_gating = down_grad * normed
    scaled = head_gain * d_normed
    d_attended = (
        inv_rms * scaled
        - attended * inv_rms**3 * jnp.mean(attended * scaled, axis=-1, keepdims=True)
    ).astype(bf16)
    d_weights = jnp.einsum("md,nd->mn", d_attended, values, preferred_element_type=f32)
    d_values = jnp.einsum("mn,md->nd", weights, d_attended, preferred_element_type=f32)
    d_scores = jnp.where(
        allowed, d_weights * silu_slope(scores * score_scale) * (score_scale / MAXLEN), 0.0
    ).astype(bf16)
    d_queries = jnp.einsum("mn,nd->md", d_scores, keys_head, preferred_element_type=f32)
    d_keys = jnp.einsum("mn,md->nd", d_scores, queries, preferred_element_type=f32)
    d_activated = jnp.stack([d_gating, d_values, d_queries, d_keys], axis=1)
    d_projected = (d_activated * silu_slope(proj4)).astype(bf16)
    own_grad = lax.dynamic_slice_in_dim(d_projected, inner_start, col_width, 2).reshape(
        owned_rows, 4 * col_width
    )
    grad_part = jnp.einsum("rn,tkn->trk", own_grad, own_proj, preferred_element_type=f32)
    out_sum = reduce_by_permutes(sibling_sum(out_part.astype(bf16)))
    grad_sum = reduce_blocks(sibling_sum(grad_part.astype(bf16)))
    mixed_out = (own_tokens.astype(f32) + out_sum).astype(bf16)
    token_rows = (own_cotan.astype(f32) + grad_sum).astype(bf16)

    def by_rows(term_mine, term_other):
        pair = jnp.stack([term_mine, term_other], axis=1)
        pair = jnp.where(core == 0, pair, pair[:, ::-1])
        return pair.reshape((D,) + term_mine.shape[2:])

    proj_term = by_rows(
        jnp.einsum("trc,rn->tcn", mine_tok, own_grad, preferred_element_type=f32),
        jnp.einsum("trc,rn->tcn", other_tok, own_grad, preferred_element_type=f32),
    )
    out_term = by_rows(
        jnp.einsum("trc,rd->tcd", mine_cot, own_gated, preferred_element_type=f32),
        jnp.einsum("trc,rd->tcd", other_cot, own_gated, preferred_element_type=f32),
    )
    terms = jnp.concatenate([proj_term, out_term], axis=1).astype(bf16)
    term_blocks = terms.reshape((dp_count, D // dp_count) + terms.shape[1:])
    term_sum = lax.dynamic_index_in_dim(term_blocks, dp_index, 0, keepdims=False).astype(f32)
    for k in range(1, dp_count):
        outgoing = lax.dynamic_index_in_dim(term_blocks, dp_index ^ k, 0, keepdims=False)
        partners = [(d, d ^ k) for d in range(dp_count)]
        term_sum = term_sum + lax.ppermute(outgoing, "dp", partners).astype(f32)
    proj_grad = term_sum[:, : 4 * col_width].reshape(-1, 4, col_width)
    out_grad = term_sum[:, 4 * col_width :].T

    back_src = jnp.minimum(recv_start[:, None] + places[None, :], owned_rows - 1)
    back_send = pick_rows(back_src.reshape(-1), token_rows).reshape(dp_count, MAXLEN, col_width)
    back_grads = exchange(back_send)
    back_grads = back_grads.reshape(dp_count * MAXLEN, col_width)
    load_ids = jnp.arange(load_rows, dtype=jnp.int32)
    seq_of = jnp.sum((load_ids[:, None] >= my_starts[None, :]).astype(jnp.int32), axis=1) - 1
    seq_pick = seq_of[:, None] == seq_ids[None, :]
    owner_of = jnp.sum(jnp.where(seq_pick, my_owners[None, :], 0), axis=1)
    start_of = jnp.sum(jnp.where(seq_pick, my_starts[None, :], 0), axis=1)
    back_ids = (owner_of ^ dp_index) * MAXLEN + jnp.minimum(load_ids - start_of, MAXLEN - 1)
    row_used = load_ids < jnp.sum(my_lengths)
    token_grad = pick_rows(jnp.where(row_used, back_ids, -1), back_grads)
    return (mixed_out, token_grad, proj_grad, out_grad)


def solution(mesh):
    in_specs = (P("dp", "tensor"), P("dp", "tensor"), P(), P(), P(), P(), P())
    out_specs = (P("dp", "tensor"), P("dp", "tensor"), P("dp", None, "tensor"), P("tensor", "dp"))
    return jax.shard_map(local, mesh=mesh, in_specs=in_specs, out_specs=out_specs, check_vma=False)
```

```python
import math

import jax
import jax.numpy as jnp
from jax import lax
from jax.sharding import PartitionSpec as P

D = 1024
H = 8
MAXLEN = 192


norm_eps = 1e-05


def silu_slope(argument):
    sigmoid_val = jax.nn.sigmoid(argument)
    return sigmoid_val * (1.0 + argument * (1.0 - sigmoid_val))


def exclusive_sum(counts):
    return jnp.cumsum(counts) - counts


def local(tokens, cotangent, lengths, owners, proj_weight, norm_gain, out_weight):
    f32 = jnp.float32
    bf16 = jnp.bfloat16
    dp_count = lax.axis_size("dp")
    tensor_count = lax.axis_size("tensor")
    dp_index = lax.axis_index("dp")
    tensor_index = lax.axis_index("tensor")
    col_width = tokens.shape[1]
    load_rows = tokens.shape[0]
    head_dim = D // H
    score_scale = 1.0 / math.sqrt(head_dim)
    owned_rows = dp_count * (9 * MAXLEN // 16)
    places = jnp.arange(MAXLEN, dtype=jnp.int32)
    peer_ids = jnp.arange(dp_count, dtype=jnp.int32)
    seq_ids = jnp.arange(lengths.shape[1], dtype=jnp.int32)

    my_lengths = lengths[dp_index]
    my_owners = owners[dp_index]
    my_starts = exclusive_sum(my_lengths)
    sent_to = my_owners[None, :] == peer_ids[:, None]
    send_start = jnp.sum(jnp.where(sent_to, my_starts[None, :], 0), axis=1)
    send_ids = jnp.minimum(send_start[:, None] + places[None, :], load_rows - 1)
    def exchange(blocks):
        pieces = [lax.dynamic_index_in_dim(blocks, dp_index, 0, keepdims=False)]
        for k in range(1, dp_count):
            outgoing = lax.dynamic_index_in_dim(blocks, dp_index ^ k, 0, keepdims=False)
            pieces.append(lax.ppermute(outgoing, "dp", [(d, d ^ k) for d in range(dp_count)]))
        return jnp.stack(pieces)

    def pick_rows(row_ids, source):
        one_hot = (row_ids[:, None] == jnp.arange(source.shape[0], dtype=jnp.int32)[None, :]).astype(bf16)
        return jnp.dot(one_hot, source, preferred_element_type=f32).astype(bf16)

    flat_send = send_ids.reshape(-1)
    send_both = pick_rows(flat_send, jnp.concatenate([tokens, cotangent], axis=1)).reshape(
        dp_count, MAXLEN, 2 * col_width
    )
    recv_both = exchange(send_both)

    half_count = tensor_count // 2
    core = tensor_index % 2

    def by_core(weight, axis):
        split = weight.reshape(weight.shape[:axis] + (half_count, 2) + weight.shape[axis + 1 :])
        return (
            lax.dynamic_index_in_dim(split, core, axis + 1, keepdims=False),
            lax.dynamic_index_in_dim(split, 1 - core, axis + 1, keepdims=False),
        )

    head_start = tensor_index * H // tensor_count * head_dim
    own_start = tensor_index * col_width
    inner_start = own_start - head_start
    head_proj = lax.dynamic_slice_in_dim(proj_weight, head_start, head_dim, 2).reshape(
        tensor_count, col_width, 4 * head_dim
    )
    own_proj = lax.dynamic_slice_in_dim(proj_weight, own_start, col_width, 2).reshape(
        tensor_count, col_width, 4 * col_width
    )
    head_out = lax.dynamic_slice_in_dim(out_weight, head_start, head_dim, 0).reshape(
        head_dim, tensor_count, col_width
    )
    head_gain = lax.dynamic_slice_in_dim(norm_gain, head_start, head_dim, 0)

    proj_mine, proj_other = by_core(head_proj, 0)
    out_mine, out_other = by_core(head_out, 1)
    own_out = lax.dynamic_slice_in_dim(out_weight, own_start, col_width, 0).reshape(
        col_width, tensor_count, col_width
    )
    weight_pack = (proj_mine, proj_other, out_mine, out_other, own_proj, own_out, head_gain)
    recv_both, weight_pack = lax.optimization_barrier((recv_both, weight_pack))
    proj_mine, proj_other, out_mine, out_other, own_proj, own_out, head_gain = weight_pack

    recv_len = jnp.sum(jnp.where(owners == dp_index, lengths, 0), axis=1)
    recv_start = exclusive_sum(recv_len)
    compact_ids = jnp.arange(owned_rows, dtype=jnp.int32)
    compact_slot = (
        jnp.sum((compact_ids[:, None] >= recv_start[None, :]).astype(jnp.int32), axis=1) - 1
    )
    slot_pick = compact_slot[:, None] == peer_ids[None, :]
    compact_start = jnp.sum(jnp.where(slot_pick, recv_start[None, :], 0), axis=1)
    gather_ids = (compact_slot ^ dp_index) * MAXLEN + compact_ids - compact_start
    own_both = pick_rows(gather_ids, recv_both.reshape(dp_count * MAXLEN, 2 * col_width))
    own_tokens = own_both[:, :col_width]
    own_cotan = own_both[:, col_width:]

    same_core = [[2 * z + c for z in range(half_count)] for c in range(2)]
    sibling = [(t, t ^ 1) for t in range(tensor_count)]
    mine = lax.all_gather(own_both, "tensor", axis=0, tiled=False, axis_index_groups=same_core)
    other = lax.ppermute(mine, "tensor", sibling)
    mine_tok, mine_cot = mine[..., :col_width], mine[..., col_width:]
    other_tok, other_cot = other[..., :col_width], other[..., col_width:]

    def sibling_sum(part):
        keep, send = by_core(part, 0)
        return (keep.astype(f32) + lax.ppermute(send, "tensor", sibling).astype(f32)).astype(bf16)

    def reduce_blocks(pair_sum):
        pieces = lax.all_to_all(pair_sum, "tensor", 0, 0, tiled=True, axis_index_groups=same_core)
        return jnp.sum(pieces.astype(f32), axis=0)

    projected = jnp.einsum(
        "trc,tcn->rn", mine_tok, proj_mine, preferred_element_type=f32
    ) + jnp.einsum("trc,tcn->rn", other_tok, proj_other, preferred_element_type=f32)
    down_grad = jnp.einsum(
        "trc,dtc->rd", mine_cot, out_mine, preferred_element_type=f32
    ) + jnp.einsum("trc,dtc->rd", other_cot, out_other, preferred_element_type=f32)
    proj4 = projected.reshape(owned_rows, 4, head_dim)
    activated = jax.nn.silu(proj4).astype(bf16)
    gating = activated[:, 0]
    values = activated[:, 1]
    queries = activated[:, 2]
    keys_head = activated[:, 3]
    scores = jnp.einsum("md,nd->mn", queries, keys_head, preferred_element_type=f32)
    allowed = (compact_slot[:, None] == compact_slot[None, :]) & (
        compact_ids[:, None] >= compact_ids[None, :]
    )
    weights = jnp.where(allowed, jax.nn.silu(scores * score_scale) / MAXLEN, 0.0).astype(bf16)
    attended = jnp.einsum("mn,nd->md", weights, values, preferred_element_type=f32)
    inv_rms = lax.rsqrt(jnp.mean(attended * attended, axis=-1, keepdims=True) + norm_eps)
    normed = attended * inv_rms * head_gain
    gated = (normed * gating).astype(bf16)
    own_gated = lax.dynamic_slice_in_dim(gated, inner_start, col_width, 1)
    out_part = jnp.einsum("rc,ctk->trk", own_gated, own_out, preferred_element_type=f32)

    d_normed = down_grad * gating
    d_gating = down_grad * normed
    scaled = head_gain * d_normed
    d_attended = (
        inv_rms * scaled
        - attended * inv_rms**3 * jnp.mean(attended * scaled, axis=-1, keepdims=True)
    ).astype(bf16)
    d_weights = jnp.einsum("md,nd->mn", d_attended, values, preferred_element_type=f32)
    d_values = jnp.einsum("mn,md->nd", weights, d_attended, preferred_element_type=f32)
    d_scores = jnp.where(
        allowed, d_weights * silu_slope(scores * score_scale) * (score_scale / MAXLEN), 0.0
    ).astype(bf16)
    d_queries = jnp.einsum("mn,nd->md", d_scores, keys_head, preferred_element_type=f32)
    d_keys = jnp.einsum("mn,md->nd", d_scores, queries, preferred_element_type=f32)
    d_activated = jnp.stack([d_gating, d_values, d_queries, d_keys], axis=1)
    d_projected = (d_activated * silu_slope(proj4)).astype(bf16)
    own_grad = lax.dynamic_slice_in_dim(d_projected, inner_start, col_width, 2).reshape(
        owned_rows, 4 * col_width
    )
    grad_part = jnp.einsum("rn,tkn->trk", own_grad, own_proj, preferred_element_type=f32)
    both_sum = reduce_blocks(
        jnp.concatenate([sibling_sum(out_part.astype(bf16)), sibling_sum(grad_part.astype(bf16))], axis=2)
    )
    out_sum = both_sum[:, :col_width]
    grad_sum = both_sum[:, col_width:]
    mixed_out = (own_tokens.astype(f32) + out_sum).astype(bf16)
    token_rows = (own_cotan.astype(f32) + grad_sum).astype(bf16)

    def by_rows(term_mine, term_other):
        pair = jnp.stack([term_mine, term_other], axis=1)
        pair = jnp.where(core == 0, pair, pair[:, ::-1])
        return pair.reshape((D,) + term_mine.shape[2:])

    proj_term = by_rows(
        jnp.einsum("trc,rn->tcn", mine_tok, own_grad, preferred_element_type=f32),
        jnp.einsum("trc,rn->tcn", other_tok, own_grad, preferred_element_type=f32),
    )
    out_term = by_rows(
        jnp.einsum("trc,rd->tcd", mine_cot, own_gated, preferred_element_type=f32),
        jnp.einsum("trc,rd->tcd", other_cot, own_gated, preferred_element_type=f32),
    )
    terms = jnp.concatenate([proj_term, out_term], axis=1).astype(bf16)
    term_blocks = terms.reshape((dp_count, D // dp_count) + terms.shape[1:])
    term_sum = lax.dynamic_index_in_dim(term_blocks, dp_index, 0, keepdims=False).astype(f32)
    for k in range(1, dp_count):
        outgoing = lax.dynamic_index_in_dim(term_blocks, dp_index ^ k, 0, keepdims=False)
        partners = [(d, d ^ k) for d in range(dp_count)]
        term_sum = term_sum + lax.ppermute(outgoing, "dp", partners).astype(f32)
    proj_grad = term_sum[:, : 4 * col_width].reshape(-1, 4, col_width)
    out_grad = term_sum[:, 4 * col_width :].T

    back_src = jnp.minimum(recv_start[:, None] + places[None, :], owned_rows - 1)
    back_send = pick_rows(back_src.reshape(-1), token_rows).reshape(dp_count, MAXLEN, col_width)
    back_grads = exchange(back_send)
    back_grads = back_grads.reshape(dp_count * MAXLEN, col_width)
    load_ids = jnp.arange(load_rows, dtype=jnp.int32)
    seq_of = jnp.sum((load_ids[:, None] >= my_starts[None, :]).astype(jnp.int32), axis=1) - 1
    seq_pick = seq_of[:, None] == seq_ids[None, :]
    owner_of = jnp.sum(jnp.where(seq_pick, my_owners[None, :], 0), axis=1)
    start_of = jnp.sum(jnp.where(seq_pick, my_starts[None, :], 0), axis=1)
    back_ids = (owner_of ^ dp_index) * MAXLEN + jnp.minimum(load_ids - start_of, MAXLEN - 1)
    row_used = load_ids < jnp.sum(my_lengths)
    token_grad = pick_rows(jnp.where(row_used, back_ids, -1), back_grads)
    return (mixed_out, token_grad, proj_grad, out_grad)


def solution(mesh):
    in_specs = (P("dp", "tensor"), P("dp", "tensor"), P(), P(), P(), P(), P())
    out_specs = (P("dp", "tensor"), P("dp", "tensor"), P("dp", None, "tensor"), P("tensor", "dp"))
    return jax.shard_map(local, mesh=mesh, in_specs=in_specs, out_specs=out_specs, check_vma=False)
```

```python
import math

import jax
import jax.numpy as jnp
from jax import lax
from jax.sharding import PartitionSpec as P

D = 1024
H = 8
MAXLEN = 192


norm_eps = 1e-05


def silu_slope(argument):
    sigmoid_val = jax.nn.sigmoid(argument)
    return sigmoid_val * (1.0 + argument * (1.0 - sigmoid_val))


def exclusive_sum(counts):
    return jnp.cumsum(counts) - counts


def local(tokens, cotangent, lengths, owners, proj_weight, norm_gain, out_weight):
    f32 = jnp.float32
    bf16 = jnp.bfloat16
    dp_count = lax.axis_size("dp")
    tensor_count = lax.axis_size("tensor")
    dp_index = lax.axis_index("dp")
    tensor_index = lax.axis_index("tensor")
    col_width = tokens.shape[1]
    load_rows = tokens.shape[0]
    head_dim = D // H
    score_scale = 1.0 / math.sqrt(head_dim)
    owned_rows = dp_count * (9 * MAXLEN // 16)
    places = jnp.arange(MAXLEN, dtype=jnp.int32)
    peer_ids = jnp.arange(dp_count, dtype=jnp.int32)
    seq_ids = jnp.arange(lengths.shape[1], dtype=jnp.int32)

    my_lengths = lengths[dp_index]
    my_owners = owners[dp_index]
    my_starts = exclusive_sum(my_lengths)
    sent_to = my_owners[None, :] == peer_ids[:, None]
    send_start = jnp.sum(jnp.where(sent_to, my_starts[None, :], 0), axis=1)
    send_ids = jnp.minimum(send_start[:, None] + places[None, :], load_rows - 1)
    def exchange(blocks):
        pieces = [lax.dynamic_index_in_dim(blocks, dp_index, 0, keepdims=False)]
        for k in range(1, dp_count):
            outgoing = lax.dynamic_index_in_dim(blocks, dp_index ^ k, 0, keepdims=False)
            pieces.append(lax.ppermute(outgoing, "dp", [(d, d ^ k) for d in range(dp_count)]))
        return pieces

    def pick_from_pieces(row_ids, pieces):
        rows = pieces[0].shape[0]
        total = None
        for k, piece in enumerate(pieces):
            span = k * rows + jnp.arange(rows, dtype=jnp.int32)
            one_hot = (row_ids[:, None] == span[None, :]).astype(bf16)
            term = jnp.dot(one_hot, piece, preferred_element_type=f32)
            total = term if total is None else total + term
        return total.astype(bf16)

    def pick_rows(row_ids, source):
        one_hot = (row_ids[:, None] == jnp.arange(source.shape[0], dtype=jnp.int32)[None, :]).astype(bf16)
        return jnp.dot(one_hot, source, preferred_element_type=f32).astype(bf16)

    flat_send = send_ids.reshape(-1)
    send_both = pick_rows(flat_send, jnp.concatenate([tokens, cotangent], axis=1)).reshape(
        dp_count, MAXLEN, 2 * col_width
    )
    recv_both = exchange(send_both)

    half_count = tensor_count // 2
    core = tensor_index % 2

    def by_core(weight, axis):
        split = weight.reshape(weight.shape[:axis] + (half_count, 2) + weight.shape[axis + 1 :])
        return (
            lax.dynamic_index_in_dim(split, core, axis + 1, keepdims=False),
            lax.dynamic_index_in_dim(split, 1 - core, axis + 1, keepdims=False),
        )

    head_start = tensor_index * H // tensor_count * head_dim
    own_start = tensor_index * col_width
    inner_start = own_start - head_start
    head_proj = lax.dynamic_slice_in_dim(proj_weight, head_start, head_dim, 2).reshape(
        tensor_count, col_width, 4 * head_dim
    )
    own_proj = lax.dynamic_slice_in_dim(proj_weight, own_start, col_width, 2).reshape(
        tensor_count, col_width, 4 * col_width
    )
    head_out = lax.dynamic_slice_in_dim(out_weight, head_start, head_dim, 0).reshape(
        head_dim, tensor_count, col_width
    )
    head_gain = lax.dynamic_slice_in_dim(norm_gain, head_start, head_dim, 0)

    proj_mine, proj_other = by_core(head_proj, 0)
    out_mine, out_other = by_core(head_out, 1)
    own_out = lax.dynamic_slice_in_dim(out_weight, own_start, col_width, 0).reshape(
        col_width, tensor_count, col_width
    )
    weight_pack = (proj_mine, proj_other, out_mine, out_other, own_proj, own_out, head_gain)
    recv_both, weight_pack = lax.optimization_barrier((recv_both, weight_pack))
    proj_mine, proj_other, out_mine, out_other, own_proj, own_out, head_gain = weight_pack

    recv_len = jnp.sum(jnp.where(owners == dp_index, lengths, 0), axis=1)
    recv_start = exclusive_sum(recv_len)
    compact_ids = jnp.arange(owned_rows, dtype=jnp.int32)
    compact_slot = (
        jnp.sum((compact_ids[:, None] >= recv_start[None, :]).astype(jnp.int32), axis=1) - 1
    )
    slot_pick = compact_slot[:, None] == peer_ids[None, :]
    compact_start = jnp.sum(jnp.where(slot_pick, recv_start[None, :], 0), axis=1)
    gather_ids = (compact_slot ^ dp_index) * MAXLEN + compact_ids - compact_start
    own_both = pick_from_pieces(gather_ids, recv_both)
    own_tokens = own_both[:, :col_width]
    own_cotan = own_both[:, col_width:]

    same_core = [[2 * z + c for z in range(half_count)] for c in range(2)]
    sibling = [(t, t ^ 1) for t in range(tensor_count)]
    mine = lax.all_gather(own_both, "tensor", axis=0, tiled=False, axis_index_groups=same_core)
    other = lax.ppermute(mine, "tensor", sibling)
    mine_tok, mine_cot = mine[..., :col_width], mine[..., col_width:]
    other_tok, other_cot = other[..., :col_width], other[..., col_width:]

    def sibling_sum(part):
        keep, send = by_core(part, 0)
        return (keep.astype(f32) + lax.ppermute(send, "tensor", sibling).astype(f32)).astype(bf16)

    def reduce_blocks(pair_sum):
        pieces = lax.all_to_all(pair_sum, "tensor", 0, 0, tiled=True, axis_index_groups=same_core)
        return jnp.sum(pieces.astype(f32), axis=0)

    projected = jnp.einsum(
        "trc,tcn->rn", mine_tok, proj_mine, preferred_element_type=f32
    ) + jnp.einsum("trc,tcn->rn", other_tok, proj_other, preferred_element_type=f32)
    down_grad = jnp.einsum(
        "trc,dtc->rd", mine_cot, out_mine, preferred_element_type=f32
    ) + jnp.einsum("trc,dtc->rd", other_cot, out_other, preferred_element_type=f32)
    proj4 = projected.reshape(owned_rows, 4, head_dim)
    activated = jax.nn.silu(proj4).astype(bf16)
    gating = activated[:, 0]
    values = activated[:, 1]
    queries = activated[:, 2]
    keys_head = activated[:, 3]
    scores = jnp.einsum("md,nd->mn", queries, keys_head, preferred_element_type=f32)
    allowed = (compact_slot[:, None] == compact_slot[None, :]) & (
        compact_ids[:, None] >= compact_ids[None, :]
    )
    weights = jnp.where(allowed, jax.nn.silu(scores * score_scale) / MAXLEN, 0.0).astype(bf16)
    attended = jnp.einsum("mn,nd->md", weights, values, preferred_element_type=f32)
    inv_rms = lax.rsqrt(jnp.mean(attended * attended, axis=-1, keepdims=True) + norm_eps)
    normed = attended * inv_rms * head_gain
    gated = (normed * gating).astype(bf16)
    own_gated = lax.dynamic_slice_in_dim(gated, inner_start, col_width, 1)
    out_part = jnp.einsum("rc,ctk->trk", own_gated, own_out, preferred_element_type=f32)

    d_normed = down_grad * gating
    d_gating = down_grad * normed
    scaled = head_gain * d_normed
    d_attended = (
        inv_rms * scaled
        - attended * inv_rms**3 * jnp.mean(attended * scaled, axis=-1, keepdims=True)
    ).astype(bf16)
    d_weights = jnp.einsum("md,nd->mn", d_attended, values, preferred_element_type=f32)
    d_values = jnp.einsum("mn,md->nd", weights, d_attended, preferred_element_type=f32)
    d_scores = jnp.where(
        allowed, d_weights * silu_slope(scores * score_scale) * (score_scale / MAXLEN), 0.0
    ).astype(bf16)
    d_queries = jnp.einsum("mn,nd->md", d_scores, keys_head, preferred_element_type=f32)
    d_keys = jnp.einsum("mn,md->nd", d_scores, queries, preferred_element_type=f32)
    d_activated = jnp.stack([d_gating, d_values, d_queries, d_keys], axis=1)
    d_projected = (d_activated * silu_slope(proj4)).astype(bf16)
    own_grad = lax.dynamic_slice_in_dim(d_projected, inner_start, col_width, 2).reshape(
        owned_rows, 4 * col_width
    )
    grad_part = jnp.einsum("rn,tkn->trk", own_grad, own_proj, preferred_element_type=f32)
    both_sum = reduce_blocks(
        jnp.concatenate([sibling_sum(out_part.astype(bf16)), sibling_sum(grad_part.astype(bf16))], axis=2)
    )
    out_sum = both_sum[:, :col_width]
    grad_sum = both_sum[:, col_width:]
    mixed_out = (own_tokens.astype(f32) + out_sum).astype(bf16)
    token_rows = (own_cotan.astype(f32) + grad_sum).astype(bf16)

    def by_rows(term_mine, term_other):
        pair = jnp.stack([term_mine, term_other], axis=1)
        pair = jnp.where(core == 0, pair, pair[:, ::-1])
        return pair.reshape((D,) + term_mine.shape[2:])

    proj_term = by_rows(
        jnp.einsum("trc,rn->tcn", mine_tok, own_grad, preferred_element_type=f32),
        jnp.einsum("trc,rn->tcn", other_tok, own_grad, preferred_element_type=f32),
    )
    out_term = by_rows(
        jnp.einsum("trc,rd->tcd", mine_cot, own_gated, preferred_element_type=f32),
        jnp.einsum("trc,rd->tcd", other_cot, own_gated, preferred_element_type=f32),
    )
    terms = jnp.concatenate([proj_term, out_term], axis=1).astype(bf16)
    term_blocks = terms.reshape((dp_count, D // dp_count) + terms.shape[1:])
    term_sum = lax.dynamic_index_in_dim(term_blocks, dp_index, 0, keepdims=False).astype(f32)
    for k in range(1, dp_count):
        outgoing = lax.dynamic_index_in_dim(term_blocks, dp_index ^ k, 0, keepdims=False)
        partners = [(d, d ^ k) for d in range(dp_count)]
        term_sum = term_sum + lax.ppermute(outgoing, "dp", partners).astype(f32)
    proj_grad = term_sum[:, : 4 * col_width].reshape(-1, 4, col_width)
    out_grad = term_sum[:, 4 * col_width :].T

    back_src = jnp.minimum(recv_start[:, None] + places[None, :], owned_rows - 1)
    back_send = pick_rows(back_src.reshape(-1), token_rows).reshape(dp_count, MAXLEN, col_width)
    back_grads = exchange(back_send)
    load_ids = jnp.arange(load_rows, dtype=jnp.int32)
    seq_of = jnp.sum((load_ids[:, None] >= my_starts[None, :]).astype(jnp.int32), axis=1) - 1
    seq_pick = seq_of[:, None] == seq_ids[None, :]
    owner_of = jnp.sum(jnp.where(seq_pick, my_owners[None, :], 0), axis=1)
    start_of = jnp.sum(jnp.where(seq_pick, my_starts[None, :], 0), axis=1)
    back_ids = (owner_of ^ dp_index) * MAXLEN + jnp.minimum(load_ids - start_of, MAXLEN - 1)
    row_used = load_ids < jnp.sum(my_lengths)
    token_grad = pick_from_pieces(jnp.where(row_used, back_ids, -1), back_grads)
    return (mixed_out, token_grad, proj_grad, out_grad)


def solution(mesh):
    in_specs = (P("dp", "tensor"), P("dp", "tensor"), P(), P(), P(), P(), P())
    out_specs = (P("dp", "tensor"), P("dp", "tensor"), P("dp", None, "tensor"), P("tensor", "dp"))
    return jax.shard_map(local, mesh=mesh, in_specs=in_specs, out_specs=out_specs, check_vma=False)
```

```python
import math

import jax
import jax.numpy as jnp
from jax import lax
from jax.sharding import PartitionSpec as P

D = 1024
H = 8
MAXLEN = 192


norm_eps = 1e-05


def silu_slope(argument):
    sigmoid_val = jax.nn.sigmoid(argument)
    return sigmoid_val * (1.0 + argument * (1.0 - sigmoid_val))


def exclusive_sum(counts):
    return jnp.cumsum(counts) - counts


def local(tokens, cotangent, lengths, owners, proj_weight, norm_gain, out_weight):
    f32 = jnp.float32
    bf16 = jnp.bfloat16
    dp_count = lax.axis_size("dp")
    tensor_count = lax.axis_size("tensor")
    dp_index = lax.axis_index("dp")
    tensor_index = lax.axis_index("tensor")
    col_width = tokens.shape[1]
    load_rows = tokens.shape[0]
    head_dim = D // H
    score_scale = 1.0 / math.sqrt(head_dim)
    owned_rows = dp_count * (9 * MAXLEN // 16)
    places = jnp.arange(MAXLEN, dtype=jnp.int32)
    peer_ids = jnp.arange(dp_count, dtype=jnp.int32)
    seq_ids = jnp.arange(lengths.shape[1], dtype=jnp.int32)

    my_lengths = lengths[dp_index]
    my_owners = owners[dp_index]
    my_starts = exclusive_sum(my_lengths)
    sent_to = my_owners[None, :] == peer_ids[:, None]
    send_start = jnp.sum(jnp.where(sent_to, my_starts[None, :], 0), axis=1)
    send_ids = jnp.minimum(send_start[:, None] + places[None, :], load_rows - 1)
    def exchange(blocks):
        pieces = [lax.dynamic_index_in_dim(blocks, dp_index, 0, keepdims=False)]
        for k in range(1, dp_count):
            outgoing = lax.dynamic_index_in_dim(blocks, dp_index ^ k, 0, keepdims=False)
            pieces.append(lax.ppermute(outgoing, "dp", [(d, d ^ k) for d in range(dp_count)]))
        return jnp.stack(pieces)

    def pick_rows(row_ids, source):
        one_hot = (row_ids[:, None] == jnp.arange(source.shape[0], dtype=jnp.int32)[None, :]).astype(bf16)
        return jnp.dot(one_hot, source, preferred_element_type=f32).astype(bf16)

    flat_send = send_ids.reshape(-1)
    send_both = pick_rows(flat_send, jnp.concatenate([tokens, cotangent], axis=1)).reshape(
        dp_count, MAXLEN, 2 * col_width
    )
    recv_both = exchange(send_both)

    half_count = tensor_count // 2
    core = tensor_index % 2

    def by_core(weight, axis):
        split = weight.reshape(weight.shape[:axis] + (half_count, 2) + weight.shape[axis + 1 :])
        return (
            lax.dynamic_index_in_dim(split, core, axis + 1, keepdims=False),
            lax.dynamic_index_in_dim(split, 1 - core, axis + 1, keepdims=False),
        )

    head_start = tensor_index * H // tensor_count * head_dim
    own_start = tensor_index * col_width
    inner_start = own_start - head_start
    head_proj = lax.dynamic_slice_in_dim(proj_weight, head_start, head_dim, 2).reshape(
        tensor_count, col_width, 4 * head_dim
    )
    own_proj = lax.dynamic_slice_in_dim(proj_weight, own_start, col_width, 2).reshape(
        tensor_count, col_width, 4 * col_width
    )
    head_out = lax.dynamic_slice_in_dim(out_weight, head_start, head_dim, 0).reshape(
        head_dim, tensor_count, col_width
    )
    head_gain = lax.dynamic_slice_in_dim(norm_gain, head_start, head_dim, 0)

    proj_mine, proj_other = by_core(head_proj, 0)
    out_mine, out_other = by_core(head_out, 1)
    own_out = lax.dynamic_slice_in_dim(out_weight, own_start, col_width, 0).reshape(
        col_width, tensor_count, col_width
    )
    weight_pack = (proj_mine, proj_other, out_mine, out_other, own_proj, own_out)
    recv_both, weight_pack = lax.optimization_barrier((recv_both, weight_pack))
    proj_mine, proj_other, out_mine, out_other, own_proj, own_out = weight_pack

    recv_len = jnp.sum(jnp.where(owners == dp_index, lengths, 0), axis=1)
    recv_start = exclusive_sum(recv_len)
    compact_ids = jnp.arange(owned_rows, dtype=jnp.int32)
    compact_slot = (
        jnp.sum((compact_ids[:, None] >= recv_start[None, :]).astype(jnp.int32), axis=1) - 1
    )
    slot_pick = compact_slot[:, None] == peer_ids[None, :]
    compact_start = jnp.sum(jnp.where(slot_pick, recv_start[None, :], 0), axis=1)
    gather_ids = (compact_slot ^ dp_index) * MAXLEN + compact_ids - compact_start
    own_both = pick_rows(gather_ids, recv_both.reshape(dp_count * MAXLEN, 2 * col_width))
    own_tokens = own_both[:, :col_width]
    own_cotan = own_both[:, col_width:]

    same_core = [[2 * z + c for z in range(half_count)] for c in range(2)]
    sibling = [(t, t ^ 1) for t in range(tensor_count)]
    mine = lax.all_gather(own_both, "tensor", axis=0, tiled=False, axis_index_groups=same_core)
    other = lax.ppermute(mine, "tensor", sibling)
    mine_tok, mine_cot = mine[..., :col_width], mine[..., col_width:]
    other_tok, other_cot = other[..., :col_width], other[..., col_width:]

    def sibling_sum(part):
        keep, send = by_core(part, 0)
        return (keep.astype(f32) + lax.ppermute(send, "tensor", sibling).astype(f32)).astype(bf16)

    def reduce_blocks(pair_sum):
        pieces = lax.all_to_all(pair_sum, "tensor", 0, 0, tiled=True, axis_index_groups=same_core)
        return jnp.sum(pieces.astype(f32), axis=0)

    projected = jnp.einsum(
        "trc,tcn->rn", mine_tok, proj_mine, preferred_element_type=f32
    ) + jnp.einsum("trc,tcn->rn", other_tok, proj_other, preferred_element_type=f32)
    down_grad = jnp.einsum(
        "trc,dtc->rd", mine_cot, out_mine, preferred_element_type=f32
    ) + jnp.einsum("trc,dtc->rd", other_cot, out_other, preferred_element_type=f32)
    proj4 = projected.reshape(owned_rows, 4, head_dim)
    activated = jax.nn.silu(proj4).astype(bf16)
    gating = activated[:, 0]
    values = activated[:, 1]
    queries = activated[:, 2]
    keys_head = activated[:, 3]
    scores = jnp.einsum("md,nd->mn", queries, keys_head, preferred_element_type=f32)
    allowed = (compact_slot[:, None] == compact_slot[None, :]) & (
        compact_ids[:, None] >= compact_ids[None, :]
    )
    weights = jnp.where(allowed, jax.nn.silu(scores * score_scale) / MAXLEN, 0.0).astype(bf16)
    attended = jnp.einsum("mn,nd->md", weights, values, preferred_element_type=f32)
    inv_rms = lax.rsqrt(jnp.mean(attended * attended, axis=-1, keepdims=True) + norm_eps)
    normed = attended * inv_rms * head_gain
    gated = (normed * gating).astype(bf16)
    own_gated = lax.dynamic_slice_in_dim(gated, inner_start, col_width, 1)
    out_part = jnp.einsum("rc,ctk->trk", own_gated, own_out, preferred_element_type=f32)

    d_normed = down_grad * gating
    d_gating = down_grad * normed
    scaled = head_gain * d_normed
    d_attended = (
        inv_rms * scaled
        - attended * inv_rms**3 * jnp.mean(attended * scaled, axis=-1, keepdims=True)
    ).astype(bf16)
    d_weights = jnp.einsum("md,nd->mn", d_attended, values, preferred_element_type=f32)
    d_values = jnp.einsum("mn,md->nd", weights, d_attended, preferred_element_type=f32)
    d_scores = jnp.where(
        allowed, d_weights * silu_slope(scores * score_scale) * (score_scale / MAXLEN), 0.0
    ).astype(bf16)
    d_queries = jnp.einsum("mn,nd->md", d_scores, keys_head, preferred_element_type=f32)
    d_keys = jnp.einsum("mn,md->nd", d_scores, queries, preferred_element_type=f32)
    d_activated = jnp.stack([d_gating, d_values, d_queries, d_keys], axis=1)
    d_projected = (d_activated * silu_slope(proj4)).astype(bf16)
    own_grad = lax.dynamic_slice_in_dim(d_projected, inner_start, col_width, 2).reshape(
        owned_rows, 4 * col_width
    )
    grad_part = jnp.einsum("rn,tkn->trk", own_grad, own_proj, preferred_element_type=f32)
    both_sum = reduce_blocks(
        jnp.concatenate([sibling_sum(out_part.astype(bf16)), sibling_sum(grad_part.astype(bf16))], axis=2)
    )
    out_sum = both_sum[:, :col_width]
    grad_sum = both_sum[:, col_width:]
    mixed_out = (own_tokens.astype(f32) + out_sum).astype(bf16)
    token_rows = (own_cotan.astype(f32) + grad_sum).astype(bf16)

    def by_rows(term_mine, term_other):
        pair = jnp.stack([term_mine, term_other], axis=1)
        pair = jnp.where(core == 0, pair, pair[:, ::-1])
        return pair.reshape((D,) + term_mine.shape[2:])

    proj_term = by_rows(
        jnp.einsum("trc,rn->tcn", mine_tok, own_grad, preferred_element_type=f32),
        jnp.einsum("trc,rn->tcn", other_tok, own_grad, preferred_element_type=f32),
    )
    out_term = by_rows(
        jnp.einsum("trc,rd->tcd", mine_cot, own_gated, preferred_element_type=f32),
        jnp.einsum("trc,rd->tcd", other_cot, own_gated, preferred_element_type=f32),
    )
    terms = jnp.concatenate([proj_term, out_term], axis=1).astype(bf16)
    term_blocks = terms.reshape((dp_count, D // dp_count) + terms.shape[1:])
    term_sum = lax.dynamic_index_in_dim(term_blocks, dp_index, 0, keepdims=False).astype(f32)
    for k in range(1, dp_count):
        outgoing = lax.dynamic_index_in_dim(term_blocks, dp_index ^ k, 0, keepdims=False)
        partners = [(d, d ^ k) for d in range(dp_count)]
        term_sum = term_sum + lax.ppermute(outgoing, "dp", partners).astype(f32)
    proj_grad = term_sum[:, : 4 * col_width].reshape(-1, 4, col_width)
    out_grad = term_sum[:, 4 * col_width :].T

    back_src = jnp.minimum(recv_start[:, None] + places[None, :], owned_rows - 1)
    back_send = pick_rows(back_src.reshape(-1), token_rows).reshape(dp_count, MAXLEN, col_width)
    back_grads = exchange(back_send)
    back_grads = back_grads.reshape(dp_count * MAXLEN, col_width)
    load_ids = jnp.arange(load_rows, dtype=jnp.int32)
    seq_of = jnp.sum((load_ids[:, None] >= my_starts[None, :]).astype(jnp.int32), axis=1) - 1
    seq_pick = seq_of[:, None] == seq_ids[None, :]
    owner_of = jnp.sum(jnp.where(seq_pick, my_owners[None, :], 0), axis=1)
    start_of = jnp.sum(jnp.where(seq_pick, my_starts[None, :], 0), axis=1)
    back_ids = (owner_of ^ dp_index) * MAXLEN + jnp.minimum(load_ids - start_of, MAXLEN - 1)
    row_used = load_ids < jnp.sum(my_lengths)
    token_grad = pick_rows(jnp.where(row_used, back_ids, -1), back_grads)
    return (mixed_out, token_grad, proj_grad, out_grad)


def solution(mesh):
    in_specs = (P("dp", "tensor"), P("dp", "tensor"), P(), P(), P(), P(), P())
    out_specs = (P("dp", "tensor"), P("dp", "tensor"), P("dp", None, "tensor"), P("tensor", "dp"))
    return jax.shard_map(local, mesh=mesh, in_specs=in_specs, out_specs=out_specs, check_vma=False)
```
